32 devices in a mesh: visit: 4 (over z), row: 2 (over core), col: 4 (over y, x).
Axes of the slice: x: 2, y: 2, z: 4, core: 2. Of those that a mesh axis runs over, the one named last changes fastest.
Arguments:
- images: bfloat16 [16, 1024, 2048], P('visit', 'row', 'col'), may hold values from -10 to 10, as said below
- coeffs: float32 [16, 3], P('visit'), may hold values from 0.3 to 1.2
- pair_list: int32 [8, 3], replicated, may hold values from 0 to 480, as said below
- weights: bfloat16 [16, 2, 4], P('visit', 'row', 'col'), may hold values from 0.5 to 4
- resample_bank: bfloat16 [12, 512, 512], replicated, may hold values from -0.25 to 0.25
- warp_index: int32 [16, 2, 4, 2], P('visit', 'row', 'col'), may hold values from 0 to 11
- destinations: int32 [16, 2, 4, 4], P('visit', 'row', 'col'), may hold values from 0 to 3, as said below
- counts: int32 [16, 2, 4], P('visit', 'row', 'col'), may hold values from 3 to 4
Outputs:
- coadd_patch: float32 [4, 1024, 2048], P('visit', 'row', 'col')
- plane_fit: float32 [16, 3], P('visit')
The draws below stay inside these ranges and needn't reach their ends.
Inputs may be any that keep to these rules, and one draw needn't show every extreme that they name: `images`: noise plus a per-exposure sky plane. `pair_list`: every exposure appears in exactly one pair; offsets lie in 0 to 480, both ends used. `destinations`: the used entries of one tile's list are distinct; each tile lists the patch of its own visit index; a patch drawn with skew, which may be the device's own visit patch, is listed by all 4 tiles at each device position.
All inputs are finite; a program needn't handle non-finite values.
Results may differ from the reference program's by a relative error of at most 0.015.
Values may be sent and summed in bfloat16 or wider, within the bound.
No kernel may reach another device: no remote copies, remote signals or barrier semaphores. Data moves between devices by JAX's collectives and lax.ppermute only.
A program may use at most 192 MiB of HBM per device.

```python
import math
import jax
import jax.numpy as jnp
from jax import lax

TILE = 512
HALO = 16
STRIP = 32
NBASIS = 3
MAXD = 4
NBANK = 12
EXP_DEV = 4
N_EXP = 16
N_VISIT = 4
N_ROW = 2
N_COL = 4


def draw_images(key, part):
    noise_key, sky_key = jax.random.split(key)
    height = N_ROW * TILE
    breadth = N_COL * TILE
    noise = jnp.clip(jax.random.normal(noise_key, (N_EXP, height, breadth), jnp.float32), -4.0, 4.0)
    sky = jax.random.uniform(sky_key, (N_EXP, 3), jnp.float32, -2.0, 2.0)
    ycoord = (jnp.arange(height).astype(jnp.float32) + 0.5) / height * 2.0 - 1.0
    xcoord = (jnp.arange(breadth).astype(jnp.float32) + 0.5) / breadth * 2.0 - 1.0
    values = noise + sky[:, 0, None, None] + sky[:, 1, None, None] * xcoord[None, None, :] + sky[:, 2, None, None] * ycoord[None, :, None]
    return values.astype(jnp.bfloat16)


def draw_pair_list(key, part):
    order_key, offset_key = jax.random.split(jax.random.fold_in(key, 5))
    order = jax.random.permutation(order_key, N_EXP).astype(jnp.int32)
    offsets = jax.random.randint(offset_key, (N_EXP // 2,), 0, TILE - STRIP + 1).astype(jnp.int32)
    offsets = offsets.at[0].set(0).at[N_EXP // 2 - 1].set(TILE - STRIP)
    return jnp.stack([order[0::2], order[1::2], offsets], 1).astype(jnp.int32)


def route_tables(key):
    folded = jax.random.fold_in(key, 11)
    subkeys = jax.random.split(folded, 6)
    popular = jax.random.permutation(subkeys[0], N_VISIT).astype(jnp.int32)
    device_shape = (N_VISIT, 1, N_ROW, N_COL)
    chosen_rank = jnp.minimum(jax.random.randint(subkeys[1], device_shape, 0, N_VISIT), jax.random.randint(subkeys[2], device_shape, 0, N_VISIT))
    hottest = popular[chosen_rank]
    owners = jnp.arange(N_VISIT, dtype=jnp.int32)
    visits = jnp.arange(N_VISIT, dtype=jnp.int32)[:, None, None, None, None]
    scores = jax.random.randint(subkeys[3], (N_VISIT, EXP_DEV, N_ROW, N_COL, N_VISIT), 0, 4096) * N_VISIT + owners
    scores = scores + jnp.where(owners == hottest[..., None], 2 ** 23, 0) + jnp.where(owners == visits, 2 ** 22, 0)
    ranked = lax.top_k(scores.astype(jnp.int32), MAXD)[1].astype(jnp.int32)
    how_many = jax.random.randint(subkeys[4], (N_VISIT, EXP_DEV, N_ROW, N_COL), MAXD - 1, MAXD + 1).astype(jnp.int32)
    filler = jax.random.randint(subkeys[5], ranked.shape, 0, N_VISIT).astype(jnp.int32)
    usable = jnp.arange(MAXD, dtype=jnp.int32) < how_many[..., None]
    listed = jnp.where(usable, ranked, filler)
    return (listed.reshape(N_EXP, N_ROW, N_COL, MAXD), how_many.reshape(N_EXP, N_ROW, N_COL))


def draw_destinations(key, part):
    return route_tables(key)[0]


def draw_counts(key, part):
    return route_tables(key)[1]


def plant(values, rng, low, high):
    longest = values.shape.index(max(values.shape))
    spots = []
    for shift in (0, 1):
        where = [jax.random.randint(jax.random.fold_in(rng, axis), (), 0, length) for axis, length in enumerate(values.shape)]
        where[longest] = (where[longest] + shift) % values.shape[longest]
        spots.append(tuple(where))
    return values.at[spots[0]].set(low).at[spots[1]].set(high)


def block_scale(own_key, dims, pieces, least, top_value):
    factor_of = 1.0
    for position, parts in pieces:
        draws = jax.random.uniform(jax.random.fold_in(jax.random.fold_in(own_key, 6), position), (parts,), jnp.float32, least / len(pieces), top_value / len(pieces))
        factor_of = factor_of * jnp.repeat(jnp.exp(draws), dims[position] // parts).reshape((-1,) + (1,) * (len(dims) - 1 - position))
    return factor_of


def normal_values(rng, shape, deviation, most, kind=jnp.bfloat16):
    return jnp.clip(deviation * jax.random.normal(rng, shape, jnp.float32), -most, most).astype(kind)


def setup_inputs(seed: int = 0) -> dict:
    seeds = jax.random.split(jax.random.key(seed), 9)
    images = draw_images(jax.random.fold_in(seeds[8], 71), 0)
    coeffs = jnp.clip(0.3 + 0.90000004 * jax.random.uniform(seeds[1], (N_EXP, NBASIS), jnp.float32) ** block_scale(seeds[1], (N_EXP, NBASIS), ((0, 4),), -0.2, 0.2), 0.3, 1.2)
    pair_list = draw_pair_list(jax.random.fold_in(seeds[8], 71), 0)
    weights = jnp.clip(jnp.exp(math.log(4.0) - 2.0794415 * jax.random.uniform(seeds[3], (N_EXP, N_ROW, N_COL), jnp.float32) ** block_scale(seeds[3], (N_EXP, N_ROW, N_COL), ((0, 4), (1, 2), (2, 4)), -0.2, 0.2)), 0.5, 4.0).astype(jnp.bfloat16)
    resample_bank = normal_values(seeds[4], (NBANK, TILE, TILE), TILE ** -0.5, 0.25)
    warp_index = plant(jax.random.randint(seeds[5], (N_EXP, N_ROW, N_COL, 2), 0, NBANK), jax.random.fold_in(seeds[5], 1), 0, NBANK - 1).astype(jnp.int32)
    destinations = draw_destinations(jax.random.fold_in(seeds[8], 71), 0)
    counts = draw_counts(jax.random.fold_in(seeds[8], 71), 0)
    return dict(images=images, coeffs=coeffs, pair_list=pair_list, weights=weights, resample_bank=resample_bank, warp_index=warp_index, destinations=destinations, counts=counts)


SIGMA_PARTS = (0.0625, 0.125, 0.25)

def tap_values(width, sigma):
    spread = (jnp.arange(2 * width + 1) - width).astype(jnp.float32)
    curve = jnp.exp(-spread * spread / (2.0 * sigma * sigma))
    return (curve / jnp.sum(curve)).astype(jnp.bfloat16)

def centred(index, length):
    return (index.astype(jnp.float32) + 0.5) / length * 2.0 - 1.0

def solve_three(normal, moments):
    lower = jnp.linalg.cholesky(normal)
    first = moments[..., 0] / lower[..., 0, 0]
    second = (moments[..., 1] - lower[..., 1, 0] * first) / lower[..., 1, 1]
    third = (moments[..., 2] - lower[..., 2, 0] * first - lower[..., 2, 1] * second) / lower[..., 2, 2]
    upper_top = third / lower[..., 2, 2]
    upper_mid = (second - lower[..., 2, 1] * upper_top) / lower[..., 1, 1]
    upper_low = (first - lower[..., 1, 0] * upper_mid - lower[..., 2, 0] * upper_top) / lower[..., 0, 0]
    return jnp.stack([upper_low, upper_mid, upper_top], -1)

def reference(images, coeffs, pair_list, weights, resample_bank, warp_index, destinations, counts):
    height = N_ROW * TILE
    breadth = N_COL * TILE
    tables = [tap_values(HALO, HALO * fraction).astype(jnp.float32) for fraction in SIGMA_PARTS]
    first_col = pair_list[:, 0].astype(jnp.int32)
    second_col = pair_list[:, 1].astype(jnp.int32)
    offsets = pair_list[:, 2].astype(jnp.int32)
    columns = centred(jnp.arange(breadth), breadth)
    rows_all = centred(jnp.arange(height), height)

    def one_exposure(number):
        image = images[number].astype(jnp.float32)
        padded = jnp.pad(image, HALO)
        matched = jnp.zeros((height, breadth), jnp.float32)
        for kernel in range(len(SIGMA_PARTS)):
            taps = tables[kernel]
            across = jnp.zeros((height, breadth + 2 * HALO), jnp.float32)
            for shift in range(2 * HALO + 1):
                across = across + taps[shift] * padded[shift:shift + height, :]
            across = lax.optimization_barrier(across.astype(jnp.bfloat16)).astype(jnp.float32)
            smoothed = jnp.zeros((height, breadth), jnp.float32)
            for shift in range(2 * HALO + 1):
                smoothed = smoothed + taps[shift] * across[:, shift:shift + breadth]
            matched = matched + coeffs[number, kernel] * smoothed
        hit_first = first_col == number
        hit_second = second_col == number
        partner = jnp.sum(jnp.where(hit_first, second_col, 0) + jnp.where(hit_second, first_col, 0)).astype(jnp.int32)
        offset = jnp.sum(jnp.where(hit_first | hit_second, offsets, 0)).astype(jnp.int32)
        strip_rows = (jnp.arange(N_ROW, dtype=jnp.int32)[:, None] * TILE + offset + jnp.arange(STRIP, dtype=jnp.int32)[None, :]).reshape(-1)
        theirs = jnp.take(images[partner], strip_rows, axis=0).astype(jnp.float32)
        nearby = jnp.take(matched, strip_rows, axis=0)
        difference = nearby - theirs
        pixel_weight = 1.0 / (1.0 + theirs * theirs)
        strip_shape = difference.shape
        ycoord = centred(strip_rows, height)
        regressors = jnp.stack([jnp.ones(strip_shape, jnp.float32), jnp.broadcast_to(columns[None, :], strip_shape), jnp.broadcast_to(ycoord[:, None], strip_shape)], 0)
        weighted = regressors * pixel_weight[None]
        normal = jnp.einsum('aij,bij->ab', weighted, regressors, precision=lax.Precision.HIGHEST)
        moments = jnp.einsum('aij,ij->a', weighted, difference, precision=lax.Precision.HIGHEST)
        plane = solve_three(normal, moments)
        corrected = (matched - (plane[0] + plane[1] * columns[None, :] + plane[2] * rows_all[:, None])).astype(jnp.bfloat16)
        blocks = corrected.reshape(N_ROW, TILE, N_COL, TILE).transpose(0, 2, 1, 3).astype(jnp.float32)
        choose = warp_index[number].astype(jnp.int32)
        row_maps = resample_bank[choose[..., 0]].astype(jnp.float32)
        col_maps = resample_bank[choose[..., 1]].astype(jnp.float32)
        halfway = jnp.einsum('rcij,rcjk->rcik', row_maps, blocks, precision=lax.Precision.HIGHEST)
        halfway = lax.optimization_barrier(halfway.astype(jnp.bfloat16)).astype(jnp.float32)
        warped = jnp.einsum('rcik,rclk->rcil', halfway, col_maps, precision=lax.Precision.HIGHEST).astype(jnp.bfloat16)
        return (plane, warped)
    plane_fit, warped = lax.map(one_exposure, jnp.arange(N_EXP, dtype=jnp.int32))
    usable = jnp.arange(MAXD, dtype=jnp.int32)[None, None, None, :] < counts[..., None]
    owners = jnp.arange(N_VISIT, dtype=jnp.int32)
    member = jnp.any(usable[..., None] & (destinations[..., None] == owners), axis=3)
    chosen = jnp.where(member, weights[..., None].astype(jnp.float32), 0.0)
    numerator = jnp.einsum('ercv,ercij->vrcij', chosen, warped.astype(jnp.float32), precision=lax.Precision.HIGHEST)
    denominator = jnp.sum(chosen, axis=0).transpose(2, 0, 1)
    coadd_patch = numerator / denominator[..., None, None]
    coadd_patch = coadd_patch.transpose(0, 1, 3, 2, 4).reshape(N_VISIT, height, breadth)
    return (coadd_patch, plane_fit)
```

```python
import jax
import jax.numpy as jnp
from jax import lax
from jax.sharding import PartitionSpec as P

HALO = 16
STRIP = 32
MAXD = 4


SIGMA_PARTS = (0.0625, 0.125, 0.25)


def extended(value, sides, width):
    for axis, dim in sides:
        devices, length = (lax.axis_size(axis), value.shape[dim])
        up = [(i, (i + 1) % devices) for i in range(devices - 1)]
        down = [(j, i) for i, j in up]
        last = lax.slice_in_dim(value, length - width, length, axis=dim)
        initial = lax.slice_in_dim(value, 0, width, axis=dim)
        before = lax.ppermute(last, axis, up)
        after = lax.ppermute(initial, axis, down)
        value = jnp.concatenate([before, value, after], axis=dim)
    return value


def band_table(length, width, sigma):
    spread = (jnp.arange(2 * width + 1) - width).astype(jnp.float32)
    curve = jnp.exp(-spread * spread / (2.0 * sigma * sigma))
    total = jnp.sum(curve)
    rows_grid = lax.broadcasted_iota(jnp.int32, (length, length + 2 * width), 0)
    cols_grid = lax.broadcasted_iota(jnp.int32, (length, length + 2 * width), 1)
    offset = (cols_grid - rows_grid - width).astype(jnp.float32)
    values = jnp.exp(-offset * offset / (2.0 * sigma * sigma)) / total
    return jnp.where(jnp.abs(offset) <= width, values, 0.0).astype(jnp.bfloat16)


def centred(index, length):
    return (index.astype(jnp.float32) + 0.5) / length * 2.0 - 1.0


def solve_three(normal, moments):
    lower = jnp.linalg.cholesky(normal)
    first = moments[..., 0] / lower[..., 0, 0]
    second = (moments[..., 1] - lower[..., 1, 0] * first) / lower[..., 1, 1]
    third = (moments[..., 2] - lower[..., 2, 0] * first - lower[..., 2, 1] * second) / lower[
        ..., 2, 2
    ]
    upper_top = third / lower[..., 2, 2]
    upper_mid = (second - lower[..., 2, 1] * upper_top) / lower[..., 1, 1]
    upper_low = (first - lower[..., 1, 0] * upper_mid - lower[..., 2, 0] * upper_top) / lower[
        ..., 0, 0
    ]
    return jnp.stack([upper_low, upper_mid, upper_top], -1)


def butterfly_sum(values, axes):
    for axis, size in axes:
        if size & (size - 1) == 0:
            bit = 1
            while bit < size:
                pairs = [(i, i ^ bit) for i in range(size)]
                values = jax.tree.map(lambda v: v + lax.ppermute(v, axis, pairs), values)
                bit *= 2
        else:
            position = lax.axis_index(axis)
            def gathered(v):
                parts = [v]
                for shift in range(1, size):
                    pairs = [(i, (i + shift) % size) for i in range(size)]
                    parts.append(lax.ppermute(v, axis, pairs))
                stacked = jnp.stack(parts, 0)
                order = (position - jnp.arange(size)) % size
                canonical = jnp.zeros_like(stacked).at[order].set(stacked)
                return jnp.sum(canonical, axis=0)
            values = jax.tree.map(gathered, values)
    return values


def rows_from(source, anchor):
    return lax.dynamic_slice_in_dim(source, anchor, STRIP, 0)


def shards(images, coeffs, pair_list, weights, resample_bank, warp_index, destinations, counts):
    exp_dev = images.shape[0]
    tile_len = images.shape[1]
    row_count = lax.axis_size("row")
    col_count = lax.axis_size("col")
    visit_count = lax.axis_size("visit")
    row_pos = lax.axis_index("row")
    col_pos = lax.axis_index("col")
    visit_pos = lax.axis_index("visit")
    height = row_count * tile_len
    breadth = col_count * tile_len
    padded = extended(images, (("row", 1), ("col", 2)), HALO)
    matched = jnp.zeros((exp_dev, tile_len, tile_len), jnp.float32)
    for kernel in range(len(SIGMA_PARTS)):
        table = band_table(tile_len, HALO, HALO * SIGMA_PARTS[kernel])
        across = jnp.einsum(
            "ij,ejl->eil", table, padded, preferred_element_type=jnp.float32
        ).astype(jnp.bfloat16)
        smoothed = jnp.einsum("eil,ml->eim", across, table, preferred_element_type=jnp.float32)
        matched = matched + coeffs[:, kernel, None, None] * smoothed
    own_ids = visit_pos * exp_dev + jnp.arange(exp_dev, dtype=jnp.int32)
    first_col = pair_list[:, 0]
    second_col = pair_list[:, 1]
    offsets = pair_list[:, 2]
    hit_first = first_col[None, :] == own_ids[:, None]
    hit_second = second_col[None, :] == own_ids[:, None]
    partner = jnp.sum(
        jnp.where(hit_first, second_col[None, :], 0) + jnp.where(hit_second, first_col[None, :], 0),
        axis=1,
    )
    offset = jnp.sum(jnp.where(hit_first | hit_second, offsets[None, :], 0), axis=1)
    own_strip = jax.vmap(rows_from)(images, offset)
    listed = destinations[:, 0, 0, :]
    how_many = counts[:, 0, 0]
    usable = jnp.arange(MAXD, dtype=jnp.int32)[None, :] < how_many[:, None]
    owners = jnp.arange(visit_count, dtype=jnp.int32)
    member = jnp.any(usable[:, :, None] & (listed[:, :, None] == owners[None, None, :]), axis=1)
    tile_weight = weights[:, 0, 0]
    nothing = jnp.zeros((), jnp.bfloat16)
    picked = jnp.where(member, tile_weight[:, None], nothing)
    strip_rows_n = exp_dev * STRIP
    extra = -(-(exp_dev * visit_count) // tile_len)
    extra = -(-extra // 16) * 16
    tail = jnp.zeros((extra * tile_len,), jnp.bfloat16)
    tail = tail.at[: exp_dev * visit_count].set(picked.reshape(-1)).reshape(extra, tile_len)
    payload = jnp.concatenate([own_strip.reshape(strip_rows_n, tile_len), tail], axis=0)
    received = [payload]
    for shift in range(1, visit_count):
        pairs = [(i, (i + shift) % visit_count) for i in range(visit_count)]
        received.append(lax.ppermute(payload, "visit", pairs))
    stacked = jnp.stack(received, 0)
    strips_all = stacked[:, :strip_rows_n].reshape(visit_count * exp_dev, STRIP, tile_len)
    picked_all = stacked[:, strip_rows_n:].reshape(visit_count, -1)[:, : exp_dev * visit_count]
    picked_all = picked_all.reshape(visit_count, exp_dev, visit_count)
    partner_visit = partner // exp_dev
    slot = (visit_pos - partner_visit) % visit_count
    theirs = jnp.take(strips_all, slot * exp_dev + partner % exp_dev, axis=0).astype(jnp.float32)
    own_patch = jnp.take(picked_all, visit_pos, axis=2).astype(jnp.float32)
    denominator = jnp.sum(own_patch).reshape(1)
    nearby = jax.vmap(rows_from)(matched, offset)
    difference = nearby - theirs
    pixel_weight = 1.0 / (1.0 + theirs * theirs)
    strip_rows = row_pos * tile_len + offset[:, None] + jnp.arange(STRIP, dtype=jnp.int32)[None, :]
    ycoord = centred(strip_rows, height)[:, :, None]
    xcoord = centred(col_pos * tile_len + jnp.arange(tile_len, dtype=jnp.int32), breadth)
    xgrid = xcoord[None, None, :]
    weight_x = pixel_weight * xgrid
    weight_y = pixel_weight * ycoord
    sum_w = jnp.sum(pixel_weight, axis=(1, 2))
    sum_x = jnp.sum(weight_x, axis=(1, 2))
    sum_y = jnp.sum(weight_y, axis=(1, 2))
    sum_xx = jnp.sum(weight_x * xgrid, axis=(1, 2))
    sum_xy = jnp.sum(weight_x * ycoord, axis=(1, 2))
    sum_yy = jnp.sum(weight_y * ycoord, axis=(1, 2))
    normal = jnp.stack(
        [
            jnp.stack([sum_w, sum_x, sum_y], -1),
            jnp.stack([sum_x, sum_xx, sum_xy], -1),
            jnp.stack([sum_y, sum_xy, sum_yy], -1),
        ],
        1,
    )
    moments = jnp.stack(
        [
            jnp.sum(pixel_weight * difference, axis=(1, 2)),
            jnp.sum(weight_x * difference, axis=(1, 2)),
            jnp.sum(weight_y * difference, axis=(1, 2)),
        ],
        -1,
    )
    packed = jnp.concatenate([normal.reshape(exp_dev, 9), moments], axis=1)
    packed = butterfly_sum(packed, (("row", row_count), ("col", col_count)))
    normal = packed[:, :9].reshape(exp_dev, 3, 3)
    moments = packed[:, 9:]
    plane_fit = solve_three(normal, moments)
    row_coord = centred(row_pos * tile_len + jnp.arange(tile_len, dtype=jnp.int32), height)
    background = (
        plane_fit[:, 0, None, None]
        + plane_fit[:, 1, None, None] * xcoord[None, None, :]
        + plane_fit[:, 2, None, None] * row_coord[None, :, None]
    )
    corrected = (matched - background).astype(jnp.bfloat16)
    choose = warp_index[:, 0, 0, :]
    row_maps = jnp.stack(
        [lax.dynamic_index_in_dim(resample_bank, choose[e, 0], 0, False) for e in range(exp_dev)]
    )
    col_maps = jnp.stack(
        [lax.dynamic_index_in_dim(resample_bank, choose[e, 1], 0, False) for e in range(exp_dev)]
    )
    halfway = jnp.einsum(
        "eij,ejk->eik", row_maps, corrected, preferred_element_type=jnp.float32
    ).astype(jnp.bfloat16)
    warped = jnp.einsum(
        "eik,elk->eil", halfway, col_maps, preferred_element_type=jnp.float32
    ).astype(jnp.bfloat16)
    partial_sum = jnp.einsum("ev,eij->vij", picked, warped, preferred_element_type=jnp.float32)
    numerator = lax.psum_scatter(
        partial_sum.astype(jnp.bfloat16), "visit", scatter_dimension=0, tiled=True
    ).astype(jnp.float32)
    coadd_patch = numerator / denominator[:, None, None]
    return (coadd_patch, plane_fit)


def solution(mesh):
    in_specs = (
        P("visit", "row", "col"),
        P("visit", None),
        P(),
        P("visit", "row", "col"),
        P(),
        P("visit", "row", "col", None),
        P("visit", "row", "col", None),
        P("visit", "row", "col"),
    )
    out_specs = (P("visit", "row", "col"), P("visit", None))
    return jax.shard_map(shards, mesh=mesh, in_specs=in_specs, out_specs=out_specs, check_vma=False)
```

```python
import jax
import jax.numpy as jnp
from jax import lax
from jax.sharding import PartitionSpec as P

HALO = 16
STRIP = 32
MAXD = 4


SIGMA_PARTS = (0.0625, 0.125, 0.25)


def extended(value, sides, width):
    for axis, dim in sides:
        devices, length = (lax.axis_size(axis), value.shape[dim])
        up = [(i, (i + 1) % devices) for i in range(devices - 1)]
        down = [(j, i) for i, j in up]
        last = lax.slice_in_dim(value, length - width, length, axis=dim)
        initial = lax.slice_in_dim(value, 0, width, axis=dim)
        before = lax.ppermute(last, axis, up)
        after = lax.ppermute(initial, axis, down)
        value = jnp.concatenate([before, value, after], axis=dim)
    return value


def band_table(length, width, sigma):
    spread = (jnp.arange(2 * width + 1) - width).astype(jnp.float32)
    curve = jnp.exp(-spread * spread / (2.0 * sigma * sigma))
    total = jnp.sum(curve)
    rows_grid = lax.broadcasted_iota(jnp.int32, (length, length + 2 * width), 0)
    cols_grid = lax.broadcasted_iota(jnp.int32, (length, length + 2 * width), 1)
    offset = (cols_grid - rows_grid - width).astype(jnp.float32)
    values = jnp.exp(-offset * offset / (2.0 * sigma * sigma)) / total
    return jnp.where(jnp.abs(offset) <= width, values, 0.0).astype(jnp.bfloat16)


def centred(index, length):
    return (index.astype(jnp.float32) + 0.5) / length * 2.0 - 1.0


def solve_three(normal, moments):
    lower = jnp.linalg.cholesky(normal)
    first = moments[..., 0] / lower[..., 0, 0]
    second = (moments[..., 1] - lower[..., 1, 0] * first) / lower[..., 1, 1]
    third = (moments[..., 2] - lower[..., 2, 0] * first - lower[..., 2, 1] * second) / lower[
        ..., 2, 2
    ]
    upper_top = third / lower[..., 2, 2]
    upper_mid = (second - lower[..., 2, 1] * upper_top) / lower[..., 1, 1]
    upper_low = (first - lower[..., 1, 0] * upper_mid - lower[..., 2, 0] * upper_top) / lower[
        ..., 0, 0
    ]
    return jnp.stack([upper_low, upper_mid, upper_top], -1)


def butterfly_sum(values, axes):
    for axis, size in axes:
        if size & (size - 1) == 0:
            bit = 1
            while bit < size:
                pairs = [(i, i ^ bit) for i in range(size)]
                values = jax.tree.map(lambda v: v + lax.ppermute(v, axis, pairs), values)
                bit *= 2
        else:
            position = lax.axis_index(axis)
            def gathered(v):
                parts = [v]
                for shift in range(1, size):
                    pairs = [(i, (i + shift) % size) for i in range(size)]
                    parts.append(lax.ppermute(v, axis, pairs))
                stacked = jnp.stack(parts, 0)
                order = (position - jnp.arange(size)) % size
                canonical = jnp.zeros_like(stacked).at[order].set(stacked)
                return jnp.sum(canonical, axis=0)
            values = jax.tree.map(gathered, values)
    return values


def rows_from(source, anchor):
    return lax.dynamic_slice_in_dim(source, anchor, STRIP, 0)


def shards(images, coeffs, pair_list, weights, resample_bank, warp_index, destinations, counts):
    exp_dev = images.shape[0]
    tile_len = images.shape[1]
    row_count = lax.axis_size("row")
    col_count = lax.axis_size("col")
    visit_count = lax.axis_size("visit")
    row_pos = lax.axis_index("row")
    col_pos = lax.axis_index("col")
    visit_pos = lax.axis_index("visit")
    height = row_count * tile_len
    breadth = col_count * tile_len
    padded = extended(images, (("row", 1), ("col", 2)), HALO)
    own_ids = visit_pos * exp_dev + jnp.arange(exp_dev, dtype=jnp.int32)
    first_col = pair_list[:, 0]
    second_col = pair_list[:, 1]
    offsets = pair_list[:, 2]
    hit_first = first_col[None, :] == own_ids[:, None]
    hit_second = second_col[None, :] == own_ids[:, None]
    partner = jnp.sum(
        jnp.where(hit_first, second_col[None, :], 0) + jnp.where(hit_second, first_col[None, :], 0),
        axis=1,
    )
    offset = jnp.sum(jnp.where(hit_first | hit_second, offsets[None, :], 0), axis=1)
    own_strip = jnp.stack([rows_from(images[e], offset[e]) for e in range(exp_dev)])
    listed = destinations[:, 0, 0, :]
    how_many = counts[:, 0, 0]
    usable = jnp.arange(MAXD, dtype=jnp.int32)[None, :] < how_many[:, None]
    owners = jnp.arange(visit_count, dtype=jnp.int32)
    member = jnp.any(usable[:, :, None] & (listed[:, :, None] == owners[None, None, :]), axis=1)
    tile_weight = weights[:, 0, 0]
    nothing = jnp.zeros((), jnp.bfloat16)
    picked = jnp.where(member, tile_weight[:, None], nothing)
    strip_rows_n = exp_dev * STRIP
    extra = -(-(exp_dev * visit_count) // tile_len)
    extra = -(-extra // 16) * 16
    tail = jnp.zeros((extra * tile_len,), jnp.bfloat16)
    tail = tail.at[: exp_dev * visit_count].set(picked.reshape(-1)).reshape(extra, tile_len)
    payload = jnp.concatenate([own_strip.reshape(strip_rows_n, tile_len), tail], axis=0)
    received = [payload]
    for shift in range(1, visit_count):
        pairs = [(i, (i + shift) % visit_count) for i in range(visit_count)]
        received.append(lax.ppermute(payload, "visit", pairs))
    stacked = jnp.stack(received, 0)
    strips_all = stacked[:, :strip_rows_n].reshape(visit_count * exp_dev, STRIP, tile_len)
    picked_all = stacked[:, strip_rows_n:].reshape(visit_count, -1)[:, : exp_dev * visit_count]
    picked_all = picked_all.reshape(visit_count, exp_dev, visit_count)
    partner_visit = partner // exp_dev
    slot = (visit_pos - partner_visit) % visit_count
    theirs = jnp.take(strips_all, slot * exp_dev + partner % exp_dev, axis=0).astype(jnp.float32)
    own_patch = jnp.take(picked_all, visit_pos, axis=2).astype(jnp.float32)
    denominator = jnp.sum(own_patch).reshape(1)
    tables = [band_table(tile_len, HALO, HALO * part) for part in SIGMA_PARTS]
    window = STRIP + 2 * HALO
    pieces = jnp.stack(
        [lax.dynamic_slice_in_dim(padded[e], offset[e], window, 0) for e in range(exp_dev)]
    )
    nearby = jnp.zeros((exp_dev, STRIP, tile_len), jnp.float32)
    for kernel in range(len(SIGMA_PARTS)):
        table = tables[kernel]
        across = jnp.einsum(
            "ij,ejl->eil", table[:STRIP, :window], pieces, preferred_element_type=jnp.float32
        ).astype(jnp.bfloat16)
        smoothed = jnp.einsum("eil,ml->eim", across, table, preferred_element_type=jnp.float32)
        nearby = nearby + coeffs[:, kernel, None, None] * smoothed
    matched = jnp.zeros((exp_dev, tile_len, tile_len), jnp.float32)
    for kernel in range(len(SIGMA_PARTS)):
        table = tables[kernel]
        across = jnp.einsum(
            "ij,ejl->eil", table, padded, preferred_element_type=jnp.float32
        ).astype(jnp.bfloat16)
        smoothed = jnp.einsum("eil,ml->eim", across, table, preferred_element_type=jnp.float32)
        matched = matched + coeffs[:, kernel, None, None] * smoothed
    difference = nearby - theirs
    pixel_weight = 1.0 / (1.0 + theirs * theirs)
    strip_rows = row_pos * tile_len + offset[:, None] + jnp.arange(STRIP, dtype=jnp.int32)[None, :]
    ycoord = centred(strip_rows, height)[:, :, None]
    xcoord = centred(col_pos * tile_len + jnp.arange(tile_len, dtype=jnp.int32), breadth)
    xgrid = xcoord[None, None, :]
    weight_x = pixel_weight * xgrid
    weight_y = pixel_weight * ycoord
    sum_w = jnp.sum(pixel_weight, axis=(1, 2))
    sum_x = jnp.sum(weight_x, axis=(1, 2))
    sum_y = jnp.sum(weight_y, axis=(1, 2))
    sum_xx = jnp.sum(weight_x * xgrid, axis=(1, 2))
    sum_xy = jnp.sum(weight_x * ycoord, axis=(1, 2))
    sum_yy = jnp.sum(weight_y * ycoord, axis=(1, 2))
    normal = jnp.stack(
        [
            jnp.stack([sum_w, sum_x, sum_y], -1),
            jnp.stack([sum_x, sum_xx, sum_xy], -1),
            jnp.stack([sum_y, sum_xy, sum_yy], -1),
        ],
        1,
    )
    moments = jnp.stack(
        [
            jnp.sum(pixel_weight * difference, axis=(1, 2)),
            jnp.sum(weight_x * difference, axis=(1, 2)),
            jnp.sum(weight_y * difference, axis=(1, 2)),
        ],
        -1,
    )
    packed = jnp.concatenate([normal.reshape(exp_dev, 9), moments], axis=1)
    packed = butterfly_sum(packed, (("row", row_count), ("col", col_count)))
    normal = packed[:, :9].reshape(exp_dev, 3, 3)
    moments = packed[:, 9:]
    plane_fit = solve_three(normal, moments)
    row_coord = centred(row_pos * tile_len + jnp.arange(tile_len, dtype=jnp.int32), height)
    background = (
        plane_fit[:, 0, None, None]
        + plane_fit[:, 1, None, None] * xcoord[None, None, :]
        + plane_fit[:, 2, None, None] * row_coord[None, :, None]
    )
    corrected = (matched - background).astype(jnp.bfloat16)
    choose = warp_index[:, 0, 0, :]
    row_maps = jnp.stack(
        [lax.dynamic_index_in_dim(resample_bank, choose[e, 0], 0, False) for e in range(exp_dev)]
    )
    col_maps = jnp.stack(
        [lax.dynamic_index_in_dim(resample_bank, choose[e, 1], 0, False) for e in range(exp_dev)]
    )
    halfway = jnp.einsum(
        "eij,ejk->eik", row_maps, corrected, preferred_element_type=jnp.float32
    ).astype(jnp.bfloat16)
    warped = jnp.einsum(
        "eik,elk->eil", halfway, col_maps, preferred_element_type=jnp.float32
    ).astype(jnp.bfloat16)
    partial_sum = jnp.einsum("ev,eij->vij", picked, warped, preferred_element_type=jnp.float32)
    numerator = lax.psum_scatter(
        partial_sum.astype(jnp.bfloat16), "visit", scatter_dimension=0, tiled=True
    ).astype(jnp.float32)
    coadd_patch = numerator / denominator[:, None, None]
    return (coadd_patch, plane_fit)


def solution(mesh):
    in_specs = (
        P("visit", "row", "col"),
        P("visit", None),
        P(),
        P("visit", "row", "col"),
        P(),
        P("visit", "row", "col", None),
        P("visit", "row", "col", None),
        P("visit", "row", "col"),
    )
    out_specs = (P("visit", "row", "col"), P("visit", None))
    return jax.shard_map(shards, mesh=mesh, in_specs=in_specs, out_specs=out_specs, check_vma=False)
```

```python
import jax
import jax.numpy as jnp
from jax import lax
from jax.sharding import PartitionSpec as P
from jax.experimental import pallas as pl
from jax.experimental.pallas import tpu as pltpu

HALO = 16
STRIP = 32
MAXD = 4


SIGMA_PARTS = (0.0625, 0.125, 0.25)


def extended(value, sides, width):
    for axis, dim in sides:
        devices, length = (lax.axis_size(axis), value.shape[dim])
        up = [(i, (i + 1) % devices) for i in range(devices - 1)]
        down = [(j, i) for i, j in up]
        last = lax.slice_in_dim(value, length - width, length, axis=dim)
        initial = lax.slice_in_dim(value, 0, width, axis=dim)
        before = lax.ppermute(last, axis, up)
        after = lax.ppermute(initial, axis, down)
        value = jnp.concatenate([before, value, after], axis=dim)
    return value


def band_table(length, width, sigma):
    spread = (jnp.arange(2 * width + 1) - width).astype(jnp.float32)
    curve = jnp.exp(-spread * spread / (2.0 * sigma * sigma))
    total = jnp.sum(curve)
    rows_grid = lax.broadcasted_iota(jnp.int32, (length, length + 2 * width), 0)
    cols_grid = lax.broadcasted_iota(jnp.int32, (length, length + 2 * width), 1)
    offset = (cols_grid - rows_grid - width).astype(jnp.float32)
    values = jnp.exp(-offset * offset / (2.0 * sigma * sigma)) / total
    return jnp.where(jnp.abs(offset) <= width, values, 0.0).astype(jnp.bfloat16)


def centred(index, length):
    return (index.astype(jnp.float32) + 0.5) / length * 2.0 - 1.0


def solve_three(normal, moments):
    lower = jnp.linalg.cholesky(normal)
    first = moments[..., 0] / lower[..., 0, 0]
    second = (moments[..., 1] - lower[..., 1, 0] * first) / lower[..., 1, 1]
    third = (moments[..., 2] - lower[..., 2, 0] * first - lower[..., 2, 1] * second) / lower[
        ..., 2, 2
    ]
    upper_top = third / lower[..., 2, 2]
    upper_mid = (second - lower[..., 2, 1] * upper_top) / lower[..., 1, 1]
    upper_low = (first - lower[..., 1, 0] * upper_mid - lower[..., 2, 0] * upper_top) / lower[
        ..., 0, 0
    ]
    return jnp.stack([upper_low, upper_mid, upper_top], -1)


def butterfly_sum(values, axes):
    for axis, size in axes:
        if size & (size - 1) == 0:
            bit = 1
            while bit < size:
                pairs = [(i, i ^ bit) for i in range(size)]
                values = jax.tree.map(lambda v: v + lax.ppermute(v, axis, pairs), values)
                bit *= 2
        else:
            position = lax.axis_index(axis)
            def gathered(v):
                parts = [v]
                for shift in range(1, size):
                    pairs = [(i, (i + shift) % size) for i in range(size)]
                    parts.append(lax.ppermute(v, axis, pairs))
                stacked = jnp.stack(parts, 0)
                order = (position - jnp.arange(size)) % size
                canonical = jnp.zeros_like(stacked).at[order].set(stacked)
                return jnp.sum(canonical, axis=0)
            values = jax.tree.map(gathered, values)
    return values


def warp_body(idx_ref, plane_ref, xrow_ref, ycol_ref, matched_ref, rmap_ref, cmap_ref, out_ref):
    e = pl.program_id(0)
    background = (
        plane_ref[e, 0] + plane_ref[e, 1] * xrow_ref[...]
    ) + plane_ref[e, 2] * ycol_ref[...]
    corrected = (matched_ref[0] - background).astype(jnp.bfloat16)
    halfway = jnp.dot(rmap_ref[0], corrected, preferred_element_type=jnp.float32)
    warped = lax.dot_general(
        halfway.astype(jnp.bfloat16), cmap_ref[0], (((1,), (1,)), ((), ())),
        preferred_element_type=jnp.float32,
    )
    out_ref[0] = warped.astype(jnp.bfloat16)


def warp_tiles(choose, plane, xrow, ycol, matched, bank):
    exp_dev, tile_len = matched.shape[0], matched.shape[1]
    grid_spec = pltpu.PrefetchScalarGridSpec(
        num_scalar_prefetch=1,
        grid=(exp_dev,),
        in_specs=[
            pl.BlockSpec(memory_space=pltpu.SMEM),
            pl.BlockSpec((1, tile_len), lambda e, idx: (0, 0)),
            pl.BlockSpec((tile_len, 1), lambda e, idx: (0, 0)),
            pl.BlockSpec((1, tile_len, tile_len), lambda e, idx: (e, 0, 0)),
            pl.BlockSpec((1, tile_len, tile_len), lambda e, idx: (idx[e, 0], 0, 0)),
            pl.BlockSpec((1, tile_len, tile_len), lambda e, idx: (idx[e, 1], 0, 0)),
        ],
        out_specs=pl.BlockSpec((1, tile_len, tile_len), lambda e, idx: (e, 0, 0)),
    )
    flops = exp_dev * 4 * tile_len ** 3
    moved = exp_dev * tile_len * tile_len * (4 + 2 + 2 + 2)
    return pl.pallas_call(
        warp_body,
        grid_spec=grid_spec,
        out_shape=jax.ShapeDtypeStruct(matched.shape, jnp.bfloat16),
        compiler_params=pltpu.CompilerParams(
            dimension_semantics=("arbitrary",), vmem_limit_bytes=48 * 1024 * 1024
        ),
        cost_estimate=pl.CostEstimate(flops=flops, bytes_accessed=moved, transcendentals=0),
    )(choose, plane, xrow, ycol, matched, bank, bank)


def rows_from(source, anchor):
    return lax.dynamic_slice_in_dim(source, anchor, STRIP, 0)


def shards(images, coeffs, pair_list, weights, resample_bank, warp_index, destinations, counts):
    exp_dev = images.shape[0]
    tile_len = images.shape[1]
    row_count = lax.axis_size("row")
    col_count = lax.axis_size("col")
    visit_count = lax.axis_size("visit")
    row_pos = lax.axis_index("row")
    col_pos = lax.axis_index("col")
    visit_pos = lax.axis_index("visit")
    height = row_count * tile_len
    breadth = col_count * tile_len
    padded = extended(images, (("row", 1), ("col", 2)), HALO)
    own_ids = visit_pos * exp_dev + jnp.arange(exp_dev, dtype=jnp.int32)
    first_col = pair_list[:, 0]
    second_col = pair_list[:, 1]
    offsets = pair_list[:, 2]
    hit_first = first_col[None, :] == own_ids[:, None]
    hit_second = second_col[None, :] == own_ids[:, None]
    partner = jnp.sum(
        jnp.where(hit_first, second_col[None, :], 0) + jnp.where(hit_second, first_col[None, :], 0),
        axis=1,
    )
    offset = jnp.sum(jnp.where(hit_first | hit_second, offsets[None, :], 0), axis=1)
    pick_rows = (
        lax.broadcasted_iota(jnp.int32, (exp_dev, STRIP, tile_len), 2)
        == offset[:, None, None] + lax.broadcasted_iota(jnp.int32, (exp_dev, STRIP, tile_len), 1)
    ).astype(jnp.bfloat16)
    own_strip = jnp.einsum(
        "esr,erl->esl", pick_rows, images, preferred_element_type=jnp.float32
    ).astype(jnp.bfloat16)
    listed = destinations[:, 0, 0, :]
    how_many = counts[:, 0, 0]
    usable = jnp.arange(MAXD, dtype=jnp.int32)[None, :] < how_many[:, None]
    owners = jnp.arange(visit_count, dtype=jnp.int32)
    member = jnp.any(usable[:, :, None] & (listed[:, :, None] == owners[None, None, :]), axis=1)
    tile_weight = weights[:, 0, 0]
    nothing = jnp.zeros((), jnp.bfloat16)
    picked = jnp.where(member, tile_weight[:, None], nothing)
    strip_rows_n = exp_dev * STRIP
    extra = -(-(exp_dev * visit_count) // tile_len)
    extra = -(-extra // 16) * 16
    tail = jnp.zeros((extra * tile_len,), jnp.bfloat16)
    tail = tail.at[: exp_dev * visit_count].set(picked.reshape(-1)).reshape(extra, tile_len)
    payload = jnp.concatenate([own_strip.reshape(strip_rows_n, tile_len), tail], axis=0)
    received = [payload]
    for shift in range(1, visit_count):
        pairs = [(i, (i + shift) % visit_count) for i in range(visit_count)]
        received.append(lax.ppermute(payload, "visit", pairs))
    stacked = jnp.stack(received, 0)
    strips_all = stacked[:, :strip_rows_n].reshape(visit_count * exp_dev, STRIP, tile_len)
    picked_all = stacked[:, strip_rows_n:].reshape(visit_count, -1)[:, : exp_dev * visit_count]
    picked_all = picked_all.reshape(visit_count, exp_dev, visit_count)
    partner_visit = partner // exp_dev
    slot = (visit_pos - partner_visit) % visit_count
    source = slot * exp_dev + partner % exp_dev
    choose_strip = (
        lax.broadcasted_iota(jnp.int32, (exp_dev, visit_count * exp_dev), 1) == source[:, None]
    ).astype(jnp.bfloat16)
    theirs = jnp.einsum(
        "ej,jsl->esl", choose_strip, strips_all, preferred_element_type=jnp.float32
    )
    own_patch = jnp.take(picked_all, visit_pos, axis=2).astype(jnp.float32)
    denominator = jnp.sum(own_patch).reshape(1)
    tables = [band_table(tile_len, HALO, HALO * part) for part in SIGMA_PARTS]
    nearby = jnp.zeros((exp_dev, STRIP, tile_len), jnp.float32)
    for kernel in range(len(SIGMA_PARTS)):
        table = tables[kernel]
        strip_table = jnp.einsum(
            "esr,rj->esj", pick_rows, table, preferred_element_type=jnp.float32
        ).astype(jnp.bfloat16)
        across = jnp.einsum(
            "esj,ejl->esl", strip_table, padded, preferred_element_type=jnp.float32
        ).astype(jnp.bfloat16)
        smoothed = jnp.einsum("eil,ml->eim", across, table, preferred_element_type=jnp.float32)
        nearby = nearby + coeffs[:, kernel, None, None] * smoothed
    matched = jnp.zeros((exp_dev, tile_len, tile_len), jnp.float32)
    for kernel in range(len(SIGMA_PARTS)):
        table = tables[kernel]
        across = jnp.einsum(
            "ij,ejl->eil", table, padded, preferred_element_type=jnp.float32
        ).astype(jnp.bfloat16)
        smoothed = jnp.einsum("eil,ml->eim", across, table, preferred_element_type=jnp.float32)
        matched = matched + coeffs[:, kernel, None, None] * smoothed
    difference = nearby - theirs
    pixel_weight = 1.0 / (1.0 + theirs * theirs)
    strip_rows = row_pos * tile_len + offset[:, None] + jnp.arange(STRIP, dtype=jnp.int32)[None, :]
    ycoord = centred(strip_rows, height)[:, :, None]
    xcoord = centred(col_pos * tile_len + jnp.arange(tile_len, dtype=jnp.int32), breadth)
    xgrid = xcoord[None, None, :]
    weight_x = pixel_weight * xgrid
    weight_y = pixel_weight * ycoord
    sum_w = jnp.sum(pixel_weight, axis=(1, 2))
    sum_x = jnp.sum(weight_x, axis=(1, 2))
    sum_y = jnp.sum(weight_y, axis=(1, 2))
    sum_xx = jnp.sum(weight_x * xgrid, axis=(1, 2))
    sum_xy = jnp.sum(weight_x * ycoord, axis=(1, 2))
    sum_yy = jnp.sum(weight_y * ycoord, axis=(1, 2))
    normal = jnp.stack(
        [
            jnp.stack([sum_w, sum_x, sum_y], -1),
            jnp.stack([sum_x, sum_xx, sum_xy], -1),
            jnp.stack([sum_y, sum_xy, sum_yy], -1),
        ],
        1,
    )
    moments = jnp.stack(
        [
            jnp.sum(pixel_weight * difference, axis=(1, 2)),
            jnp.sum(weight_x * difference, axis=(1, 2)),
            jnp.sum(weight_y * difference, axis=(1, 2)),
        ],
        -1,
    )
    packed = jnp.concatenate([normal.reshape(exp_dev, 9), moments], axis=1)
    packed = butterfly_sum(packed, (("row", row_count), ("col", col_count)))
    normal = packed[:, :9].reshape(exp_dev, 3, 3)
    moments = packed[:, 9:]
    plane_fit = solve_three(normal, moments)
    row_coord = centred(row_pos * tile_len + jnp.arange(tile_len, dtype=jnp.int32), height)
    choose = warp_index[:, 0, 0, :]
    warped = warp_tiles(
        choose, plane_fit, xcoord.reshape(1, tile_len), row_coord.reshape(tile_len, 1),
        matched, resample_bank,
    )
    partial_sum = jnp.einsum("ev,eij->vij", picked, warped, preferred_element_type=jnp.float32)
    numerator = lax.psum_scatter(
        partial_sum.astype(jnp.bfloat16), "visit", scatter_dimension=0, tiled=True
    ).astype(jnp.float32)
    coadd_patch = numerator / denominator[:, None, None]
    return (coadd_patch, plane_fit)


def solution(mesh):
    in_specs = (
        P("visit", "row", "col"),
        P("visit", None),
        P(),
        P("visit", "row", "col"),
        P(),
        P("visit", "row", "col", None),
        P("visit", "row", "col", None),
        P("visit", "row", "col"),
    )
    out_specs = (P("visit", "row", "col"), P("visit", None))
    return jax.shard_map(shards, mesh=mesh, in_specs=in_specs, out_specs=out_specs, check_vma=False)
```

```python
import jax
import jax.numpy as jnp
from jax import lax
from jax.sharding import PartitionSpec as P
from jax.experimental import pallas as pl
from jax.experimental.pallas import tpu as pltpu

HALO = 16
STRIP = 32
MAXD = 4


SIGMA_PARTS = (0.0625, 0.125, 0.25)


def extended(value, sides, width):
    for axis, dim in sides:
        devices, length = (lax.axis_size(axis), value.shape[dim])
        up = [(i, (i + 1) % devices) for i in range(devices - 1)]
        down = [(j, i) for i, j in up]
        last = lax.slice_in_dim(value, length - width, length, axis=dim)
        initial = lax.slice_in_dim(value, 0, width, axis=dim)
        before = lax.ppermute(last, axis, up)
        after = lax.ppermute(initial, axis, down)
        value = jnp.concatenate([before, value, after], axis=dim)
    return value


def band_table(length, width, sigma):
    spread = (jnp.arange(2 * width + 1) - width).astype(jnp.float32)
    curve = jnp.exp(-spread * spread / (2.0 * sigma * sigma))
    total = jnp.sum(curve)
    rows_grid = lax.broadcasted_iota(jnp.int32, (length, length + 2 * width), 0)
    cols_grid = lax.broadcasted_iota(jnp.int32, (length, length + 2 * width), 1)
    offset = (cols_grid - rows_grid - width).astype(jnp.float32)
    values = jnp.exp(-offset * offset / (2.0 * sigma * sigma)) / total
    return jnp.where(jnp.abs(offset) <= width, values, 0.0).astype(jnp.bfloat16)


def centred(index, length):
    return (index.astype(jnp.float32) + 0.5) / length * 2.0 - 1.0


def solve_three(normal, moments):
    lower = jnp.linalg.cholesky(normal)
    first = moments[..., 0] / lower[..., 0, 0]
    second = (moments[..., 1] - lower[..., 1, 0] * first) / lower[..., 1, 1]
    third = (moments[..., 2] - lower[..., 2, 0] * first - lower[..., 2, 1] * second) / lower[
        ..., 2, 2
    ]
    upper_top = third / lower[..., 2, 2]
    upper_mid = (second - lower[..., 2, 1] * upper_top) / lower[..., 1, 1]
    upper_low = (first - lower[..., 1, 0] * upper_mid - lower[..., 2, 0] * upper_top) / lower[
        ..., 0, 0
    ]
    return jnp.stack([upper_low, upper_mid, upper_top], -1)


def butterfly_sum(values, axes):
    for axis, size in axes:
        if size & (size - 1) == 0:
            bit = 1
            while bit < size:
                pairs = [(i, i ^ bit) for i in range(size)]
                values = jax.tree.map(lambda v: v + lax.ppermute(v, axis, pairs), values)
                bit *= 2
        else:
            position = lax.axis_index(axis)
            def gathered(v):
                parts = [v]
                for shift in range(1, size):
                    pairs = [(i, (i + shift) % size) for i in range(size)]
                    parts.append(lax.ppermute(v, axis, pairs))
                stacked = jnp.stack(parts, 0)
                order = (position - jnp.arange(size)) % size
                canonical = jnp.zeros_like(stacked).at[order].set(stacked)
                return jnp.sum(canonical, axis=0)
            values = jax.tree.map(gathered, values)
    return values


def conv_body(coef_ref, vt_ref, ht_ref, padded_ref, out_ref):
    e = pl.program_id(0)
    image = padded_ref[0]
    total = None
    for kernel in range(len(SIGMA_PARTS)):
        across = jnp.dot(vt_ref[0, kernel], image, preferred_element_type=jnp.float32)
        smoothed = lax.dot_general(
            across.astype(jnp.bfloat16), ht_ref[kernel], (((1,), (1,)), ((), ())),
            preferred_element_type=jnp.float32,
        )
        term = coef_ref[e, kernel] * smoothed
        total = term if total is None else total + term
    out_ref[0] = total


def conv_tiles(coeffs, vtables, htables, padded, per_exposure):
    exp_dev, wide = padded.shape[0], padded.shape[1]
    nk, out_rows = vtables.shape[-3], vtables.shape[-2]
    tile_len = htables.shape[1]
    if per_exposure:
        vspec = pl.BlockSpec((1, nk, out_rows, wide), lambda e: (e, 0, 0, 0))
    else:
        vtables = vtables[None]
        vspec = pl.BlockSpec((1, nk, out_rows, wide), lambda e: (0, 0, 0, 0))
    flops = exp_dev * nk * 2 * out_rows * wide * (wide + tile_len)
    moved = exp_dev * wide * wide * 2 + exp_dev * out_rows * tile_len * 4
    return pl.pallas_call(
        conv_body,
        grid=(exp_dev,),
        in_specs=[
            pl.BlockSpec(memory_space=pltpu.SMEM),
            vspec,
            pl.BlockSpec((nk, tile_len, wide), lambda e: (0, 0, 0)),
            pl.BlockSpec((1, wide, wide), lambda e: (e, 0, 0)),
        ],
        out_specs=pl.BlockSpec((1, out_rows, tile_len), lambda e: (e, 0, 0)),
        out_shape=jax.ShapeDtypeStruct((exp_dev, out_rows, tile_len), jnp.float32),
        compiler_params=pltpu.CompilerParams(
            dimension_semantics=("arbitrary",), vmem_limit_bytes=48 * 1024 * 1024
        ),
        cost_estimate=pl.CostEstimate(flops=flops, bytes_accessed=moved, transcendentals=0),
    )(coeffs, vtables, htables, padded)


def warp_body(idx_ref, plane_ref, xrow_ref, ycol_ref, matched_ref, rmap_ref, cmap_ref, out_ref):
    e = pl.program_id(0)
    background = (
        plane_ref[e, 0] + plane_ref[e, 1] * xrow_ref[...]
    ) + plane_ref[e, 2] * ycol_ref[...]
    corrected = (matched_ref[0] - background).astype(jnp.bfloat16)
    halfway = jnp.dot(rmap_ref[0], corrected, preferred_element_type=jnp.float32)
    warped = lax.dot_general(
        halfway.astype(jnp.bfloat16), cmap_ref[0], (((1,), (1,)), ((), ())),
        preferred_element_type=jnp.float32,
    )
    out_ref[0] = warped.astype(jnp.bfloat16)


def warp_tiles(choose, plane, xrow, ycol, matched, bank):
    exp_dev, tile_len = matched.shape[0], matched.shape[1]
    grid_spec = pltpu.PrefetchScalarGridSpec(
        num_scalar_prefetch=1,
        grid=(exp_dev,),
        in_specs=[
            pl.BlockSpec(memory_space=pltpu.SMEM),
            pl.BlockSpec((1, tile_len), lambda e, idx: (0, 0)),
            pl.BlockSpec((tile_len, 1), lambda e, idx: (0, 0)),
            pl.BlockSpec((1, tile_len, tile_len), lambda e, idx: (e, 0, 0)),
            pl.BlockSpec((1, tile_len, tile_len), lambda e, idx: (idx[e, 0], 0, 0)),
            pl.BlockSpec((1, tile_len, tile_len), lambda e, idx: (idx[e, 1], 0, 0)),
        ],
        out_specs=pl.BlockSpec((1, tile_len, tile_len), lambda e, idx: (e, 0, 0)),
    )
    flops = exp_dev * 4 * tile_len ** 3
    moved = exp_dev * tile_len * tile_len * (4 + 2 + 2 + 2)
    return pl.pallas_call(
        warp_body,
        grid_spec=grid_spec,
        out_shape=jax.ShapeDtypeStruct(matched.shape, jnp.bfloat16),
        compiler_params=pltpu.CompilerParams(
            dimension_semantics=("arbitrary",), vmem_limit_bytes=48 * 1024 * 1024
        ),
        cost_estimate=pl.CostEstimate(flops=flops, bytes_accessed=moved, transcendentals=0),
    )(choose, plane, xrow, ycol, matched, bank, bank)


def rows_from(source, anchor):
    return lax.dynamic_slice_in_dim(source, anchor, STRIP, 0)


def shards(images, coeffs, pair_list, weights, resample_bank, warp_index, destinations, counts):
    exp_dev = images.shape[0]
    tile_len = images.shape[1]
    row_count = lax.axis_size("row")
    col_count = lax.axis_size("col")
    visit_count = lax.axis_size("visit")
    row_pos = lax.axis_index("row")
    col_pos = lax.axis_index("col")
    visit_pos = lax.axis_index("visit")
    height = row_count * tile_len
    breadth = col_count * tile_len
    padded = extended(images, (("row", 1), ("col", 2)), HALO)
    own_ids = visit_pos * exp_dev + jnp.arange(exp_dev, dtype=jnp.int32)
    first_col = pair_list[:, 0]
    second_col = pair_list[:, 1]
    offsets = pair_list[:, 2]
    hit_first = first_col[None, :] == own_ids[:, None]
    hit_second = second_col[None, :] == own_ids[:, None]
    partner = jnp.sum(
        jnp.where(hit_first, second_col[None, :], 0) + jnp.where(hit_second, first_col[None, :], 0),
        axis=1,
    )
    offset = jnp.sum(jnp.where(hit_first | hit_second, offsets[None, :], 0), axis=1)
    pick_rows = (
        lax.broadcasted_iota(jnp.int32, (exp_dev, STRIP, tile_len), 2)
        == offset[:, None, None] + lax.broadcasted_iota(jnp.int32, (exp_dev, STRIP, tile_len), 1)
    ).astype(jnp.bfloat16)
    own_strip = jnp.einsum(
        "esr,erl->esl", pick_rows, images, preferred_element_type=jnp.float32
    ).astype(jnp.bfloat16)
    listed = destinations[:, 0, 0, :]
    how_many = counts[:, 0, 0]
    usable = jnp.arange(MAXD, dtype=jnp.int32)[None, :] < how_many[:, None]
    owners = jnp.arange(visit_count, dtype=jnp.int32)
    member = jnp.any(usable[:, :, None] & (listed[:, :, None] == owners[None, None, :]), axis=1)
    tile_weight = weights[:, 0, 0]
    nothing = jnp.zeros((), jnp.bfloat16)
    picked = jnp.where(member, tile_weight[:, None], nothing)
    strip_rows_n = exp_dev * STRIP
    extra = -(-(exp_dev * visit_count) // tile_len)
    extra = -(-extra // 16) * 16
    tail = jnp.zeros((extra * tile_len,), jnp.bfloat16)
    tail = tail.at[: exp_dev * visit_count].set(picked.reshape(-1)).reshape(extra, tile_len)
    payload = jnp.concatenate([own_strip.reshape(strip_rows_n, tile_len), tail], axis=0)
    received = [payload]
    for shift in range(1, visit_count):
        pairs = [(i, (i + shift) % visit_count) for i in range(visit_count)]
        received.append(lax.ppermute(payload, "visit", pairs))
    stacked = jnp.stack(received, 0)
    strips_all = stacked[:, :strip_rows_n].reshape(visit_count * exp_dev, STRIP, tile_len)
    picked_all = stacked[:, strip_rows_n:].reshape(visit_count, -1)[:, : exp_dev * visit_count]
    picked_all = picked_all.reshape(visit_count, exp_dev, visit_count)
    partner_visit = partner // exp_dev
    slot = (visit_pos - partner_visit) % visit_count
    source = slot * exp_dev + partner % exp_dev
    choose_strip = (
        lax.broadcasted_iota(jnp.int32, (exp_dev, visit_count * exp_dev), 1) == source[:, None]
    ).astype(jnp.bfloat16)
    theirs = jnp.einsum(
        "ej,jsl->esl", choose_strip, strips_all, preferred_element_type=jnp.float32
    )
    own_patch = jnp.take(picked_all, visit_pos, axis=2).astype(jnp.float32)
    denominator = jnp.sum(own_patch).reshape(1)
    tables = [band_table(tile_len, HALO, HALO * part) for part in SIGMA_PARTS]
    stacked_tables = jnp.stack(tables)
    strip_tables = jnp.einsum(
        "esr,krj->eksj", pick_rows, stacked_tables, preferred_element_type=jnp.float32
    ).astype(jnp.bfloat16)
    nearby = conv_tiles(coeffs, strip_tables, stacked_tables, padded, True)
    matched = conv_tiles(coeffs, stacked_tables, stacked_tables, padded, False)
    difference = nearby - theirs
    pixel_weight = 1.0 / (1.0 + theirs * theirs)
    strip_rows = row_pos * tile_len + offset[:, None] + jnp.arange(STRIP, dtype=jnp.int32)[None, :]
    ycoord = centred(strip_rows, height)[:, :, None]
    xcoord = centred(col_pos * tile_len + jnp.arange(tile_len, dtype=jnp.int32), breadth)
    xgrid = xcoord[None, None, :]
    weight_x = pixel_weight * xgrid
    weight_y = pixel_weight * ycoord
    sum_w = jnp.sum(pixel_weight, axis=(1, 2))
    sum_x = jnp.sum(weight_x, axis=(1, 2))
    sum_y = jnp.sum(weight_y, axis=(1, 2))
    sum_xx = jnp.sum(weight_x * xgrid, axis=(1, 2))
    sum_xy = jnp.sum(weight_x * ycoord, axis=(1, 2))
    sum_yy = jnp.sum(weight_y * ycoord, axis=(1, 2))
    normal = jnp.stack(
        [
            jnp.stack([sum_w, sum_x, sum_y], -1),
            jnp.stack([sum_x, sum_xx, sum_xy], -1),
            jnp.stack([sum_y, sum_xy, sum_yy], -1),
        ],
        1,
    )
    moments = jnp.stack(
        [
            jnp.sum(pixel_weight * difference, axis=(1, 2)),
            jnp.sum(weight_x * difference, axis=(1, 2)),
            jnp.sum(weight_y * difference, axis=(1, 2)),
        ],
        -1,
    )
    packed = jnp.concatenate([normal.reshape(exp_dev, 9), moments], axis=1)
    packed = butterfly_sum(packed, (("row", row_count), ("col", col_count)))
    normal = packed[:, :9].reshape(exp_dev, 3, 3)
    moments = packed[:, 9:]
    plane_fit = solve_three(normal, moments)
    row_coord = centred(row_pos * tile_len + jnp.arange(tile_len, dtype=jnp.int32), height)
    choose = warp_index[:, 0, 0, :]
    warped = warp_tiles(
        choose, plane_fit, xcoord.reshape(1, tile_len), row_coord.reshape(tile_len, 1),
        matched, resample_bank,
    )
    partial_sum = jnp.einsum("ev,eij->vij", picked, warped, preferred_element_type=jnp.float32)
    numerator = lax.psum_scatter(
        partial_sum.astype(jnp.bfloat16), "visit", scatter_dimension=0, tiled=True
    ).astype(jnp.float32)
    coadd_patch = numerator / denominator[:, None, None]
    return (coadd_patch, plane_fit)


def solution(mesh):
    in_specs = (
        P("visit", "row", "col"),
        P("visit", None),
        P(),
        P("visit", "row", "col"),
        P(),
        P("visit", "row", "col", None),
        P("visit", "row", "col", None),
        P("visit", "row", "col"),
    )
    out_specs = (P("visit", "row", "col"), P("visit", None))
    return jax.shard_map(shards, mesh=mesh, in_specs=in_specs, out_specs=out_specs, check_vma=False)
```

```python
import jax
import jax.numpy as jnp
from jax import lax
from jax.sharding import PartitionSpec as P
from jax.experimental import pallas as pl
from jax.experimental.pallas import tpu as pltpu

HALO = 16
STRIP = 32
MAXD = 4


SIGMA_PARTS = (0.0625, 0.125, 0.25)


def extended(value, sides, width):
    for axis, dim in sides:
        devices, length = (lax.axis_size(axis), value.shape[dim])
        last = lax.slice_in_dim(value, length - width, length, axis=dim)
        initial = lax.slice_in_dim(value, 0, width, axis=dim)
        if devices == 2:
            position = lax.axis_index(axis)
            facing = jnp.where(position == 0, last, initial)
            arrived = lax.ppermute(facing, axis, [(0, 1), (1, 0)])
            empty = jnp.zeros_like(arrived)
            before = jnp.where(position == 1, arrived, empty)
            after = jnp.where(position == 0, arrived, empty)
        else:
            up = [(i, (i + 1) % devices) for i in range(devices - 1)]
            down = [(j, i) for i, j in up]
            before = lax.ppermute(last, axis, up)
            after = lax.ppermute(initial, axis, down)
        value = jnp.concatenate([before, value, after], axis=dim)
    return value


def band_table(length, width, sigma):
    spread = (jnp.arange(2 * width + 1) - width).astype(jnp.float32)
    curve = jnp.exp(-spread * spread / (2.0 * sigma * sigma))
    total = jnp.sum(curve)
    rows_grid = lax.broadcasted_iota(jnp.int32, (length, length + 2 * width), 0)
    cols_grid = lax.broadcasted_iota(jnp.int32, (length, length + 2 * width), 1)
    offset = (cols_grid - rows_grid - width).astype(jnp.float32)
    values = jnp.exp(-offset * offset / (2.0 * sigma * sigma)) / total
    return jnp.where(jnp.abs(offset) <= width, values, 0.0).astype(jnp.bfloat16)


def centred(index, length):
    return (index.astype(jnp.float32) + 0.5) / length * 2.0 - 1.0


def solve_three(normal, moments):
    lower = jnp.linalg.cholesky(normal)
    first = moments[..., 0] / lower[..., 0, 0]
    second = (moments[..., 1] - lower[..., 1, 0] * first) / lower[..., 1, 1]
    third = (moments[..., 2] - lower[..., 2, 0] * first - lower[..., 2, 1] * second) / lower[
        ..., 2, 2
    ]
    upper_top = third / lower[..., 2, 2]
    upper_mid = (second - lower[..., 2, 1] * upper_top) / lower[..., 1, 1]
    upper_low = (first - lower[..., 1, 0] * upper_mid - lower[..., 2, 0] * upper_top) / lower[
        ..., 0, 0
    ]
    return jnp.stack([upper_low, upper_mid, upper_top], -1)


def butterfly_sum(values, axes):
    for axis, size in axes:
        if size & (size - 1) == 0:
            bit = 1
            while bit < size:
                pairs = [(i, i ^ bit) for i in range(size)]
                values = jax.tree.map(lambda v: v + lax.ppermute(v, axis, pairs), values)
                bit *= 2
        else:
            position = lax.axis_index(axis)
            def gathered(v):
                parts = [v]
                for shift in range(1, size):
                    pairs = [(i, (i + shift) % size) for i in range(size)]
                    parts.append(lax.ppermute(v, axis, pairs))
                stacked = jnp.stack(parts, 0)
                order = (position - jnp.arange(size)) % size
                canonical = jnp.zeros_like(stacked).at[order].set(stacked)
                return jnp.sum(canonical, axis=0)
            values = jax.tree.map(gathered, values)
    return values


def conv_body(coef_ref, vt_ref, ht_ref, padded_ref, out_ref):
    e = pl.program_id(0)
    image = padded_ref[0]
    total = None
    for kernel in range(len(SIGMA_PARTS)):
        across = jnp.dot(vt_ref[0, kernel], image, preferred_element_type=jnp.float32)
        smoothed = lax.dot_general(
            across.astype(jnp.bfloat16), ht_ref[kernel], (((1,), (1,)), ((), ())),
            preferred_element_type=jnp.float32,
        )
        term = coef_ref[e, kernel] * smoothed
        total = term if total is None else total + term
    out_ref[0] = total


def conv_tiles(coeffs, vtables, htables, padded, per_exposure):
    exp_dev, wide = padded.shape[0], padded.shape[1]
    nk, out_rows = vtables.shape[-3], vtables.shape[-2]
    tile_len = htables.shape[1]
    if per_exposure:
        vspec = pl.BlockSpec((1, nk, out_rows, wide), lambda e: (e, 0, 0, 0))
    else:
        vtables = vtables[None]
        vspec = pl.BlockSpec((1, nk, out_rows, wide), lambda e: (0, 0, 0, 0))
    flops = exp_dev * nk * 2 * out_rows * wide * (wide + tile_len)
    moved = exp_dev * wide * wide * 2 + exp_dev * out_rows * tile_len * 4
    return pl.pallas_call(
        conv_body,
        grid=(exp_dev,),
        in_specs=[
            pl.BlockSpec(memory_space=pltpu.SMEM),
            vspec,
            pl.BlockSpec((nk, tile_len, wide), lambda e: (0, 0, 0)),
            pl.BlockSpec((1, wide, wide), lambda e: (e, 0, 0)),
        ],
        out_specs=pl.BlockSpec((1, out_rows, tile_len), lambda e: (e, 0, 0)),
        out_shape=jax.ShapeDtypeStruct((exp_dev, out_rows, tile_len), jnp.float32),
        compiler_params=pltpu.CompilerParams(
            dimension_semantics=("arbitrary",), vmem_limit_bytes=48 * 1024 * 1024
        ),
        cost_estimate=pl.CostEstimate(flops=flops, bytes_accessed=moved, transcendentals=0),
    )(coeffs, vtables, htables, padded)


def warp_body(idx_ref, plane_ref, xrow_ref, ycol_ref, matched_ref, rmap_ref, cmap_ref, out_ref):
    e = pl.program_id(0)
    background = (
        plane_ref[e, 0] + plane_ref[e, 1] * xrow_ref[...]
    ) + plane_ref[e, 2] * ycol_ref[...]
    corrected = (matched_ref[0] - background).astype(jnp.bfloat16)
    halfway = jnp.dot(rmap_ref[0], corrected, preferred_element_type=jnp.float32)
    warped = lax.dot_general(
        halfway.astype(jnp.bfloat16), cmap_ref[0], (((1,), (1,)), ((), ())),
        preferred_element_type=jnp.float32,
    )
    out_ref[0] = warped.astype(jnp.bfloat16)


def warp_tiles(choose, plane, xrow, ycol, matched, bank):
    exp_dev, tile_len = matched.shape[0], matched.shape[1]
    grid_spec = pltpu.PrefetchScalarGridSpec(
        num_scalar_prefetch=1,
        grid=(exp_dev,),
        in_specs=[
            pl.BlockSpec(memory_space=pltpu.SMEM),
            pl.BlockSpec((1, tile_len), lambda e, idx: (0, 0)),
            pl.BlockSpec((tile_len, 1), lambda e, idx: (0, 0)),
            pl.BlockSpec((1, tile_len, tile_len), lambda e, idx: (e, 0, 0)),
            pl.BlockSpec((1, tile_len, tile_len), lambda e, idx: (idx[e, 0], 0, 0)),
            pl.BlockSpec((1, tile_len, tile_len), lambda e, idx: (idx[e, 1], 0, 0)),
        ],
        out_specs=pl.BlockSpec((1, tile_len, tile_len), lambda e, idx: (e, 0, 0)),
    )
    flops = exp_dev * 4 * tile_len ** 3
    moved = exp_dev * tile_len * tile_len * (4 + 2 + 2 + 2)
    return pl.pallas_call(
        warp_body,
        grid_spec=grid_spec,
        out_shape=jax.ShapeDtypeStruct(matched.shape, jnp.bfloat16),
        compiler_params=pltpu.CompilerParams(
            dimension_semantics=("arbitrary",), vmem_limit_bytes=48 * 1024 * 1024
        ),
        cost_estimate=pl.CostEstimate(flops=flops, bytes_accessed=moved, transcendentals=0),
    )(choose, plane, xrow, ycol, matched, bank, bank)


def rows_from(source, anchor):
    return lax.dynamic_slice_in_dim(source, anchor, STRIP, 0)


def shards(images, coeffs, pair_list, weights, resample_bank, warp_index, destinations, counts):
    exp_dev = images.shape[0]
    tile_len = images.shape[1]
    row_count = lax.axis_size("row")
    col_count = lax.axis_size("col")
    visit_count = lax.axis_size("visit")
    row_pos = lax.axis_index("row")
    col_pos = lax.axis_index("col")
    visit_pos = lax.axis_index("visit")
    height = row_count * tile_len
    breadth = col_count * tile_len
    padded = extended(images, (("col", 2), ("row", 1)), HALO)
    own_ids = visit_pos * exp_dev + jnp.arange(exp_dev, dtype=jnp.int32)
    first_col = pair_list[:, 0]
    second_col = pair_list[:, 1]
    offsets = pair_list[:, 2]
    hit_first = first_col[None, :] == own_ids[:, None]
    hit_second = second_col[None, :] == own_ids[:, None]
    partner = jnp.sum(
        jnp.where(hit_first, second_col[None, :], 0) + jnp.where(hit_second, first_col[None, :], 0),
        axis=1,
    )
    offset = jnp.sum(jnp.where(hit_first | hit_second, offsets[None, :], 0), axis=1)
    pick_rows = (
        lax.broadcasted_iota(jnp.int32, (exp_dev, STRIP, tile_len), 2)
        == offset[:, None, None] + lax.broadcasted_iota(jnp.int32, (exp_dev, STRIP, tile_len), 1)
    ).astype(jnp.bfloat16)
    own_strip = jnp.einsum(
        "esr,erl->esl", pick_rows, images, preferred_element_type=jnp.float32
    ).astype(jnp.bfloat16)
    listed = destinations[:, 0, 0, :]
    how_many = counts[:, 0, 0]
    usable = jnp.arange(MAXD, dtype=jnp.int32)[None, :] < how_many[:, None]
    owners = jnp.arange(visit_count, dtype=jnp.int32)
    member = jnp.any(usable[:, :, None] & (listed[:, :, None] == owners[None, None, :]), axis=1)
    tile_weight = weights[:, 0, 0]
    nothing = jnp.zeros((), jnp.bfloat16)
    picked = jnp.where(member, tile_weight[:, None], nothing)
    strip_rows_n = exp_dev * STRIP
    extra = -(-(exp_dev * visit_count) // tile_len)
    extra = -(-extra // 16) * 16
    tail = jnp.zeros((extra * tile_len,), jnp.bfloat16)
    tail = tail.at[: exp_dev * visit_count].set(picked.reshape(-1)).reshape(extra, tile_len)
    payload = jnp.concatenate([own_strip.reshape(strip_rows_n, tile_len), tail], axis=0)
    received = [payload]
    for shift in range(1, visit_count):
        pairs = [(i, (i + shift) % visit_count) for i in range(visit_count)]
        received.append(lax.ppermute(payload, "visit", pairs))
    stacked = jnp.stack(received, 0)
    strips_all = stacked[:, :strip_rows_n].reshape(visit_count * exp_dev, STRIP, tile_len)
    picked_all = stacked[:, strip_rows_n:].reshape(visit_count, -1)[:, : exp_dev * visit_count]
    picked_all = picked_all.reshape(visit_count, exp_dev, visit_count)
    partner_visit = partner // exp_dev
    slot = (visit_pos - partner_visit) % visit_count
    source = slot * exp_dev + partner % exp_dev
    choose_strip = (
        lax.broadcasted_iota(jnp.int32, (exp_dev, visit_count * exp_dev), 1) == source[:, None]
    ).astype(jnp.bfloat16)
    theirs = jnp.einsum(
        "ej,jsl->esl", choose_strip, strips_all, preferred_element_type=jnp.float32
    )
    own_patch = jnp.take(picked_all, visit_pos, axis=2).astype(jnp.float32)
    denominator = jnp.sum(own_patch).reshape(1)
    stacked_tables = jnp.stack([band_table(tile_len, HALO, HALO * part) for part in SIGMA_PARTS])
    strip_tables = jnp.einsum(
        "esr,krj->eksj", pick_rows, stacked_tables, preferred_element_type=jnp.float32
    ).astype(jnp.bfloat16)
    nearby = conv_tiles(coeffs, strip_tables, stacked_tables, padded, True)
    matched = conv_tiles(coeffs, stacked_tables, stacked_tables, padded, False)
    difference = nearby - theirs
    pixel_weight = 1.0 / (1.0 + theirs * theirs)
    strip_rows = row_pos * tile_len + offset[:, None] + jnp.arange(STRIP, dtype=jnp.int32)[None, :]
    ycoord = centred(strip_rows, height)[:, :, None]
    xcoord = centred(col_pos * tile_len + jnp.arange(tile_len, dtype=jnp.int32), breadth)
    xgrid = xcoord[None, None, :]
    weight_x = pixel_weight * xgrid
    weight_y = pixel_weight * ycoord
    sum_w = jnp.sum(pixel_weight, axis=(1, 2))
    sum_x = jnp.sum(weight_x, axis=(1, 2))
    sum_y = jnp.sum(weight_y, axis=(1, 2))
    sum_xx = jnp.sum(weight_x * xgrid, axis=(1, 2))
    sum_xy = jnp.sum(weight_x * ycoord, axis=(1, 2))
    sum_yy = jnp.sum(weight_y * ycoord, axis=(1, 2))
    normal = jnp.stack(
        [
            jnp.stack([sum_w, sum_x, sum_y], -1),
            jnp.stack([sum_x, sum_xx, sum_xy], -1),
            jnp.stack([sum_y, sum_xy, sum_yy], -1),
        ],
        1,
    )
    moments = jnp.stack(
        [
            jnp.sum(pixel_weight * difference, axis=(1, 2)),
            jnp.sum(weight_x * difference, axis=(1, 2)),
            jnp.sum(weight_y * difference, axis=(1, 2)),
        ],
        -1,
    )
    packed = jnp.concatenate([normal.reshape(exp_dev, 9), moments], axis=1)
    packed = butterfly_sum(packed, (("row", row_count), ("col", col_count)))
    normal = packed[:, :9].reshape(exp_dev, 3, 3)
    moments = packed[:, 9:]
    plane_fit = solve_three(normal, moments)
    row_coord = centred(row_pos * tile_len + jnp.arange(tile_len, dtype=jnp.int32), height)
    choose = warp_index[:, 0, 0, :]
    warped = warp_tiles(
        choose, plane_fit, xcoord.reshape(1, tile_len), row_coord.reshape(tile_len, 1),
        matched, resample_bank,
    )
    partial_sum = jnp.einsum("ev,eij->vij", picked, warped, preferred_element_type=jnp.float32)
    numerator = lax.psum_scatter(
        partial_sum.astype(jnp.bfloat16), "visit", scatter_dimension=0, tiled=True
    ).astype(jnp.float32)
    coadd_patch = numerator / denominator[:, None, None]
    return (coadd_patch, plane_fit)


def solution(mesh):
    in_specs = (
        P("visit", "row", "col"),
        P("visit", None),
        P(),
        P("visit", "row", "col"),
        P(),
        P("visit", "row", "col", None),
        P("visit", "row", "col", None),
        P("visit", "row", "col"),
    )
    out_specs = (P("visit", "row", "col"), P("visit", None))
    return jax.shard_map(shards, mesh=mesh, in_specs=in_specs, out_specs=out_specs, check_vma=False)
```

```python
import jax
import jax.numpy as jnp
from jax import lax
from jax.sharding import PartitionSpec as P
from jax.experimental import pallas as pl
from jax.experimental.pallas import tpu as pltpu

HALO = 16
STRIP = 32
MAXD = 4


SIGMA_PARTS = (0.0625, 0.125, 0.25)


def extended(value, sides, width):
    for axis, dim in sides:
        devices, length = (lax.axis_size(axis), value.shape[dim])
        last = lax.slice_in_dim(value, length - width, length, axis=dim)
        initial = lax.slice_in_dim(value, 0, width, axis=dim)
        minor = dim == value.ndim - 1
        if minor:
            flat = value.shape[:-2] + (-1,)
            turned = jnp.swapaxes(last, -1, -2).shape
            last = jnp.swapaxes(last, -1, -2).reshape(flat)
            initial = jnp.swapaxes(initial, -1, -2).reshape(flat)
        if devices == 2:
            position = lax.axis_index(axis)
            facing = jnp.where(position == 0, last, initial)
            arrived = lax.ppermute(facing, axis, [(0, 1), (1, 0)])
            empty = jnp.zeros_like(arrived)
            before = jnp.where(position == 1, arrived, empty)
            after = jnp.where(position == 0, arrived, empty)
        else:
            up = [(i, (i + 1) % devices) for i in range(devices - 1)]
            down = [(j, i) for i, j in up]
            before = lax.ppermute(last, axis, up)
            after = lax.ppermute(initial, axis, down)
        if minor:
            before = jnp.swapaxes(before.reshape(turned), -1, -2)
            after = jnp.swapaxes(after.reshape(turned), -1, -2)
        value = jnp.concatenate([before, value, after], axis=dim)
    return value


def band_table(length, width, sigma):
    spread = (jnp.arange(2 * width + 1) - width).astype(jnp.float32)
    curve = jnp.exp(-spread * spread / (2.0 * sigma * sigma))
    total = jnp.sum(curve)
    rows_grid = lax.broadcasted_iota(jnp.int32, (length, length + 2 * width), 0)
    cols_grid = lax.broadcasted_iota(jnp.int32, (length, length + 2 * width), 1)
    offset = (cols_grid - rows_grid - width).astype(jnp.float32)
    values = jnp.exp(-offset * offset / (2.0 * sigma * sigma)) / total
    return jnp.where(jnp.abs(offset) <= width, values, 0.0).astype(jnp.bfloat16)


def centred(index, length):
    return (index.astype(jnp.float32) + 0.5) / length * 2.0 - 1.0


def solve_three(normal, moments):
    lower = jnp.linalg.cholesky(normal)
    first = moments[..., 0] / lower[..., 0, 0]
    second = (moments[..., 1] - lower[..., 1, 0] * first) / lower[..., 1, 1]
    third = (moments[..., 2] - lower[..., 2, 0] * first - lower[..., 2, 1] * second) / lower[
        ..., 2, 2
    ]
    upper_top = third / lower[..., 2, 2]
    upper_mid = (second - lower[..., 2, 1] * upper_top) / lower[..., 1, 1]
    upper_low = (first - lower[..., 1, 0] * upper_mid - lower[..., 2, 0] * upper_top) / lower[
        ..., 0, 0
    ]
    return jnp.stack([upper_low, upper_mid, upper_top], -1)


def butterfly_sum(values, axes):
    for axis, size in axes:
        if size & (size - 1) == 0:
            bit = 1
            while bit < size:
                pairs = [(i, i ^ bit) for i in range(size)]
                values = jax.tree.map(lambda v: v + lax.ppermute(v, axis, pairs), values)
                bit *= 2
        else:
            position = lax.axis_index(axis)
            def gathered(v):
                parts = [v]
                for shift in range(1, size):
                    pairs = [(i, (i + shift) % size) for i in range(size)]
                    parts.append(lax.ppermute(v, axis, pairs))
                stacked = jnp.stack(parts, 0)
                order = (position - jnp.arange(size)) % size
                canonical = jnp.zeros_like(stacked).at[order].set(stacked)
                return jnp.sum(canonical, axis=0)
            values = jax.tree.map(gathered, values)
    return values


def conv_body(coef_ref, vt_ref, ht_ref, padded_ref, out_ref):
    e = pl.program_id(0)
    image = padded_ref[0]
    total = None
    for kernel in range(len(SIGMA_PARTS)):
        across = jnp.dot(vt_ref[0, kernel], image, preferred_element_type=jnp.float32)
        smoothed = lax.dot_general(
            across.astype(jnp.bfloat16), ht_ref[kernel], (((1,), (1,)), ((), ())),
            preferred_element_type=jnp.float32,
        )
        term = coef_ref[e, kernel] * smoothed
        total = term if total is None else total + term
    out_ref[0] = total


def conv_tiles(coeffs, vtables, htables, padded, per_exposure):
    exp_dev, wide = padded.shape[0], padded.shape[1]
    nk, out_rows = vtables.shape[-3], vtables.shape[-2]
    tile_len = htables.shape[1]
    if per_exposure:
        vspec = pl.BlockSpec((1, nk, out_rows, wide), lambda e: (e, 0, 0, 0))
    else:
        vtables = vtables[None]
        vspec = pl.BlockSpec((1, nk, out_rows, wide), lambda e: (0, 0, 0, 0))
    flops = exp_dev * nk * 2 * out_rows * wide * (wide + tile_len)
    moved = exp_dev * wide * wide * 2 + exp_dev * out_rows * tile_len * 4
    return pl.pallas_call(
        conv_body,
        grid=(exp_dev,),
        in_specs=[
            pl.BlockSpec(memory_space=pltpu.SMEM),
            vspec,
            pl.BlockSpec((nk, tile_len, wide), lambda e: (0, 0, 0)),
            pl.BlockSpec((1, wide, wide), lambda e: (e, 0, 0)),
        ],
        out_specs=pl.BlockSpec((1, out_rows, tile_len), lambda e: (e, 0, 0)),
        out_shape=jax.ShapeDtypeStruct((exp_dev, out_rows, tile_len), jnp.float32),
        compiler_params=pltpu.CompilerParams(
            dimension_semantics=("arbitrary",), vmem_limit_bytes=48 * 1024 * 1024
        ),
        cost_estimate=pl.CostEstimate(flops=flops, bytes_accessed=moved, transcendentals=0),
    )(coeffs, vtables, htables, padded)


def warp_body(idx_ref, plane_ref, xrow_ref, ycol_ref, matched_ref, rmap_ref, cmap_ref, out_ref):
    e = pl.program_id(0)
    background = (
        plane_ref[e, 0] + plane_ref[e, 1] * xrow_ref[...]
    ) + plane_ref[e, 2] * ycol_ref[...]
    corrected = (matched_ref[0] - background).astype(jnp.bfloat16)
    halfway = jnp.dot(rmap_ref[0], corrected, preferred_element_type=jnp.float32)
    warped = lax.dot_general(
        halfway.astype(jnp.bfloat16), cmap_ref[0], (((1,), (1,)), ((), ())),
        preferred_element_type=jnp.float32,
    )
    out_ref[0] = warped.astype(jnp.bfloat16)


def warp_tiles(choose, plane, xrow, ycol, matched, bank):
    exp_dev, tile_len = matched.shape[0], matched.shape[1]
    grid_spec = pltpu.PrefetchScalarGridSpec(
        num_scalar_prefetch=1,
        grid=(exp_dev,),
        in_specs=[
            pl.BlockSpec(memory_space=pltpu.SMEM),
            pl.BlockSpec((1, tile_len), lambda e, idx: (0, 0)),
            pl.BlockSpec((tile_len, 1), lambda e, idx: (0, 0)),
            pl.BlockSpec((1, tile_len, tile_len), lambda e, idx: (e, 0, 0)),
            pl.BlockSpec((1, tile_len, tile_len), lambda e, idx: (idx[e, 0], 0, 0)),
            pl.BlockSpec((1, tile_len, tile_len), lambda e, idx: (idx[e, 1], 0, 0)),
        ],
        out_specs=pl.BlockSpec((1, tile_len, tile_len), lambda e, idx: (e, 0, 0)),
    )
    flops = exp_dev * 4 * tile_len ** 3
    moved = exp_dev * tile_len * tile_len * (4 + 2 + 2 + 2)
    return pl.pallas_call(
        warp_body,
        grid_spec=grid_spec,
        out_shape=jax.ShapeDtypeStruct(matched.shape, jnp.bfloat16),
        compiler_params=pltpu.CompilerParams(
            dimension_semantics=("arbitrary",), vmem_limit_bytes=48 * 1024 * 1024
        ),
        cost_estimate=pl.CostEstimate(flops=flops, bytes_accessed=moved, transcendentals=0),
    )(choose, plane, xrow, ycol, matched, bank, bank)


def rows_from(source, anchor):
    return lax.dynamic_slice_in_dim(source, anchor, STRIP, 0)


def shards(images, coeffs, pair_list, weights, resample_bank, warp_index, destinations, counts):
    exp_dev = images.shape[0]
    tile_len = images.shape[1]
    row_count = lax.axis_size("row")
    col_count = lax.axis_size("col")
    visit_count = lax.axis_size("visit")
    row_pos = lax.axis_index("row")
    col_pos = lax.axis_index("col")
    visit_pos = lax.axis_index("visit")
    height = row_count * tile_len
    breadth = col_count * tile_len
    padded = extended(images, (("col", 2), ("row", 1)), HALO)
    own_ids = visit_pos * exp_dev + jnp.arange(exp_dev, dtype=jnp.int32)
    first_col = pair_list[:, 0]
    second_col = pair_list[:, 1]
    offsets = pair_list[:, 2]
    hit_first = first_col[None, :] == own_ids[:, None]
    hit_second = second_col[None, :] == own_ids[:, None]
    partner = jnp.sum(
        jnp.where(hit_first, second_col[None, :], 0) + jnp.where(hit_second, first_col[None, :], 0),
        axis=1,
    )
    offset = jnp.sum(jnp.where(hit_first | hit_second, offsets[None, :], 0), axis=1)
    pick_rows = (
        lax.broadcasted_iota(jnp.int32, (exp_dev, STRIP, tile_len), 2)
        == offset[:, None, None] + lax.broadcasted_iota(jnp.int32, (exp_dev, STRIP, tile_len), 1)
    ).astype(jnp.bfloat16)
    own_strip = jnp.einsum(
        "esr,erl->esl", pick_rows, images, preferred_element_type=jnp.float32
    ).astype(jnp.bfloat16)
    listed = destinations[:, 0, 0, :]
    how_many = counts[:, 0, 0]
    usable = jnp.arange(MAXD, dtype=jnp.int32)[None, :] < how_many[:, None]
    owners = jnp.arange(visit_count, dtype=jnp.int32)
    member = jnp.any(usable[:, :, None] & (listed[:, :, None] == owners[None, None, :]), axis=1)
    tile_weight = weights[:, 0, 0]
    nothing = jnp.zeros((), jnp.bfloat16)
    picked = jnp.where(member, tile_weight[:, None], nothing)
    strip_rows_n = exp_dev * STRIP
    extra = -(-(exp_dev * visit_count) // tile_len)
    extra = -(-extra // 16) * 16
    tail = jnp.zeros((extra * tile_len,), jnp.bfloat16)
    tail = tail.at[: exp_dev * visit_count].set(picked.reshape(-1)).reshape(extra, tile_len)
    payload = jnp.concatenate([own_strip.reshape(strip_rows_n, tile_len), tail], axis=0)
    received = [payload]
    for shift in range(1, visit_count):
        pairs = [(i, (i + shift) % visit_count) for i in range(visit_count)]
        received.append(lax.ppermute(payload, "visit", pairs))
    stacked = jnp.stack(received, 0)
    strips_all = stacked[:, :strip_rows_n].reshape(visit_count * exp_dev, STRIP, tile_len)
    picked_all = stacked[:, strip_rows_n:].reshape(visit_count, -1)[:, : exp_dev * visit_count]
    picked_all = picked_all.reshape(visit_count, exp_dev, visit_count)
    partner_visit = partner // exp_dev
    slot = (visit_pos - partner_visit) % visit_count
    source = slot * exp_dev + partner % exp_dev
    choose_strip = (
        lax.broadcasted_iota(jnp.int32, (exp_dev, visit_count * exp_dev), 1) == source[:, None]
    ).astype(jnp.bfloat16)
    theirs = jnp.einsum(
        "ej,jsl->esl", choose_strip, strips_all, preferred_element_type=jnp.float32
    )
    own_patch = jnp.take(picked_all, visit_pos, axis=2).astype(jnp.float32)
    denominator = jnp.sum(own_patch).reshape(1)
    stacked_tables = jnp.stack([band_table(tile_len, HALO, HALO * part) for part in SIGMA_PARTS])
    strip_tables = jnp.einsum(
        "esr,krj->eksj", pick_rows, stacked_tables, preferred_element_type=jnp.float32
    ).astype(jnp.bfloat16)
    nearby = conv_tiles(coeffs, strip_tables, stacked_tables, padded, True)
    matched = conv_tiles(coeffs, stacked_tables, stacked_tables, padded, False)
    difference = nearby - theirs
    pixel_weight = 1.0 / (1.0 + theirs * theirs)
    strip_rows = row_pos * tile_len + offset[:, None] + jnp.arange(STRIP, dtype=jnp.int32)[None, :]
    ycoord = centred(strip_rows, height)[:, :, None]
    xcoord = centred(col_pos * tile_len + jnp.arange(tile_len, dtype=jnp.int32), breadth)
    xgrid = xcoord[None, None, :]
    weight_x = pixel_weight * xgrid
    weight_y = pixel_weight * ycoord
    sum_w = jnp.sum(pixel_weight, axis=(1, 2))
    sum_x = jnp.sum(weight_x, axis=(1, 2))
    sum_y = jnp.sum(weight_y, axis=(1, 2))
    sum_xx = jnp.sum(weight_x * xgrid, axis=(1, 2))
    sum_xy = jnp.sum(weight_x * ycoord, axis=(1, 2))
    sum_yy = jnp.sum(weight_y * ycoord, axis=(1, 2))
    normal = jnp.stack(
        [
            jnp.stack([sum_w, sum_x, sum_y], -1),
            jnp.stack([sum_x, sum_xx, sum_xy], -1),
            jnp.stack([sum_y, sum_xy, sum_yy], -1),
        ],
        1,
    )
    moments = jnp.stack(
        [
            jnp.sum(pixel_weight * difference, axis=(1, 2)),
            jnp.sum(weight_x * difference, axis=(1, 2)),
            jnp.sum(weight_y * difference, axis=(1, 2)),
        ],
        -1,
    )
    packed = jnp.concatenate([normal.reshape(exp_dev, 9), moments], axis=1)
    packed = butterfly_sum(packed, (("row", row_count), ("col", col_count)))
    normal = packed[:, :9].reshape(exp_dev, 3, 3)
    moments = packed[:, 9:]
    plane_fit = solve_three(normal, moments)
    row_coord = centred(row_pos * tile_len + jnp.arange(tile_len, dtype=jnp.int32), height)
    choose = warp_index[:, 0, 0, :]
    warped = warp_tiles(
        choose, plane_fit, xcoord.reshape(1, tile_len), row_coord.reshape(tile_len, 1),
        matched, resample_bank,
    )
    partial_sum = jnp.einsum("ev,eij->vij", picked, warped, preferred_element_type=jnp.float32)
    numerator = lax.psum_scatter(
        partial_sum.astype(jnp.bfloat16), "visit", scatter_dimension=0, tiled=True
    ).astype(jnp.float32)
    coadd_patch = numerator / denominator[:, None, None]
    return (coadd_patch, plane_fit)


def solution(mesh):
    in_specs = (
        P("visit", "row", "col"),
        P("visit", None),
        P(),
        P("visit", "row", "col"),
        P(),
        P("visit", "row", "col", None),
        P("visit", "row", "col", None),
        P("visit", "row", "col"),
    )
    out_specs = (P("visit", "row", "col"), P("visit", None))
    return jax.shard_map(shards, mesh=mesh, in_specs=in_specs, out_specs=out_specs, check_vma=False)
```

```python
import jax
import jax.numpy as jnp
from jax import lax
from jax.sharding import PartitionSpec as P
from jax.experimental import pallas as pl
from jax.experimental.pallas import tpu as pltpu

HALO = 16
STRIP = 32
MAXD = 4


SIGMA_PARTS = (0.0625, 0.125, 0.25)


def extended(value, sides, width):
    for axis, dim in sides:
        devices, length = (lax.axis_size(axis), value.shape[dim])
        last = lax.slice_in_dim(value, length - width, length, axis=dim)
        initial = lax.slice_in_dim(value, 0, width, axis=dim)
        minor = dim == value.ndim - 1
        if minor:
            flat = value.shape[:-2] + (-1,)
            turned = jnp.swapaxes(last, -1, -2).shape
            last = jnp.swapaxes(last, -1, -2).reshape(flat)
            initial = jnp.swapaxes(initial, -1, -2).reshape(flat)
        if devices == 2:
            position = lax.axis_index(axis)
            facing = jnp.where(position == 0, last, initial)
            arrived = lax.ppermute(facing, axis, [(0, 1), (1, 0)])
            empty = jnp.zeros_like(arrived)
            before = jnp.where(position == 1, arrived, empty)
            after = jnp.where(position == 0, arrived, empty)
        else:
            up = [(i, (i + 1) % devices) for i in range(devices - 1)]
            down = [(j, i) for i, j in up]
            before = lax.ppermute(last, axis, up)
            after = lax.ppermute(initial, axis, down)
        if minor:
            before = jnp.swapaxes(before.reshape(turned), -1, -2)
            after = jnp.swapaxes(after.reshape(turned), -1, -2)
        value = jnp.concatenate([before, value, after], axis=dim)
    return value


def band_table(length, width, sigma):
    spread = (jnp.arange(2 * width + 1) - width).astype(jnp.float32)
    curve = jnp.exp(-spread * spread / (2.0 * sigma * sigma))
    total = jnp.sum(curve)
    rows_grid = lax.broadcasted_iota(jnp.int32, (length, length + 2 * width), 0)
    cols_grid = lax.broadcasted_iota(jnp.int32, (length, length + 2 * width), 1)
    offset = (cols_grid - rows_grid - width).astype(jnp.float32)
    values = jnp.exp(-offset * offset / (2.0 * sigma * sigma)) / total
    return jnp.where(jnp.abs(offset) <= width, values, 0.0).astype(jnp.bfloat16)


def centred(index, length):
    return (index.astype(jnp.float32) + 0.5) / length * 2.0 - 1.0


def solve_three(normal, moments):
    lower = jnp.linalg.cholesky(normal)
    first = moments[..., 0] / lower[..., 0, 0]
    second = (moments[..., 1] - lower[..., 1, 0] * first) / lower[..., 1, 1]
    third = (moments[..., 2] - lower[..., 2, 0] * first - lower[..., 2, 1] * second) / lower[
        ..., 2, 2
    ]
    upper_top = third / lower[..., 2, 2]
    upper_mid = (second - lower[..., 2, 1] * upper_top) / lower[..., 1, 1]
    upper_low = (first - lower[..., 1, 0] * upper_mid - lower[..., 2, 0] * upper_top) / lower[
        ..., 0, 0
    ]
    return jnp.stack([upper_low, upper_mid, upper_top], -1)


def butterfly_sum(values, axes):
    for axis, size in axes:
        if size & (size - 1) == 0:
            bit = 1
            while bit < size:
                pairs = [(i, i ^ bit) for i in range(size)]
                values = jax.tree.map(lambda v: v + lax.ppermute(v, axis, pairs), values)
                bit *= 2
        else:
            position = lax.axis_index(axis)
            def gathered(v):
                parts = [v]
                for shift in range(1, size):
                    pairs = [(i, (i + shift) % size) for i in range(size)]
                    parts.append(lax.ppermute(v, axis, pairs))
                stacked = jnp.stack(parts, 0)
                order = (position - jnp.arange(size)) % size
                canonical = jnp.zeros_like(stacked).at[order].set(stacked)
                return jnp.sum(canonical, axis=0)
            values = jax.tree.map(gathered, values)
    return values


def conv_body(coef_ref, vt_ref, ht_ref, padded_ref, out_ref):
    e = pl.program_id(0)
    image = padded_ref[0]
    total = None
    for kernel in range(len(SIGMA_PARTS)):
        across = jnp.dot(vt_ref[0, kernel], image, preferred_element_type=jnp.float32)
        smoothed = lax.dot_general(
            across.astype(jnp.bfloat16), ht_ref[kernel], (((1,), (1,)), ((), ())),
            preferred_element_type=jnp.float32,
        )
        term = coef_ref[e, kernel] * smoothed
        total = term if total is None else total + term
    out_ref[0] = total


def conv_tiles(coeffs, vtables, htables, padded, per_exposure):
    exp_dev, wide = padded.shape[0], padded.shape[1]
    nk, out_rows = vtables.shape[-3], vtables.shape[-2]
    tile_len = htables.shape[1]
    if per_exposure:
        vspec = pl.BlockSpec((1, nk, out_rows, wide), lambda e: (e, 0, 0, 0))
    else:
        vtables = vtables[None]
        vspec = pl.BlockSpec((1, nk, out_rows, wide), lambda e: (0, 0, 0, 0))
    flops = exp_dev * nk * 2 * out_rows * wide * (wide + tile_len)
    moved = exp_dev * wide * wide * 2 + exp_dev * out_rows * tile_len * 4
    return pl.pallas_call(
        conv_body,
        grid=(exp_dev,),
        in_specs=[
            pl.BlockSpec(memory_space=pltpu.SMEM),
            vspec,
            pl.BlockSpec((nk, tile_len, wide), lambda e: (0, 0, 0)),
            pl.BlockSpec((1, wide, wide), lambda e: (e, 0, 0)),
        ],
        out_specs=pl.BlockSpec((1, out_rows, tile_len), lambda e: (e, 0, 0)),
        out_shape=jax.ShapeDtypeStruct((exp_dev, out_rows, tile_len), jnp.float32),
        compiler_params=pltpu.CompilerParams(
            dimension_semantics=("arbitrary",), vmem_limit_bytes=48 * 1024 * 1024
        ),
        cost_estimate=pl.CostEstimate(flops=flops, bytes_accessed=moved, transcendentals=0),
    )(coeffs, vtables, htables, padded)


BLOCK = 128


def band_body(coef_ref, blk_ref, padded_ref, out_ref):
    e = pl.program_id(0)
    tile_len = out_ref.shape[1]
    total = None
    for kernel in range(len(SIGMA_PARTS)):
        block = blk_ref[kernel]
        rows = [
            jnp.dot(block, padded_ref[0, start:start + 2 * BLOCK, :], preferred_element_type=jnp.float32)
            for start in range(0, tile_len, BLOCK)
        ]
        across = jnp.concatenate(rows, 0).astype(jnp.bfloat16)
        cols = [
            lax.dot_general(
                across[:, start:start + 2 * BLOCK], block, (((1,), (1,)), ((), ())),
                preferred_element_type=jnp.float32,
            )
            for start in range(0, tile_len, BLOCK)
        ]
        term = coef_ref[e, kernel] * jnp.concatenate(cols, 1)
        total = term if total is None else total + term
    out_ref[0] = total


def band_tiles(coeffs, blocks, padded, tile_len):
    exp_dev, wide = padded.shape[0], padded.shape[1]
    nk = blocks.shape[0]
    steps = tile_len // BLOCK
    flops = exp_dev * nk * steps * 2 * BLOCK * 2 * BLOCK * (wide + tile_len)
    moved = exp_dev * wide * wide * 2 + exp_dev * tile_len * tile_len * 4
    return pl.pallas_call(
        band_body,
        grid=(exp_dev,),
        in_specs=[
            pl.BlockSpec(memory_space=pltpu.SMEM),
            pl.BlockSpec((nk, BLOCK, 2 * BLOCK), lambda e: (0, 0, 0)),
            pl.BlockSpec((1, wide, wide), lambda e: (e, 0, 0)),
        ],
        out_specs=pl.BlockSpec((1, tile_len, tile_len), lambda e: (e, 0, 0)),
        out_shape=jax.ShapeDtypeStruct((exp_dev, tile_len, tile_len), jnp.float32),
        compiler_params=pltpu.CompilerParams(
            dimension_semantics=("arbitrary",), vmem_limit_bytes=48 * 1024 * 1024
        ),
        cost_estimate=pl.CostEstimate(flops=flops, bytes_accessed=moved, transcendentals=0),
    )(coeffs, blocks, padded)


def warp_body(idx_ref, plane_ref, xrow_ref, ycol_ref, matched_ref, rmap_ref, cmap_ref, out_ref):
    e = pl.program_id(0)
    background = (
        plane_ref[e, 0] + plane_ref[e, 1] * xrow_ref[...]
    ) + plane_ref[e, 2] * ycol_ref[...]
    corrected = (matched_ref[0] - background).astype(jnp.bfloat16)
    halfway = jnp.dot(rmap_ref[0], corrected, preferred_element_type=jnp.float32)
    warped = lax.dot_general(
        halfway.astype(jnp.bfloat16), cmap_ref[0], (((1,), (1,)), ((), ())),
        preferred_element_type=jnp.float32,
    )
    out_ref[0] = warped.astype(jnp.bfloat16)


def warp_tiles(choose, plane, xrow, ycol, matched, bank):
    exp_dev, tile_len = matched.shape[0], matched.shape[1]
    grid_spec = pltpu.PrefetchScalarGridSpec(
        num_scalar_prefetch=1,
        grid=(exp_dev,),
        in_specs=[
            pl.BlockSpec(memory_space=pltpu.SMEM),
            pl.BlockSpec((1, tile_len), lambda e, idx: (0, 0)),
            pl.BlockSpec((tile_len, 1), lambda e, idx: (0, 0)),
            pl.BlockSpec((1, tile_len, tile_len), lambda e, idx: (e, 0, 0)),
            pl.BlockSpec((1, tile_len, tile_len), lambda e, idx: (idx[e, 0], 0, 0)),
            pl.BlockSpec((1, tile_len, tile_len), lambda e, idx: (idx[e, 1], 0, 0)),
        ],
        out_specs=pl.BlockSpec((1, tile_len, tile_len), lambda e, idx: (e, 0, 0)),
    )
    flops = exp_dev * 4 * tile_len ** 3
    moved = exp_dev * tile_len * tile_len * (4 + 2 + 2 + 2)
    return pl.pallas_call(
        warp_body,
        grid_spec=grid_spec,
        out_shape=jax.ShapeDtypeStruct(matched.shape, jnp.bfloat16),
        compiler_params=pltpu.CompilerParams(
            dimension_semantics=("arbitrary",), vmem_limit_bytes=48 * 1024 * 1024
        ),
        cost_estimate=pl.CostEstimate(flops=flops, bytes_accessed=moved, transcendentals=0),
    )(choose, plane, xrow, ycol, matched, bank, bank)


def rows_from(source, anchor):
    return lax.dynamic_slice_in_dim(source, anchor, STRIP, 0)


def shards(images, coeffs, pair_list, weights, resample_bank, warp_index, destinations, counts):
    exp_dev = images.shape[0]
    tile_len = images.shape[1]
    row_count = lax.axis_size("row")
    col_count = lax.axis_size("col")
    visit_count = lax.axis_size("visit")
    row_pos = lax.axis_index("row")
    col_pos = lax.axis_index("col")
    visit_pos = lax.axis_index("visit")
    height = row_count * tile_len
    breadth = col_count * tile_len
    padded = extended(images, (("col", 2), ("row", 1)), HALO)
    own_ids = visit_pos * exp_dev + jnp.arange(exp_dev, dtype=jnp.int32)
    first_col = pair_list[:, 0]
    second_col = pair_list[:, 1]
    offsets = pair_list[:, 2]
    hit_first = first_col[None, :] == own_ids[:, None]
    hit_second = second_col[None, :] == own_ids[:, None]
    partner = jnp.sum(
        jnp.where(hit_first, second_col[None, :], 0) + jnp.where(hit_second, first_col[None, :], 0),
        axis=1,
    )
    offset = jnp.sum(jnp.where(hit_first | hit_second, offsets[None, :], 0), axis=1)
    pick_rows = (
        lax.broadcasted_iota(jnp.int32, (exp_dev, STRIP, tile_len), 2)
        == offset[:, None, None] + lax.broadcasted_iota(jnp.int32, (exp_dev, STRIP, tile_len), 1)
    ).astype(jnp.bfloat16)
    own_strip = jnp.einsum(
        "esr,erl->esl", pick_rows, images, preferred_element_type=jnp.float32
    ).astype(jnp.bfloat16)
    listed = destinations[:, 0, 0, :]
    how_many = counts[:, 0, 0]
    usable = jnp.arange(MAXD, dtype=jnp.int32)[None, :] < how_many[:, None]
    owners = jnp.arange(visit_count, dtype=jnp.int32)
    member = jnp.any(usable[:, :, None] & (listed[:, :, None] == owners[None, None, :]), axis=1)
    tile_weight = weights[:, 0, 0]
    nothing = jnp.zeros((), jnp.bfloat16)
    picked = jnp.where(member, tile_weight[:, None], nothing)
    strip_rows_n = exp_dev * STRIP
    extra = -(-(exp_dev * visit_count) // tile_len)
    extra = -(-extra // 16) * 16
    tail = jnp.zeros((extra * tile_len,), jnp.bfloat16)
    tail = tail.at[: exp_dev * visit_count].set(picked.reshape(-1)).reshape(extra, tile_len)
    payload = jnp.concatenate([own_strip.reshape(strip_rows_n, tile_len), tail], axis=0)
    received = [payload]
    for shift in range(1, visit_count):
        pairs = [(i, (i + shift) % visit_count) for i in range(visit_count)]
        received.append(lax.ppermute(payload, "visit", pairs))
    stacked = jnp.stack(received, 0)
    strips_all = stacked[:, :strip_rows_n].reshape(visit_count * exp_dev, STRIP, tile_len)
    picked_all = stacked[:, strip_rows_n:].reshape(visit_count, -1)[:, : exp_dev * visit_count]
    picked_all = picked_all.reshape(visit_count, exp_dev, visit_count)
    partner_visit = partner // exp_dev
    slot = (visit_pos - partner_visit) % visit_count
    source = slot * exp_dev + partner % exp_dev
    choose_strip = (
        lax.broadcasted_iota(jnp.int32, (exp_dev, visit_count * exp_dev), 1) == source[:, None]
    ).astype(jnp.bfloat16)
    theirs = jnp.einsum(
        "ej,jsl->esl", choose_strip, strips_all, preferred_element_type=jnp.float32
    )
    own_patch = jnp.take(picked_all, visit_pos, axis=2).astype(jnp.float32)
    denominator = jnp.sum(own_patch).reshape(1)
    stacked_tables = jnp.stack([band_table(tile_len, HALO, HALO * part) for part in SIGMA_PARTS])
    strip_tables = jnp.einsum(
        "esr,krj->eksj", pick_rows, stacked_tables, preferred_element_type=jnp.float32
    ).astype(jnp.bfloat16)
    nearby = conv_tiles(coeffs, strip_tables, stacked_tables, padded, True)
    spare = 2 * BLOCK + tile_len - BLOCK - padded.shape[1]
    roomy = jnp.pad(padded, ((0, 0), (0, spare), (0, spare)))
    blocks = stacked_tables[:, :BLOCK, : 2 * BLOCK]
    matched = band_tiles(coeffs, blocks, roomy, tile_len)
    difference = nearby - theirs
    pixel_weight = 1.0 / (1.0 + theirs * theirs)
    strip_rows = row_pos * tile_len + offset[:, None] + jnp.arange(STRIP, dtype=jnp.int32)[None, :]
    ycoord = centred(strip_rows, height)[:, :, None]
    xcoord = centred(col_pos * tile_len + jnp.arange(tile_len, dtype=jnp.int32), breadth)
    xgrid = xcoord[None, None, :]
    weight_x = pixel_weight * xgrid
    weight_y = pixel_weight * ycoord
    sum_w = jnp.sum(pixel_weight, axis=(1, 2))
    sum_x = jnp.sum(weight_x, axis=(1, 2))
    sum_y = jnp.sum(weight_y, axis=(1, 2))
    sum_xx = jnp.sum(weight_x * xgrid, axis=(1, 2))
    sum_xy = jnp.sum(weight_x * ycoord, axis=(1, 2))
    sum_yy = jnp.sum(weight_y * ycoord, axis=(1, 2))
    normal = jnp.stack(
        [
            jnp.stack([sum_w, sum_x, sum_y], -1),
            jnp.stack([sum_x, sum_xx, sum_xy], -1),
            jnp.stack([sum_y, sum_xy, sum_yy], -1),
        ],
        1,
    )
    moments = jnp.stack(
        [
            jnp.sum(pixel_weight * difference, axis=(1, 2)),
            jnp.sum(weight_x * difference, axis=(1, 2)),
            jnp.sum(weight_y * difference, axis=(1, 2)),
        ],
        -1,
    )
    packed = jnp.concatenate([normal.reshape(exp_dev, 9), moments], axis=1)
    packed = butterfly_sum(packed, (("row", row_count), ("col", col_count)))
    normal = packed[:, :9].reshape(exp_dev, 3, 3)
    moments = packed[:, 9:]
    plane_fit = solve_three(normal, moments)
    row_coord = centred(row_pos * tile_len + jnp.arange(tile_len, dtype=jnp.int32), height)
    choose = warp_index[:, 0, 0, :]
    warped = warp_tiles(
        choose, plane_fit, xcoord.reshape(1, tile_len), row_coord.reshape(tile_len, 1),
        matched, resample_bank,
    )
    partial_sum = jnp.einsum("ev,eij->vij", picked, warped, preferred_element_type=jnp.float32)
    numerator = lax.psum_scatter(
        partial_sum.astype(jnp.bfloat16), "visit", scatter_dimension=0, tiled=True
    ).astype(jnp.float32)
    coadd_patch = numerator / denominator[:, None, None]
    return (coadd_patch, plane_fit)


def solution(mesh):
    in_specs = (
        P("visit", "row", "col"),
        P("visit", None),
        P(),
        P("visit", "row", "col"),
        P(),
        P("visit", "row", "col", None),
        P("visit", "row", "col", None),
        P("visit", "row", "col"),
    )
    out_specs = (P("visit", "row", "col"), P("visit", None))
    return jax.shard_map(shards, mesh=mesh, in_specs=in_specs, out_specs=out_specs, check_vma=False)
```

```python
import jax
import jax.numpy as jnp
from jax import lax
from jax.sharding import PartitionSpec as P
from jax.experimental import pallas as pl
from jax.experimental.pallas import tpu as pltpu

HALO = 16
STRIP = 32
MAXD = 4


SIGMA_PARTS = (0.0625, 0.125, 0.25)


def extended(value, sides, width):
    for axis, dim in sides:
        devices, length = (lax.axis_size(axis), value.shape[dim])
        last = lax.slice_in_dim(value, length - width, length, axis=dim)
        initial = lax.slice_in_dim(value, 0, width, axis=dim)
        minor = dim == value.ndim - 1
        if minor:
            flat = value.shape[:-2] + (-1,)
            turned = jnp.swapaxes(last, -1, -2).shape
            last = jnp.swapaxes(last, -1, -2).reshape(flat)
            initial = jnp.swapaxes(initial, -1, -2).reshape(flat)
        if devices == 2:
            position = lax.axis_index(axis)
            facing = jnp.where(position == 0, last, initial)
            arrived = lax.ppermute(facing, axis, [(0, 1), (1, 0)])
            empty = jnp.zeros_like(arrived)
            before = jnp.where(position == 1, arrived, empty)
            after = jnp.where(position == 0, arrived, empty)
        else:
            up = [(i, (i + 1) % devices) for i in range(devices - 1)]
            down = [(j, i) for i, j in up]
            before = lax.ppermute(last, axis, up)
            after = lax.ppermute(initial, axis, down)
        if minor:
            before = jnp.swapaxes(before.reshape(turned), -1, -2)
            after = jnp.swapaxes(after.reshape(turned), -1, -2)
        value = jnp.concatenate([before, value, after], axis=dim)
    return value


def band_values(offset, width, sigma):
    spread = (jnp.arange(2 * width + 1) - width).astype(jnp.float32)
    curve = jnp.exp(-spread * spread / (2.0 * sigma * sigma))
    total = jnp.sum(curve)
    offset = offset.astype(jnp.float32)
    values = jnp.exp(-offset * offset / (2.0 * sigma * sigma)) / total
    return jnp.where(jnp.abs(offset) <= width, values, 0.0).astype(jnp.bfloat16)


def band_table(length, width, sigma):
    spread = (jnp.arange(2 * width + 1) - width).astype(jnp.float32)
    curve = jnp.exp(-spread * spread / (2.0 * sigma * sigma))
    total = jnp.sum(curve)
    rows_grid = lax.broadcasted_iota(jnp.int32, (length, length + 2 * width), 0)
    cols_grid = lax.broadcasted_iota(jnp.int32, (length, length + 2 * width), 1)
    offset = (cols_grid - rows_grid - width).astype(jnp.float32)
    values = jnp.exp(-offset * offset / (2.0 * sigma * sigma)) / total
    return jnp.where(jnp.abs(offset) <= width, values, 0.0).astype(jnp.bfloat16)


def centred(index, length):
    return (index.astype(jnp.float32) + 0.5) / length * 2.0 - 1.0


def solve_three(normal, moments):
    lower = jnp.linalg.cholesky(normal)
    first = moments[..., 0] / lower[..., 0, 0]
    second = (moments[..., 1] - lower[..., 1, 0] * first) / lower[..., 1, 1]
    third = (moments[..., 2] - lower[..., 2, 0] * first - lower[..., 2, 1] * second) / lower[
        ..., 2, 2
    ]
    upper_top = third / lower[..., 2, 2]
    upper_mid = (second - lower[..., 2, 1] * upper_top) / lower[..., 1, 1]
    upper_low = (first - lower[..., 1, 0] * upper_mid - lower[..., 2, 0] * upper_top) / lower[
        ..., 0, 0
    ]
    return jnp.stack([upper_low, upper_mid, upper_top], -1)


def butterfly_sum(values, axes):
    for axis, size in axes:
        if size & (size - 1) == 0:
            bit = 1
            while bit < size:
                pairs = [(i, i ^ bit) for i in range(size)]
                values = jax.tree.map(lambda v: v + lax.ppermute(v, axis, pairs), values)
                bit *= 2
        else:
            position = lax.axis_index(axis)
            def gathered(v):
                parts = [v]
                for shift in range(1, size):
                    pairs = [(i, (i + shift) % size) for i in range(size)]
                    parts.append(lax.ppermute(v, axis, pairs))
                stacked = jnp.stack(parts, 0)
                order = (position - jnp.arange(size)) % size
                canonical = jnp.zeros_like(stacked).at[order].set(stacked)
                return jnp.sum(canonical, axis=0)
            values = jax.tree.map(gathered, values)
    return values


def conv_body(coef_ref, vt_ref, ht_ref, padded_ref, out_ref):
    e = pl.program_id(0)
    image = padded_ref[0]
    total = None
    for kernel in range(len(SIGMA_PARTS)):
        across = jnp.dot(vt_ref[0, kernel], image, preferred_element_type=jnp.float32)
        smoothed = lax.dot_general(
            across.astype(jnp.bfloat16), ht_ref[kernel], (((1,), (1,)), ((), ())),
            preferred_element_type=jnp.float32,
        )
        term = coef_ref[e, kernel] * smoothed
        total = term if total is None else total + term
    out_ref[0] = total


def conv_tiles(coeffs, vtables, htables, padded, per_exposure):
    exp_dev, wide = padded.shape[0], padded.shape[1]
    nk, out_rows = vtables.shape[-3], vtables.shape[-2]
    tile_len = htables.shape[1]
    if per_exposure:
        vspec = pl.BlockSpec((1, nk, out_rows, wide), lambda e: (e, 0, 0, 0))
    else:
        vtables = vtables[None]
        vspec = pl.BlockSpec((1, nk, out_rows, wide), lambda e: (0, 0, 0, 0))
    flops = exp_dev * nk * 2 * out_rows * wide * (wide + tile_len)
    moved = exp_dev * wide * wide * 2 + exp_dev * out_rows * tile_len * 4
    return pl.pallas_call(
        conv_body,
        grid=(exp_dev,),
        in_specs=[
            pl.BlockSpec(memory_space=pltpu.SMEM),
            vspec,
            pl.BlockSpec((nk, tile_len, wide), lambda e: (0, 0, 0)),
            pl.BlockSpec((1, wide, wide), lambda e: (e, 0, 0)),
        ],
        out_specs=pl.BlockSpec((1, out_rows, tile_len), lambda e: (e, 0, 0)),
        out_shape=jax.ShapeDtypeStruct((exp_dev, out_rows, tile_len), jnp.float32),
        compiler_params=pltpu.CompilerParams(
            dimension_semantics=("arbitrary",), vmem_limit_bytes=48 * 1024 * 1024
        ),
        cost_estimate=pl.CostEstimate(flops=flops, bytes_accessed=moved, transcendentals=0),
    )(coeffs, vtables, htables, padded)


BLOCK = 128


def band_body(coef_ref, blk_ref, padded_ref, out_ref):
    e = pl.program_id(0)
    tile_len = out_ref.shape[1]
    total = None
    for kernel in range(len(SIGMA_PARTS)):
        block = blk_ref[kernel]
        rows = [
            jnp.dot(block, padded_ref[0, start:start + 2 * BLOCK, :], preferred_element_type=jnp.float32)
            for start in range(0, tile_len, BLOCK)
        ]
        across = jnp.concatenate(rows, 0).astype(jnp.bfloat16)
        cols = [
            lax.dot_general(
                across[:, start:start + 2 * BLOCK], block, (((1,), (1,)), ((), ())),
                preferred_element_type=jnp.float32,
            )
            for start in range(0, tile_len, BLOCK)
        ]
        term = coef_ref[e, kernel] * jnp.concatenate(cols, 1)
        total = term if total is None else total + term
    out_ref[0] = total


def band_tiles(coeffs, blocks, padded, tile_len):
    exp_dev, wide = padded.shape[0], padded.shape[1]
    nk = blocks.shape[0]
    steps = tile_len // BLOCK
    flops = exp_dev * nk * steps * 2 * BLOCK * 2 * BLOCK * (wide + tile_len)
    moved = exp_dev * wide * wide * 2 + exp_dev * tile_len * tile_len * 4
    return pl.pallas_call(
        band_body,
        grid=(exp_dev,),
        in_specs=[
            pl.BlockSpec(memory_space=pltpu.SMEM),
            pl.BlockSpec((nk, BLOCK, 2 * BLOCK), lambda e: (0, 0, 0)),
            pl.BlockSpec((1, wide, wide), lambda e: (e, 0, 0)),
        ],
        out_specs=pl.BlockSpec((1, tile_len, tile_len), lambda e: (e, 0, 0)),
        out_shape=jax.ShapeDtypeStruct((exp_dev, tile_len, tile_len), jnp.float32),
        compiler_params=pltpu.CompilerParams(
            dimension_semantics=("arbitrary",), vmem_limit_bytes=48 * 1024 * 1024
        ),
        cost_estimate=pl.CostEstimate(flops=flops, bytes_accessed=moved, transcendentals=0),
    )(coeffs, blocks, padded)


def strip_body(coef_ref, st_ref, blk_ref, padded_ref, out_ref):
    e = pl.program_id(0)
    tile_len = out_ref.shape[2]
    image = padded_ref[0]
    total = None
    for kernel in range(len(SIGMA_PARTS)):
        block = blk_ref[kernel]
        across = jnp.dot(st_ref[0, kernel], image, preferred_element_type=jnp.float32)
        across = across.astype(jnp.bfloat16)
        cols = [
            lax.dot_general(
                across[:, start:start + 2 * BLOCK], block, (((1,), (1,)), ((), ())),
                preferred_element_type=jnp.float32,
            )
            for start in range(0, tile_len, BLOCK)
        ]
        term = coef_ref[e, kernel] * jnp.concatenate(cols, 1)
        total = term if total is None else total + term
    out_ref[0] = total


def strip_tiles(coeffs, strip_tables, blocks, padded, tile_len):
    exp_dev, wide = padded.shape[0], padded.shape[1]
    nk, rows = strip_tables.shape[1], strip_tables.shape[2]
    flops = exp_dev * nk * 2 * rows * (wide * wide + 2 * BLOCK * tile_len)
    moved = exp_dev * wide * wide * 2 + exp_dev * rows * tile_len * 4
    return pl.pallas_call(
        strip_body,
        grid=(exp_dev,),
        in_specs=[
            pl.BlockSpec(memory_space=pltpu.SMEM),
            pl.BlockSpec((1, nk, rows, wide), lambda e: (e, 0, 0, 0)),
            pl.BlockSpec((nk, BLOCK, 2 * BLOCK), lambda e: (0, 0, 0)),
            pl.BlockSpec((1, wide, wide), lambda e: (e, 0, 0)),
        ],
        out_specs=pl.BlockSpec((1, rows, tile_len), lambda e: (e, 0, 0)),
        out_shape=jax.ShapeDtypeStruct((exp_dev, rows, tile_len), jnp.float32),
        compiler_params=pltpu.CompilerParams(
            dimension_semantics=("arbitrary",), vmem_limit_bytes=48 * 1024 * 1024
        ),
        cost_estimate=pl.CostEstimate(flops=flops, bytes_accessed=moved, transcendentals=0),
    )(coeffs, strip_tables, blocks, padded)


def warp_body(idx_ref, plane_ref, xrow_ref, ycol_ref, matched_ref, rmap_ref, cmap_ref, out_ref):
    e = pl.program_id(0)
    background = (
        plane_ref[e, 0] + plane_ref[e, 1] * xrow_ref[...]
    ) + plane_ref[e, 2] * ycol_ref[...]
    corrected = (matched_ref[0] - background).astype(jnp.bfloat16)
    halfway = jnp.dot(rmap_ref[0], corrected, preferred_element_type=jnp.float32)
    warped = lax.dot_general(
        halfway.astype(jnp.bfloat16), cmap_ref[0], (((1,), (1,)), ((), ())),
        preferred_element_type=jnp.float32,
    )
    out_ref[0] = warped.astype(jnp.bfloat16)


def warp_tiles(choose, plane, xrow, ycol, matched, bank):
    exp_dev, tile_len = matched.shape[0], matched.shape[1]
    grid_spec = pltpu.PrefetchScalarGridSpec(
        num_scalar_prefetch=1,
        grid=(exp_dev,),
        in_specs=[
            pl.BlockSpec(memory_space=pltpu.SMEM),
            pl.BlockSpec((1, tile_len), lambda e, idx: (0, 0)),
            pl.BlockSpec((tile_len, 1), lambda e, idx: (0, 0)),
            pl.BlockSpec((1, tile_len, tile_len), lambda e, idx: (e, 0, 0)),
            pl.BlockSpec((1, tile_len, tile_len), lambda e, idx: (idx[e, 0], 0, 0)),
            pl.BlockSpec((1, tile_len, tile_len), lambda e, idx: (idx[e, 1], 0, 0)),
        ],
        out_specs=pl.BlockSpec((1, tile_len, tile_len), lambda e, idx: (e, 0, 0)),
    )
    flops = exp_dev * 4 * tile_len ** 3
    moved = exp_dev * tile_len * tile_len * (4 + 2 + 2 + 2)
    return pl.pallas_call(
        warp_body,
        grid_spec=grid_spec,
        out_shape=jax.ShapeDtypeStruct(matched.shape, jnp.bfloat16),
        compiler_params=pltpu.CompilerParams(
            dimension_semantics=("arbitrary",), vmem_limit_bytes=48 * 1024 * 1024
        ),
        cost_estimate=pl.CostEstimate(flops=flops, bytes_accessed=moved, transcendentals=0),
    )(choose, plane, xrow, ycol, matched, bank, bank)


def rows_from(source, anchor):
    return lax.dynamic_slice_in_dim(source, anchor, STRIP, 0)


def shards(images, coeffs, pair_list, weights, resample_bank, warp_index, destinations, counts):
    exp_dev = images.shape[0]
    tile_len = images.shape[1]
    row_count = lax.axis_size("row")
    col_count = lax.axis_size("col")
    visit_count = lax.axis_size("visit")
    row_pos = lax.axis_index("row")
    col_pos = lax.axis_index("col")
    visit_pos = lax.axis_index("visit")
    height = row_count * tile_len
    breadth = col_count * tile_len
    padded = extended(images, (("col", 2), ("row", 1)), HALO)
    own_ids = visit_pos * exp_dev + jnp.arange(exp_dev, dtype=jnp.int32)
    first_col = pair_list[:, 0]
    second_col = pair_list[:, 1]
    offsets = pair_list[:, 2]
    hit_first = first_col[None, :] == own_ids[:, None]
    hit_second = second_col[None, :] == own_ids[:, None]
    partner = jnp.sum(
        jnp.where(hit_first, second_col[None, :], 0) + jnp.where(hit_second, first_col[None, :], 0),
        axis=1,
    )
    offset = jnp.sum(jnp.where(hit_first | hit_second, offsets[None, :], 0), axis=1)
    pick_rows = (
        lax.broadcasted_iota(jnp.int32, (exp_dev, STRIP, tile_len), 2)
        == offset[:, None, None] + lax.broadcasted_iota(jnp.int32, (exp_dev, STRIP, tile_len), 1)
    ).astype(jnp.bfloat16)
    own_strip = jnp.einsum(
        "esr,erl->esl", pick_rows, images, preferred_element_type=jnp.float32
    ).astype(jnp.bfloat16)
    listed = destinations[:, 0, 0, :]
    how_many = counts[:, 0, 0]
    usable = jnp.arange(MAXD, dtype=jnp.int32)[None, :] < how_many[:, None]
    owners = jnp.arange(visit_count, dtype=jnp.int32)
    member = jnp.any(usable[:, :, None] & (listed[:, :, None] == owners[None, None, :]), axis=1)
    tile_weight = weights[:, 0, 0]
    nothing = jnp.zeros((), jnp.bfloat16)
    picked = jnp.where(member, tile_weight[:, None], nothing)
    strip_rows_n = exp_dev * STRIP
    extra = -(-(exp_dev * visit_count) // tile_len)
    extra = -(-extra // 16) * 16
    tail = jnp.zeros((extra * tile_len,), jnp.bfloat16)
    tail = tail.at[: exp_dev * visit_count].set(picked.reshape(-1)).reshape(extra, tile_len)
    payload = jnp.concatenate([own_strip.reshape(strip_rows_n, tile_len), tail], axis=0)
    received = [payload]
    for shift in range(1, visit_count):
        pairs = [(i, (i + shift) % visit_count) for i in range(visit_count)]
        received.append(lax.ppermute(payload, "visit", pairs))
    stacked = jnp.stack(received, 0)
    strips_all = stacked[:, :strip_rows_n].reshape(visit_count * exp_dev, STRIP, tile_len)
    picked_all = stacked[:, strip_rows_n:].reshape(visit_count, -1)[:, : exp_dev * visit_count]
    picked_all = picked_all.reshape(visit_count, exp_dev, visit_count)
    partner_visit = partner // exp_dev
    slot = (visit_pos - partner_visit) % visit_count
    source = slot * exp_dev + partner % exp_dev
    choose_strip = (
        lax.broadcasted_iota(jnp.int32, (exp_dev, visit_count * exp_dev), 1) == source[:, None]
    ).astype(jnp.bfloat16)
    theirs = jnp.einsum(
        "ej,jsl->esl", choose_strip, strips_all, preferred_element_type=jnp.float32
    )
    own_patch = jnp.take(picked_all, visit_pos, axis=2).astype(jnp.float32)
    denominator = jnp.sum(own_patch).reshape(1)
    spare = 2 * BLOCK + tile_len - BLOCK - (tile_len + 2 * HALO)
    roomy = jnp.pad(padded, ((0, 0), (0, spare), (0, spare)))
    wide = roomy.shape[1]
    block_offset = (
        lax.broadcasted_iota(jnp.int32, (BLOCK, 2 * BLOCK), 1)
        - lax.broadcasted_iota(jnp.int32, (BLOCK, 2 * BLOCK), 0)
        - HALO
    )
    blocks = jnp.stack([band_values(block_offset, HALO, HALO * part) for part in SIGMA_PARTS])
    strip_offset = (
        lax.broadcasted_iota(jnp.int32, (exp_dev, STRIP, wide), 2)
        - lax.broadcasted_iota(jnp.int32, (exp_dev, STRIP, wide), 1)
        - offset[:, None, None]
        - HALO
    )
    strip_tables = jnp.stack(
        [band_values(strip_offset, HALO, HALO * part) for part in SIGMA_PARTS], 1
    )
    nearby = strip_tiles(coeffs, strip_tables, blocks, roomy, tile_len)
    matched = band_tiles(coeffs, blocks, roomy, tile_len)
    difference = nearby - theirs
    pixel_weight = 1.0 / (1.0 + theirs * theirs)
    strip_rows = row_pos * tile_len + offset[:, None] + jnp.arange(STRIP, dtype=jnp.int32)[None, :]
    ycoord = centred(strip_rows, height)[:, :, None]
    xcoord = centred(col_pos * tile_len + jnp.arange(tile_len, dtype=jnp.int32), breadth)
    xgrid = xcoord[None, None, :]
    weight_x = pixel_weight * xgrid
    weight_y = pixel_weight * ycoord
    sum_w = jnp.sum(pixel_weight, axis=(1, 2))
    sum_x = jnp.sum(weight_x, axis=(1, 2))
    sum_y = jnp.sum(weight_y, axis=(1, 2))
    sum_xx = jnp.sum(weight_x * xgrid, axis=(1, 2))
    sum_xy = jnp.sum(weight_x * ycoord, axis=(1, 2))
    sum_yy = jnp.sum(weight_y * ycoord, axis=(1, 2))
    normal = jnp.stack(
        [
            jnp.stack([sum_w, sum_x, sum_y], -1),
            jnp.stack([sum_x, sum_xx, sum_xy], -1),
            jnp.stack([sum_y, sum_xy, sum_yy], -1),
        ],
        1,
    )
    moments = jnp.stack(
        [
            jnp.sum(pixel_weight * difference, axis=(1, 2)),
            jnp.sum(weight_x * difference, axis=(1, 2)),
            jnp.sum(weight_y * difference, axis=(1, 2)),
        ],
        -1,
    )
    packed = jnp.concatenate([normal.reshape(exp_dev, 9), moments], axis=1)
    packed = butterfly_sum(packed, (("row", row_count), ("col", col_count)))
    normal = packed[:, :9].reshape(exp_dev, 3, 3)
    moments = packed[:, 9:]
    plane_fit = solve_three(normal, moments)
    row_coord = centred(row_pos * tile_len + jnp.arange(tile_len, dtype=jnp.int32), height)
    choose = warp_index[:, 0, 0, :]
    warped = warp_tiles(
        choose, plane_fit, xcoord.reshape(1, tile_len), row_coord.reshape(tile_len, 1),
        matched, resample_bank,
    )
    partial_sum = jnp.einsum("ev,eij->vij", picked, warped, preferred_element_type=jnp.float32)
    numerator = lax.psum_scatter(
        partial_sum.astype(jnp.bfloat16), "visit", scatter_dimension=0, tiled=True
    ).astype(jnp.float32)
    coadd_patch = numerator / denominator[:, None, None]
    return (coadd_patch, plane_fit)


def solution(mesh):
    in_specs = (
        P("visit", "row", "col"),
        P("visit", None),
        P(),
        P("visit", "row", "col"),
        P(),
        P("visit", "row", "col", None),
        P("visit", "row", "col", None),
        P("visit", "row", "col"),
    )
    out_specs = (P("visit", "row", "col"), P("visit", None))
    return jax.shard_map(shards, mesh=mesh, in_specs=in_specs, out_specs=out_specs, check_vma=False)
```

```python
import jax
import jax.numpy as jnp
from jax import lax
from jax.sharding import PartitionSpec as P
from jax.experimental import pallas as pl
from jax.experimental.pallas import tpu as pltpu

HALO = 16
STRIP = 32
MAXD = 4


SIGMA_PARTS = (0.0625, 0.125, 0.25)


def extended(value, sides, width):
    for axis, dim in sides:
        devices, length = (lax.axis_size(axis), value.shape[dim])
        last = lax.slice_in_dim(value, length - width, length, axis=dim)
        initial = lax.slice_in_dim(value, 0, width, axis=dim)
        minor = dim == value.ndim - 1
        if minor:
            flat = value.shape[:-2] + (-1,)
            turned = jnp.swapaxes(last, -1, -2).shape
            last = jnp.swapaxes(last, -1, -2).reshape(flat)
            initial = jnp.swapaxes(initial, -1, -2).reshape(flat)
        if devices == 2:
            position = lax.axis_index(axis)
            facing = jnp.where(position == 0, last, initial)
            arrived = lax.ppermute(facing, axis, [(0, 1), (1, 0)])
            empty = jnp.zeros_like(arrived)
            before = jnp.where(position == 1, arrived, empty)
            after = jnp.where(position == 0, arrived, empty)
        else:
            up = [(i, (i + 1) % devices) for i in range(devices - 1)]
            down = [(j, i) for i, j in up]
            before = lax.ppermute(last, axis, up)
            after = lax.ppermute(initial, axis, down)
        if minor:
            before = jnp.swapaxes(before.reshape(turned), -1, -2)
            after = jnp.swapaxes(after.reshape(turned), -1, -2)
        value = jnp.concatenate([before, value, after], axis=dim)
    return value


def band_table(length, width, sigma):
    spread = (jnp.arange(2 * width + 1) - width).astype(jnp.float32)
    curve = jnp.exp(-spread * spread / (2.0 * sigma * sigma))
    total = jnp.sum(curve)
    rows_grid = lax.broadcasted_iota(jnp.int32, (length, length + 2 * width), 0)
    cols_grid = lax.broadcasted_iota(jnp.int32, (length, length + 2 * width), 1)
    offset = (cols_grid - rows_grid - width).astype(jnp.float32)
    values = jnp.exp(-offset * offset / (2.0 * sigma * sigma)) / total
    return jnp.where(jnp.abs(offset) <= width, values, 0.0).astype(jnp.bfloat16)


def centred(index, length):
    return (index.astype(jnp.float32) + 0.5) / length * 2.0 - 1.0


def solve_three(normal, moments):
    lower = jnp.linalg.cholesky(normal)
    first = moments[..., 0] / lower[..., 0, 0]
    second = (moments[..., 1] - lower[..., 1, 0] * first) / lower[..., 1, 1]
    third = (moments[..., 2] - lower[..., 2, 0] * first - lower[..., 2, 1] * second) / lower[
        ..., 2, 2
    ]
    upper_top = third / lower[..., 2, 2]
    upper_mid = (second - lower[..., 2, 1] * upper_top) / lower[..., 1, 1]
    upper_low = (first - lower[..., 1, 0] * upper_mid - lower[..., 2, 0] * upper_top) / lower[
        ..., 0, 0
    ]
    return jnp.stack([upper_low, upper_mid, upper_top], -1)


def butterfly_sum(values, axes):
    for axis, size in axes:
        if size & (size - 1) == 0:
            bit = 1
            while bit < size:
                pairs = [(i, i ^ bit) for i in range(size)]
                values = jax.tree.map(lambda v: v + lax.ppermute(v, axis, pairs), values)
                bit *= 2
        else:
            position = lax.axis_index(axis)
            def gathered(v):
                parts = [v]
                for shift in range(1, size):
                    pairs = [(i, (i + shift) % size) for i in range(size)]
                    parts.append(lax.ppermute(v, axis, pairs))
                stacked = jnp.stack(parts, 0)
                order = (position - jnp.arange(size)) % size
                canonical = jnp.zeros_like(stacked).at[order].set(stacked)
                return jnp.sum(canonical, axis=0)
            values = jax.tree.map(gathered, values)
    return values


def conv_body(coef_ref, vt_ref, ht_ref, padded_ref, out_ref):
    e = pl.program_id(0)
    image = padded_ref[0]
    total = None
    for kernel in range(len(SIGMA_PARTS)):
        across = jnp.dot(vt_ref[0, kernel], image, preferred_element_type=jnp.float32)
        smoothed = lax.dot_general(
            across.astype(jnp.bfloat16), ht_ref[kernel], (((1,), (1,)), ((), ())),
            preferred_element_type=jnp.float32,
        )
        term = coef_ref[e, kernel] * smoothed
        total = term if total is None else total + term
    out_ref[0] = total


def conv_tiles(coeffs, vtables, htables, padded, per_exposure):
    exp_dev, wide = padded.shape[0], padded.shape[1]
    nk, out_rows = vtables.shape[-3], vtables.shape[-2]
    tile_len = htables.shape[1]
    if per_exposure:
        vspec = pl.BlockSpec((1, nk, out_rows, wide), lambda e: (e, 0, 0, 0))
    else:
        vtables = vtables[None]
        vspec = pl.BlockSpec((1, nk, out_rows, wide), lambda e: (0, 0, 0, 0))
    flops = exp_dev * nk * 2 * out_rows * wide * (wide + tile_len)
    moved = exp_dev * wide * wide * 2 + exp_dev * out_rows * tile_len * 4
    return pl.pallas_call(
        conv_body,
        grid=(exp_dev,),
        in_specs=[
            pl.BlockSpec(memory_space=pltpu.SMEM),
            vspec,
            pl.BlockSpec((nk, tile_len, wide), lambda e: (0, 0, 0)),
            pl.BlockSpec((1, wide, wide), lambda e: (e, 0, 0)),
        ],
        out_specs=pl.BlockSpec((1, out_rows, tile_len), lambda e: (e, 0, 0)),
        out_shape=jax.ShapeDtypeStruct((exp_dev, out_rows, tile_len), jnp.float32),
        compiler_params=pltpu.CompilerParams(
            dimension_semantics=("arbitrary",), vmem_limit_bytes=48 * 1024 * 1024
        ),
        cost_estimate=pl.CostEstimate(flops=flops, bytes_accessed=moved, transcendentals=0),
    )(coeffs, vtables, htables, padded)


BLOCK = 128


def band_body(coef_ref, blk_ref, padded_ref, out_ref):
    e = pl.program_id(0)
    tile_len = out_ref.shape[1]
    total = None
    for kernel in range(len(SIGMA_PARTS)):
        block = blk_ref[kernel]
        rows = [
            jnp.dot(block, padded_ref[0, start:start + 2 * BLOCK, :], preferred_element_type=jnp.float32)
            for start in range(0, tile_len, BLOCK)
        ]
        across = jnp.concatenate(rows, 0).astype(jnp.bfloat16)
        cols = [
            lax.dot_general(
                across[:, start:start + 2 * BLOCK], block, (((1,), (1,)), ((), ())),
                preferred_element_type=jnp.float32,
            )
            for start in range(0, tile_len, BLOCK)
        ]
        term = coef_ref[e, kernel] * jnp.concatenate(cols, 1)
        total = term if total is None else total + term
    out_ref[0] = total


def band_tiles(coeffs, blocks, padded, tile_len):
    exp_dev, wide = padded.shape[0], padded.shape[1]
    nk = blocks.shape[0]
    steps = tile_len // BLOCK
    flops = exp_dev * nk * steps * 2 * BLOCK * 2 * BLOCK * (wide + tile_len)
    moved = exp_dev * wide * wide * 2 + exp_dev * tile_len * tile_len * 4
    return pl.pallas_call(
        band_body,
        grid=(exp_dev,),
        in_specs=[
            pl.BlockSpec(memory_space=pltpu.SMEM),
            pl.BlockSpec((nk, BLOCK, 2 * BLOCK), lambda e: (0, 0, 0)),
            pl.BlockSpec((1, wide, wide), lambda e: (e, 0, 0)),
        ],
        out_specs=pl.BlockSpec((1, tile_len, tile_len), lambda e: (e, 0, 0)),
        out_shape=jax.ShapeDtypeStruct((exp_dev, tile_len, tile_len), jnp.float32),
        compiler_params=pltpu.CompilerParams(
            dimension_semantics=("arbitrary",), vmem_limit_bytes=48 * 1024 * 1024
        ),
        cost_estimate=pl.CostEstimate(flops=flops, bytes_accessed=moved, transcendentals=0),
    )(coeffs, blocks, padded)


def warp_body(idx_ref, plane_ref, pick_ref, xrow_ref, ycol_ref, matched_ref, rmap_ref, cmap_ref,
              out_ref, acc_ref):
    e = pl.program_id(0)
    background = (
        plane_ref[e, 0] + plane_ref[e, 1] * xrow_ref[...]
    ) + plane_ref[e, 2] * ycol_ref[...]
    corrected = (matched_ref[0] - background).astype(jnp.bfloat16)
    halfway = jnp.dot(rmap_ref[0], corrected, preferred_element_type=jnp.float32)
    warped = lax.dot_general(
        halfway.astype(jnp.bfloat16), cmap_ref[0], (((1,), (1,)), ((), ())),
        preferred_element_type=jnp.float32,
    )
    warped = warped.astype(jnp.bfloat16).astype(jnp.float32)
    patches = acc_ref.shape[0]

    @pl.when(e == 0)
    def _():
        for v in range(patches):
            acc_ref[v] = pick_ref[e, v] * warped

    @pl.when(e > 0)
    def _():
        for v in range(patches):
            acc_ref[v] = acc_ref[v] + pick_ref[e, v] * warped

    @pl.when(e == pl.num_programs(0) - 1)
    def _():
        out_ref[...] = acc_ref[...].astype(jnp.bfloat16)


def warp_tiles(choose, plane, picked, xrow, ycol, matched, bank):
    exp_dev, tile_len = matched.shape[0], matched.shape[1]
    patches = picked.shape[1]
    grid_spec = pltpu.PrefetchScalarGridSpec(
        num_scalar_prefetch=1,
        grid=(exp_dev,),
        in_specs=[
            pl.BlockSpec(memory_space=pltpu.SMEM),
            pl.BlockSpec(memory_space=pltpu.SMEM),
            pl.BlockSpec((1, tile_len), lambda e, idx: (0, 0)),
            pl.BlockSpec((tile_len, 1), lambda e, idx: (0, 0)),
            pl.BlockSpec((1, tile_len, tile_len), lambda e, idx: (e, 0, 0)),
            pl.BlockSpec((1, tile_len, tile_len), lambda e, idx: (idx[e, 0], 0, 0)),
            pl.BlockSpec((1, tile_len, tile_len), lambda e, idx: (idx[e, 1], 0, 0)),
        ],
        out_specs=pl.BlockSpec((patches, tile_len, tile_len), lambda e, idx: (0, 0, 0)),
        scratch_shapes=[pltpu.VMEM((patches, tile_len, tile_len), jnp.float32)],
    )
    flops = exp_dev * 4 * tile_len ** 3
    moved = exp_dev * tile_len * tile_len * (4 + 2 + 2) + patches * tile_len * tile_len * 2
    vmem = min(60 * 1024 * 1024, (16 + 3 * patches) * 1024 * 1024)
    return pl.pallas_call(
        warp_body,
        grid_spec=grid_spec,
        out_shape=jax.ShapeDtypeStruct((patches, tile_len, tile_len), jnp.bfloat16),
        compiler_params=pltpu.CompilerParams(
            dimension_semantics=("arbitrary",), vmem_limit_bytes=vmem
        ),
        cost_estimate=pl.CostEstimate(flops=flops, bytes_accessed=moved, transcendentals=0),
    )(choose, plane, picked, xrow, ycol, matched, bank, bank)


def rows_from(source, anchor):
    return lax.dynamic_slice_in_dim(source, anchor, STRIP, 0)


def shards(images, coeffs, pair_list, weights, resample_bank, warp_index, destinations, counts):
    exp_dev = images.shape[0]
    tile_len = images.shape[1]
    row_count = lax.axis_size("row")
    col_count = lax.axis_size("col")
    visit_count = lax.axis_size("visit")
    row_pos = lax.axis_index("row")
    col_pos = lax.axis_index("col")
    visit_pos = lax.axis_index("visit")
    height = row_count * tile_len
    breadth = col_count * tile_len
    padded = extended(images, (("col", 2), ("row", 1)), HALO)
    own_ids = visit_pos * exp_dev + jnp.arange(exp_dev, dtype=jnp.int32)
    first_col = pair_list[:, 0]
    second_col = pair_list[:, 1]
    offsets = pair_list[:, 2]
    hit_first = first_col[None, :] == own_ids[:, None]
    hit_second = second_col[None, :] == own_ids[:, None]
    partner = jnp.sum(
        jnp.where(hit_first, second_col[None, :], 0) + jnp.where(hit_second, first_col[None, :], 0),
        axis=1,
    )
    offset = jnp.sum(jnp.where(hit_first | hit_second, offsets[None, :], 0), axis=1)
    pick_rows = (
        lax.broadcasted_iota(jnp.int32, (exp_dev, STRIP, tile_len), 2)
        == offset[:, None, None] + lax.broadcasted_iota(jnp.int32, (exp_dev, STRIP, tile_len), 1)
    ).astype(jnp.bfloat16)
    own_strip = jnp.einsum(
        "esr,erl->esl", pick_rows, images, preferred_element_type=jnp.float32
    ).astype(jnp.bfloat16)
    listed = destinations[:, 0, 0, :]
    how_many = counts[:, 0, 0]
    usable = jnp.arange(MAXD, dtype=jnp.int32)[None, :] < how_many[:, None]
    owners = jnp.arange(visit_count, dtype=jnp.int32)
    member = jnp.any(usable[:, :, None] & (listed[:, :, None] == owners[None, None, :]), axis=1)
    tile_weight = weights[:, 0, 0]
    nothing = jnp.zeros((), jnp.bfloat16)
    picked = jnp.where(member, tile_weight[:, None], nothing)
    strip_rows_n = exp_dev * STRIP
    extra = -(-(exp_dev * visit_count) // tile_len)
    extra = -(-extra // 16) * 16
    tail = jnp.zeros((extra * tile_len,), jnp.bfloat16)
    tail = tail.at[: exp_dev * visit_count].set(picked.reshape(-1)).reshape(extra, tile_len)
    payload = jnp.concatenate([own_strip.reshape(strip_rows_n, tile_len), tail], axis=0)
    received = [payload]
    for shift in range(1, visit_count):
        pairs = [(i, (i + shift) % visit_count) for i in range(visit_count)]
        received.append(lax.ppermute(payload, "visit", pairs))
    stacked = jnp.stack(received, 0)
    strips_all = stacked[:, :strip_rows_n].reshape(visit_count * exp_dev, STRIP, tile_len)
    picked_all = stacked[:, strip_rows_n:].reshape(visit_count, -1)[:, : exp_dev * visit_count]
    picked_all = picked_all.reshape(visit_count, exp_dev, visit_count)
    partner_visit = partner // exp_dev
    slot = (visit_pos - partner_visit) % visit_count
    source = slot * exp_dev + partner % exp_dev
    choose_strip = (
        lax.broadcasted_iota(jnp.int32, (exp_dev, visit_count * exp_dev), 1) == source[:, None]
    ).astype(jnp.bfloat16)
    theirs = jnp.einsum(
        "ej,jsl->esl", choose_strip, strips_all, preferred_element_type=jnp.float32
    )
    own_patch = jnp.take(picked_all, visit_pos, axis=2).astype(jnp.float32)
    denominator = jnp.sum(own_patch).reshape(1)
    stacked_tables = jnp.stack([band_table(tile_len, HALO, HALO * part) for part in SIGMA_PARTS])
    strip_tables = jnp.einsum(
        "esr,krj->eksj", pick_rows, stacked_tables, preferred_element_type=jnp.float32
    ).astype(jnp.bfloat16)
    nearby = conv_tiles(coeffs, strip_tables, stacked_tables, padded, True)
    spare = 2 * BLOCK + tile_len - BLOCK - padded.shape[1]
    roomy = jnp.pad(padded, ((0, 0), (0, spare), (0, spare)))
    blocks = stacked_tables[:, :BLOCK, : 2 * BLOCK]
    matched = band_tiles(coeffs, blocks, roomy, tile_len)
    difference = nearby - theirs
    pixel_weight = 1.0 / (1.0 + theirs * theirs)
    strip_rows = row_pos * tile_len + offset[:, None] + jnp.arange(STRIP, dtype=jnp.int32)[None, :]
    ycoord = centred(strip_rows, height)[:, :, None]
    xcoord = centred(col_pos * tile_len + jnp.arange(tile_len, dtype=jnp.int32), breadth)
    xgrid = xcoord[None, None, :]
    weight_x = pixel_weight * xgrid
    weight_y = pixel_weight * ycoord
    sum_w = jnp.sum(pixel_weight, axis=(1, 2))
    sum_x = jnp.sum(weight_x, axis=(1, 2))
    sum_y = jnp.sum(weight_y, axis=(1, 2))
    sum_xx = jnp.sum(weight_x * xgrid, axis=(1, 2))
    sum_xy = jnp.sum(weight_x * ycoord, axis=(1, 2))
    sum_yy = jnp.sum(weight_y * ycoord, axis=(1, 2))
    normal = jnp.stack(
        [
            jnp.stack([sum_w, sum_x, sum_y], -1),
            jnp.stack([sum_x, sum_xx, sum_xy], -1),
            jnp.stack([sum_y, sum_xy, sum_yy], -1),
        ],
        1,
    )
    moments = jnp.stack(
        [
            jnp.sum(pixel_weight * difference, axis=(1, 2)),
            jnp.sum(weight_x * difference, axis=(1, 2)),
            jnp.sum(weight_y * difference, axis=(1, 2)),
        ],
        -1,
    )
    packed = jnp.concatenate([normal.reshape(exp_dev, 9), moments], axis=1)
    packed = butterfly_sum(packed, (("row", row_count), ("col", col_count)))
    normal = packed[:, :9].reshape(exp_dev, 3, 3)
    moments = packed[:, 9:]
    plane_fit = solve_three(normal, moments)
    row_coord = centred(row_pos * tile_len + jnp.arange(tile_len, dtype=jnp.int32), height)
    choose = warp_index[:, 0, 0, :]
    partial_sum = warp_tiles(
        choose, plane_fit, picked.astype(jnp.float32), xcoord.reshape(1, tile_len),
        row_coord.reshape(tile_len, 1), matched, resample_bank,
    )
    numerator = lax.psum_scatter(
        partial_sum, "visit", scatter_dimension=0, tiled=True
    ).astype(jnp.float32)
    coadd_patch = numerator / denominator[:, None, None]
    return (coadd_patch, plane_fit)


def solution(mesh):
    in_specs = (
        P("visit", "row", "col"),
        P("visit", None),
        P(),
        P("visit", "row", "col"),
        P(),
        P("visit", "row", "col", None),
        P("visit", "row", "col", None),
        P("visit", "row", "col"),
    )
    out_specs = (P("visit", "row", "col"), P("visit", None))
    return jax.shard_map(shards, mesh=mesh, in_specs=in_specs, out_specs=out_specs, check_vma=False)
```

```python
import jax
import jax.numpy as jnp
from jax import lax
from jax.sharding import PartitionSpec as P
from jax.experimental import pallas as pl
from jax.experimental.pallas import tpu as pltpu

HALO = 16
STRIP = 32
MAXD = 4


SIGMA_PARTS = (0.0625, 0.125, 0.25)


def extended(value, sides, width):
    for axis, dim in sides:
        devices, length = (lax.axis_size(axis), value.shape[dim])
        last = lax.slice_in_dim(value, length - width, length, axis=dim)
        initial = lax.slice_in_dim(value, 0, width, axis=dim)
        minor = dim == value.ndim - 1
        if minor:
            flat = value.shape[:-2] + (-1,)
            turned = jnp.swapaxes(last, -1, -2).shape
            last = jnp.swapaxes(last, -1, -2).reshape(flat)
            initial = jnp.swapaxes(initial, -1, -2).reshape(flat)
        if devices == 2:
            position = lax.axis_index(axis)
            facing = jnp.where(position == 0, last, initial)
            arrived = lax.ppermute(facing, axis, [(0, 1), (1, 0)])
            empty = jnp.zeros_like(arrived)
            before = jnp.where(position == 1, arrived, empty)
            after = jnp.where(position == 0, arrived, empty)
        else:
            up = [(i, (i + 1) % devices) for i in range(devices - 1)]
            down = [(j, i) for i, j in up]
            before = lax.ppermute(last, axis, up)
            after = lax.ppermute(initial, axis, down)
        if minor:
            before = jnp.swapaxes(before.reshape(turned), -1, -2)
            after = jnp.swapaxes(after.reshape(turned), -1, -2)
        value = jnp.concatenate([before, value, after], axis=dim)
    return value


def band_table(length, width, sigma):
    spread = (jnp.arange(2 * width + 1) - width).astype(jnp.float32)
    curve = jnp.exp(-spread * spread / (2.0 * sigma * sigma))
    total = jnp.sum(curve)
    rows_grid = lax.broadcasted_iota(jnp.int32, (length, length + 2 * width), 0)
    cols_grid = lax.broadcasted_iota(jnp.int32, (length, length + 2 * width), 1)
    offset = (cols_grid - rows_grid - width).astype(jnp.float32)
    values = jnp.exp(-offset * offset / (2.0 * sigma * sigma)) / total
    return jnp.where(jnp.abs(offset) <= width, values, 0.0).astype(jnp.bfloat16)


def centred(index, length):
    return (index.astype(jnp.float32) + 0.5) / length * 2.0 - 1.0


def solve_three(normal, moments):
    lower = jnp.linalg.cholesky(normal)
    first = moments[..., 0] / lower[..., 0, 0]
    second = (moments[..., 1] - lower[..., 1, 0] * first) / lower[..., 1, 1]
    third = (moments[..., 2] - lower[..., 2, 0] * first - lower[..., 2, 1] * second) / lower[
        ..., 2, 2
    ]
    upper_top = third / lower[..., 2, 2]
    upper_mid = (second - lower[..., 2, 1] * upper_top) / lower[..., 1, 1]
    upper_low = (first - lower[..., 1, 0] * upper_mid - lower[..., 2, 0] * upper_top) / lower[
        ..., 0, 0
    ]
    return jnp.stack([upper_low, upper_mid, upper_top], -1)


def butterfly_sum(values, axes):
    for axis, size in axes:
        if size & (size - 1) == 0:
            bit = 1
            while bit < size:
                pairs = [(i, i ^ bit) for i in range(size)]
                values = jax.tree.map(lambda v: v + lax.ppermute(v, axis, pairs), values)
                bit *= 2
        else:
            position = lax.axis_index(axis)
            def gathered(v):
                parts = [v]
                for shift in range(1, size):
                    pairs = [(i, (i + shift) % size) for i in range(size)]
                    parts.append(lax.ppermute(v, axis, pairs))
                stacked = jnp.stack(parts, 0)
                order = (position - jnp.arange(size)) % size
                canonical = jnp.zeros_like(stacked).at[order].set(stacked)
                return jnp.sum(canonical, axis=0)
            values = jax.tree.map(gathered, values)
    return values


def conv_body(coef_ref, vt_ref, ht_ref, padded_ref, out_ref):
    e = pl.program_id(0)
    image = padded_ref[0]
    total = None
    for kernel in range(len(SIGMA_PARTS)):
        across = jnp.dot(vt_ref[0, kernel], image, preferred_element_type=jnp.float32)
        smoothed = lax.dot_general(
            across.astype(jnp.bfloat16), ht_ref[kernel], (((1,), (1,)), ((), ())),
            preferred_element_type=jnp.float32,
        )
        term = coef_ref[e, kernel] * smoothed
        total = term if total is None else total + term
    out_ref[0] = total


def conv_tiles(coeffs, vtables, htables, padded, per_exposure):
    exp_dev, wide = padded.shape[0], padded.shape[1]
    nk, out_rows = vtables.shape[-3], vtables.shape[-2]
    tile_len = htables.shape[1]
    if per_exposure:
        vspec = pl.BlockSpec((1, nk, out_rows, wide), lambda e: (e, 0, 0, 0))
    else:
        vtables = vtables[None]
        vspec = pl.BlockSpec((1, nk, out_rows, wide), lambda e: (0, 0, 0, 0))
    flops = exp_dev * nk * 2 * out_rows * wide * (wide + tile_len)
    moved = exp_dev * wide * wide * 2 + exp_dev * out_rows * tile_len * 4
    return pl.pallas_call(
        conv_body,
        grid=(exp_dev,),
        in_specs=[
            pl.BlockSpec(memory_space=pltpu.SMEM),
            vspec,
            pl.BlockSpec((nk, tile_len, wide), lambda e: (0, 0, 0)),
            pl.BlockSpec((1, wide, wide), lambda e: (e, 0, 0)),
        ],
        out_specs=pl.BlockSpec((1, out_rows, tile_len), lambda e: (e, 0, 0)),
        out_shape=jax.ShapeDtypeStruct((exp_dev, out_rows, tile_len), jnp.float32),
        compiler_params=pltpu.CompilerParams(
            dimension_semantics=("arbitrary",), vmem_limit_bytes=48 * 1024 * 1024
        ),
        cost_estimate=pl.CostEstimate(flops=flops, bytes_accessed=moved, transcendentals=0),
    )(coeffs, vtables, htables, padded)


BLOCK = 128


def band_body(coef_ref, blk_ref, padded_ref, out_ref):
    e = pl.program_id(0)
    tile_len = out_ref.shape[1]
    total = None
    for kernel in range(len(SIGMA_PARTS)):
        block = blk_ref[kernel]
        rows = [
            jnp.dot(block, padded_ref[0, start:start + 2 * BLOCK, :], preferred_element_type=jnp.float32)
            for start in range(0, tile_len, BLOCK)
        ]
        across = jnp.concatenate(rows, 0).astype(jnp.bfloat16)
        cols = [
            lax.dot_general(
                across[:, start:start + 2 * BLOCK], block, (((1,), (1,)), ((), ())),
                preferred_element_type=jnp.float32,
            )
            for start in range(0, tile_len, BLOCK)
        ]
        term = coef_ref[e, kernel] * jnp.concatenate(cols, 1)
        total = term if total is None else total + term
    out_ref[0] = total


def band_tiles(coeffs, blocks, padded, tile_len):
    exp_dev, wide = padded.shape[0], padded.shape[1]
    nk = blocks.shape[0]
    steps = tile_len // BLOCK
    flops = exp_dev * nk * steps * 2 * BLOCK * 2 * BLOCK * (wide + tile_len)
    moved = exp_dev * wide * wide * 2 + exp_dev * tile_len * tile_len * 4
    return pl.pallas_call(
        band_body,
        grid=(exp_dev,),
        in_specs=[
            pl.BlockSpec(memory_space=pltpu.SMEM),
            pl.BlockSpec((nk, BLOCK, 2 * BLOCK), lambda e: (0, 0, 0)),
            pl.BlockSpec((1, wide, wide), lambda e: (e, 0, 0)),
        ],
        out_specs=pl.BlockSpec((1, tile_len, tile_len), lambda e: (e, 0, 0)),
        out_shape=jax.ShapeDtypeStruct((exp_dev, tile_len, tile_len), jnp.float32),
        compiler_params=pltpu.CompilerParams(
            dimension_semantics=("arbitrary",), vmem_limit_bytes=48 * 1024 * 1024
        ),
        cost_estimate=pl.CostEstimate(flops=flops, bytes_accessed=moved, transcendentals=0),
    )(coeffs, blocks, padded)


def warp_body(idx_ref, plane_ref, pick_ref, xrow_ref, ycol_ref, matched_ref, rmap_ref, cmap_ref,
              out_ref, acc_ref):
    e = pl.program_id(0)
    background = (
        plane_ref[e, 0] + plane_ref[e, 1] * xrow_ref[...]
    ) + plane_ref[e, 2] * ycol_ref[...]
    corrected = (matched_ref[0] - background).astype(jnp.bfloat16)
    halfway = jnp.dot(rmap_ref[0], corrected, preferred_element_type=jnp.float32)
    warped = lax.dot_general(
        halfway.astype(jnp.bfloat16), cmap_ref[0], (((1,), (1,)), ((), ())),
        preferred_element_type=jnp.float32,
    )
    warped = warped.astype(jnp.bfloat16).astype(jnp.float32)
    patches = acc_ref.shape[0]

    @pl.when(e == 0)
    def _():
        for v in range(patches):
            acc_ref[v] = pick_ref[e, v] * warped

    @pl.when(e > 0)
    def _():
        for v in range(patches):
            acc_ref[v] = acc_ref[v] + pick_ref[e, v] * warped

    @pl.when(e == pl.num_programs(0) - 1)
    def _():
        out_ref[...] = acc_ref[...].astype(jnp.bfloat16)


def warp_tiles(choose, plane, picked, xrow, ycol, matched, bank):
    exp_dev, tile_len = matched.shape[0], matched.shape[1]
    patches = picked.shape[1]
    grid_spec = pltpu.PrefetchScalarGridSpec(
        num_scalar_prefetch=1,
        grid=(exp_dev,),
        in_specs=[
            pl.BlockSpec(memory_space=pltpu.SMEM),
            pl.BlockSpec(memory_space=pltpu.SMEM),
            pl.BlockSpec((1, tile_len), lambda e, idx: (0, 0)),
            pl.BlockSpec((tile_len, 1), lambda e, idx: (0, 0)),
            pl.BlockSpec((1, tile_len, tile_len), lambda e, idx: (e, 0, 0)),
            pl.BlockSpec((1, tile_len, tile_len), lambda e, idx: (idx[e, 0], 0, 0)),
            pl.BlockSpec((1, tile_len, tile_len), lambda e, idx: (idx[e, 1], 0, 0)),
        ],
        out_specs=pl.BlockSpec((patches, tile_len, tile_len), lambda e, idx: (0, 0, 0)),
        scratch_shapes=[pltpu.VMEM((patches, tile_len, tile_len), jnp.float32)],
    )
    flops = exp_dev * 4 * tile_len ** 3
    moved = exp_dev * tile_len * tile_len * (4 + 2 + 2) + patches * tile_len * tile_len * 2
    vmem = 60 * 1024 * 1024
    return pl.pallas_call(
        warp_body,
        grid_spec=grid_spec,
        out_shape=jax.ShapeDtypeStruct((patches, tile_len, tile_len), jnp.bfloat16),
        compiler_params=pltpu.CompilerParams(
            dimension_semantics=("arbitrary",), vmem_limit_bytes=vmem
        ),
        cost_estimate=pl.CostEstimate(flops=flops, bytes_accessed=moved, transcendentals=0),
    )(choose, plane, picked, xrow, ycol, matched, bank, bank)


def rows_from(source, anchor):
    return lax.dynamic_slice_in_dim(source, anchor, STRIP, 0)


def shards(images, coeffs, pair_list, weights, resample_bank, warp_index, destinations, counts):
    exp_dev = images.shape[0]
    tile_len = images.shape[1]
    row_count = lax.axis_size("row")
    col_count = lax.axis_size("col")
    visit_count = lax.axis_size("visit")
    row_pos = lax.axis_index("row")
    col_pos = lax.axis_index("col")
    visit_pos = lax.axis_index("visit")
    height = row_count * tile_len
    breadth = col_count * tile_len
    padded = extended(images, (("col", 2), ("row", 1)), HALO)
    own_ids = visit_pos * exp_dev + jnp.arange(exp_dev, dtype=jnp.int32)
    first_col = pair_list[:, 0]
    second_col = pair_list[:, 1]
    offsets = pair_list[:, 2]
    hit_first = first_col[None, :] == own_ids[:, None]
    hit_second = second_col[None, :] == own_ids[:, None]
    partner = jnp.sum(
        jnp.where(hit_first, second_col[None, :], 0) + jnp.where(hit_second, first_col[None, :], 0),
        axis=1,
    )
    offset = jnp.sum(jnp.where(hit_first | hit_second, offsets[None, :], 0), axis=1)
    pick_rows = (
        lax.broadcasted_iota(jnp.int32, (exp_dev, STRIP, tile_len), 2)
        == offset[:, None, None] + lax.broadcasted_iota(jnp.int32, (exp_dev, STRIP, tile_len), 1)
    ).astype(jnp.bfloat16)
    own_strip = jnp.einsum(
        "esr,erl->esl", pick_rows, images, preferred_element_type=jnp.float32
    ).astype(jnp.bfloat16)
    listed = destinations[:, 0, 0, :]
    how_many = counts[:, 0, 0]
    usable = jnp.arange(MAXD, dtype=jnp.int32)[None, :] < how_many[:, None]
    owners = jnp.arange(visit_count, dtype=jnp.int32)
    member = jnp.any(usable[:, :, None] & (listed[:, :, None] == owners[None, None, :]), axis=1)
    tile_weight = weights[:, 0, 0]
    nothing = jnp.zeros((), jnp.bfloat16)
    picked = jnp.where(member, tile_weight[:, None], nothing)
    strip_rows_n = exp_dev * STRIP
    extra = -(-(exp_dev * visit_count) // tile_len)
    extra = -(-extra // 16) * 16
    tail = jnp.zeros((extra * tile_len,), jnp.bfloat16)
    tail = tail.at[: exp_dev * visit_count].set(picked.reshape(-1)).reshape(extra, tile_len)
    payload = jnp.concatenate([own_strip.reshape(strip_rows_n, tile_len), tail], axis=0)
    received = [payload]
    for shift in range(1, visit_count):
        pairs = [(i, (i + shift) % visit_count) for i in range(visit_count)]
        received.append(lax.ppermute(payload, "visit", pairs))
    stacked = jnp.stack(received, 0)
    strips_all = stacked[:, :strip_rows_n].reshape(visit_count * exp_dev, STRIP, tile_len)
    picked_all = stacked[:, strip_rows_n:].reshape(visit_count, -1)[:, : exp_dev * visit_count]
    picked_all = picked_all.reshape(visit_count, exp_dev, visit_count)
    partner_visit = partner // exp_dev
    slot = (visit_pos - partner_visit) % visit_count
    source = slot * exp_dev + partner % exp_dev
    choose_strip = (
        lax.broadcasted_iota(jnp.int32, (exp_dev, visit_count * exp_dev), 1) == source[:, None]
    ).astype(jnp.bfloat16)
    theirs = jnp.einsum(
        "ej,jsl->esl", choose_strip, strips_all, preferred_element_type=jnp.float32
    )
    own_patch = jnp.take(picked_all, visit_pos, axis=2).astype(jnp.float32)
    denominator = jnp.sum(own_patch).reshape(1)
    stacked_tables = jnp.stack([band_table(tile_len, HALO, HALO * part) for part in SIGMA_PARTS])
    strip_tables = jnp.einsum(
        "esr,krj->eksj", pick_rows, stacked_tables, preferred_element_type=jnp.float32
    ).astype(jnp.bfloat16)
    nearby = conv_tiles(coeffs, strip_tables, stacked_tables, padded, True)
    spare = 2 * BLOCK + tile_len - BLOCK - padded.shape[1]
    roomy = jnp.pad(padded, ((0, 0), (0, spare), (0, spare)))
    blocks = stacked_tables[:, :BLOCK, : 2 * BLOCK]
    matched = band_tiles(coeffs, blocks, roomy, tile_len)
    difference = nearby - theirs
    pixel_weight = 1.0 / (1.0 + theirs * theirs)
    strip_rows = row_pos * tile_len + offset[:, None] + jnp.arange(STRIP, dtype=jnp.int32)[None, :]
    ycoord = centred(strip_rows, height)[:, :, None]
    xcoord = centred(col_pos * tile_len + jnp.arange(tile_len, dtype=jnp.int32), breadth)
    xgrid = xcoord[None, None, :]
    weight_x = pixel_weight * xgrid
    weight_y = pixel_weight * ycoord
    sum_w = jnp.sum(pixel_weight, axis=(1, 2))
    sum_x = jnp.sum(weight_x, axis=(1, 2))
    sum_y = jnp.sum(weight_y, axis=(1, 2))
    sum_xx = jnp.sum(weight_x * xgrid, axis=(1, 2))
    sum_xy = jnp.sum(weight_x * ycoord, axis=(1, 2))
    sum_yy = jnp.sum(weight_y * ycoord, axis=(1, 2))
    normal = jnp.stack(
        [
            jnp.stack([sum_w, sum_x, sum_y], -1),
            jnp.stack([sum_x, sum_xx, sum_xy], -1),
            jnp.stack([sum_y, sum_xy, sum_yy], -1),
        ],
        1,
    )
    moments = jnp.stack(
        [
            jnp.sum(pixel_weight * difference, axis=(1, 2)),
            jnp.sum(weight_x * difference, axis=(1, 2)),
            jnp.sum(weight_y * difference, axis=(1, 2)),
        ],
        -1,
    )
    packed = jnp.concatenate([normal.reshape(exp_dev, 9), moments], axis=1)
    packed = butterfly_sum(packed, (("row", row_count), ("col", col_count)))
    normal = packed[:, :9].reshape(exp_dev, 3, 3)
    moments = packed[:, 9:]
    plane_fit = solve_three(normal, moments)
    row_coord = centred(row_pos * tile_len + jnp.arange(tile_len, dtype=jnp.int32), height)
    choose = warp_index[:, 0, 0, :]
    partial_sum = warp_tiles(
        choose, plane_fit, picked.astype(jnp.float32), xcoord.reshape(1, tile_len),
        row_coord.reshape(tile_len, 1), matched, resample_bank,
    )
    numerator = lax.psum_scatter(
        partial_sum, "visit", scatter_dimension=0, tiled=True
    ).astype(jnp.float32)
    coadd_patch = numerator / denominator[:, None, None]
    return (coadd_patch, plane_fit)


def solution(mesh):
    in_specs = (
        P("visit", "row", "col"),
        P("visit", None),
        P(),
        P("visit", "row", "col"),
        P(),
        P("visit", "row", "col", None),
        P("visit", "row", "col", None),
        P("visit", "row", "col"),
    )
    out_specs = (P("visit", "row", "col"), P("visit", None))
    return jax.shard_map(shards, mesh=mesh, in_specs=in_specs, out_specs=out_specs, check_vma=False)
```

```python
import functools

import jax
import jax.numpy as jnp
from jax import lax
from jax.sharding import PartitionSpec as P
from jax.experimental import pallas as pl
from jax.experimental.pallas import tpu as pltpu

HALO = 16
STRIP = 32
MAXD = 4


SIGMA_PARTS = (0.0625, 0.125, 0.25)


def extended(value, sides, width):
    for axis, dim in sides:
        devices, length = (lax.axis_size(axis), value.shape[dim])
        last = lax.slice_in_dim(value, length - width, length, axis=dim)
        initial = lax.slice_in_dim(value, 0, width, axis=dim)
        minor = dim == value.ndim - 1
        if minor:
            flat = value.shape[:-2] + (-1,)
            turned = jnp.swapaxes(last, -1, -2).shape
            last = jnp.swapaxes(last, -1, -2).reshape(flat)
            initial = jnp.swapaxes(initial, -1, -2).reshape(flat)
        if devices == 2:
            position = lax.axis_index(axis)
            facing = jnp.where(position == 0, last, initial)
            arrived = lax.ppermute(facing, axis, [(0, 1), (1, 0)])
            empty = jnp.zeros_like(arrived)
            before = jnp.where(position == 1, arrived, empty)
            after = jnp.where(position == 0, arrived, empty)
        else:
            up = [(i, (i + 1) % devices) for i in range(devices - 1)]
            down = [(j, i) for i, j in up]
            before = lax.ppermute(last, axis, up)
            after = lax.ppermute(initial, axis, down)
        if minor:
            before = jnp.swapaxes(before.reshape(turned), -1, -2)
            after = jnp.swapaxes(after.reshape(turned), -1, -2)
        value = jnp.concatenate([before, value, after], axis=dim)
    return value


def band_table(length, width, sigma):
    spread = (jnp.arange(2 * width + 1) - width).astype(jnp.float32)
    curve = jnp.exp(-spread * spread / (2.0 * sigma * sigma))
    total = jnp.sum(curve)
    rows_grid = lax.broadcasted_iota(jnp.int32, (length, length + 2 * width), 0)
    cols_grid = lax.broadcasted_iota(jnp.int32, (length, length + 2 * width), 1)
    offset = (cols_grid - rows_grid - width).astype(jnp.float32)
    values = jnp.exp(-offset * offset / (2.0 * sigma * sigma)) / total
    return jnp.where(jnp.abs(offset) <= width, values, 0.0).astype(jnp.bfloat16)


def centred(index, length):
    return (index.astype(jnp.float32) + 0.5) / length * 2.0 - 1.0


def solve_three(normal, moments):
    lower = jnp.linalg.cholesky(normal)
    first = moments[..., 0] / lower[..., 0, 0]
    second = (moments[..., 1] - lower[..., 1, 0] * first) / lower[..., 1, 1]
    third = (moments[..., 2] - lower[..., 2, 0] * first - lower[..., 2, 1] * second) / lower[
        ..., 2, 2
    ]
    upper_top = third / lower[..., 2, 2]
    upper_mid = (second - lower[..., 2, 1] * upper_top) / lower[..., 1, 1]
    upper_low = (first - lower[..., 1, 0] * upper_mid - lower[..., 2, 0] * upper_top) / lower[
        ..., 0, 0
    ]
    return jnp.stack([upper_low, upper_mid, upper_top], -1)


def butterfly_sum(values, axes):
    for axis, size in axes:
        if size & (size - 1) == 0:
            bit = 1
            while bit < size:
                pairs = [(i, i ^ bit) for i in range(size)]
                values = jax.tree.map(lambda v: v + lax.ppermute(v, axis, pairs), values)
                bit *= 2
        else:
            position = lax.axis_index(axis)
            def gathered(v):
                parts = [v]
                for shift in range(1, size):
                    pairs = [(i, (i + shift) % size) for i in range(size)]
                    parts.append(lax.ppermute(v, axis, pairs))
                stacked = jnp.stack(parts, 0)
                order = (position - jnp.arange(size)) % size
                canonical = jnp.zeros_like(stacked).at[order].set(stacked)
                return jnp.sum(canonical, axis=0)
            values = jax.tree.map(gathered, values)
    return values


def conv_body(coef_ref, vt_ref, ht_ref, padded_ref, out_ref):
    e = pl.program_id(0)
    image = padded_ref[0]
    total = None
    for kernel in range(len(SIGMA_PARTS)):
        across = jnp.dot(vt_ref[0, kernel], image, preferred_element_type=jnp.float32)
        smoothed = lax.dot_general(
            across.astype(jnp.bfloat16), ht_ref[kernel], (((1,), (1,)), ((), ())),
            preferred_element_type=jnp.float32,
        )
        term = coef_ref[e, kernel] * smoothed
        total = term if total is None else total + term
    out_ref[0] = total


def conv_tiles(coeffs, vtables, htables, padded, per_exposure):
    exp_dev, wide = padded.shape[0], padded.shape[1]
    nk, out_rows = vtables.shape[-3], vtables.shape[-2]
    tile_len = htables.shape[1]
    if per_exposure:
        vspec = pl.BlockSpec((1, nk, out_rows, wide), lambda e: (e, 0, 0, 0))
    else:
        vtables = vtables[None]
        vspec = pl.BlockSpec((1, nk, out_rows, wide), lambda e: (0, 0, 0, 0))
    flops = exp_dev * nk * 2 * out_rows * wide * (wide + tile_len)
    moved = exp_dev * wide * wide * 2 + exp_dev * out_rows * tile_len * 4
    return pl.pallas_call(
        conv_body,
        grid=(exp_dev,),
        in_specs=[
            pl.BlockSpec(memory_space=pltpu.SMEM),
            vspec,
            pl.BlockSpec((nk, tile_len, wide), lambda e: (0, 0, 0)),
            pl.BlockSpec((1, wide, wide), lambda e: (e, 0, 0)),
        ],
        out_specs=pl.BlockSpec((1, out_rows, tile_len), lambda e: (e, 0, 0)),
        out_shape=jax.ShapeDtypeStruct((exp_dev, out_rows, tile_len), jnp.float32),
        compiler_params=pltpu.CompilerParams(
            dimension_semantics=("arbitrary",), vmem_limit_bytes=48 * 1024 * 1024
        ),
        cost_estimate=pl.CostEstimate(flops=flops, bytes_accessed=moved, transcendentals=0),
    )(coeffs, vtables, htables, padded)


BLOCK = 128


def band_body(first, coef_ref, blk_ref, padded_ref, *rest):
    out_ref = rest[-1]
    e = pl.program_id(0) + first
    tile_len = out_ref.shape[1]
    total = None
    for kernel in range(len(SIGMA_PARTS)):
        block = blk_ref[kernel]
        rows = [
            jnp.dot(block, padded_ref[0, start:start + 2 * BLOCK, :], preferred_element_type=jnp.float32)
            for start in range(0, tile_len, BLOCK)
        ]
        across = jnp.concatenate(rows, 0).astype(jnp.bfloat16)
        cols = [
            lax.dot_general(
                across[:, start:start + 2 * BLOCK], block, (((1,), (1,)), ((), ())),
                preferred_element_type=jnp.float32,
            )
            for start in range(0, tile_len, BLOCK)
        ]
        term = coef_ref[e, kernel] * jnp.concatenate(cols, 1)
        total = term if total is None else total + term
    out_ref[0] = total


def band_tiles(coeffs, blocks, padded, tile_len, first, count, into):
    exp_dev, wide = padded.shape[0], padded.shape[1]
    nk = blocks.shape[0]
    steps = tile_len // BLOCK
    flops = count * nk * steps * 2 * BLOCK * 2 * BLOCK * (wide + tile_len)
    moved = count * wide * wide * 2 + count * tile_len * tile_len * 4
    in_specs = [
        pl.BlockSpec(memory_space=pltpu.SMEM),
        pl.BlockSpec((nk, BLOCK, 2 * BLOCK), lambda e: (0, 0, 0)),
        pl.BlockSpec((1, wide, wide), lambda e: (e + first, 0, 0)),
    ]
    operands = [coeffs, blocks, padded]
    aliases = {}
    if into is not None:
        in_specs.append(pl.BlockSpec(memory_space=pl.ANY))
        operands.append(into)
        aliases = {3: 0}
    return pl.pallas_call(
        functools.partial(band_body, first),
        grid=(count,),
        in_specs=in_specs,
        out_specs=pl.BlockSpec((1, tile_len, tile_len), lambda e: (e + first, 0, 0)),
        out_shape=jax.ShapeDtypeStruct((exp_dev, tile_len, tile_len), jnp.float32),
        input_output_aliases=aliases,
        compiler_params=pltpu.CompilerParams(
            dimension_semantics=("arbitrary",), vmem_limit_bytes=48 * 1024 * 1024
        ),
        cost_estimate=pl.CostEstimate(flops=flops, bytes_accessed=moved, transcendentals=0),
    )(*operands)


def warp_body(idx_ref, plane_ref, pick_ref, xrow_ref, ycol_ref, matched_ref, rmap_ref, cmap_ref,
              out_ref, acc_ref):
    e = pl.program_id(0)
    background = (
        plane_ref[e, 0] + plane_ref[e, 1] * xrow_ref[...]
    ) + plane_ref[e, 2] * ycol_ref[...]
    corrected = (matched_ref[0] - background).astype(jnp.bfloat16)
    halfway = jnp.dot(rmap_ref[0], corrected, preferred_element_type=jnp.float32)
    warped = lax.dot_general(
        halfway.astype(jnp.bfloat16), cmap_ref[0], (((1,), (1,)), ((), ())),
        preferred_element_type=jnp.float32,
    )
    warped = warped.astype(jnp.bfloat16).astype(jnp.float32)
    patches = acc_ref.shape[0]

    @pl.when(e == 0)
    def _():
        for v in range(patches):
            acc_ref[v] = pick_ref[e, v] * warped

    @pl.when(e > 0)
    def _():
        for v in range(patches):
            acc_ref[v] = acc_ref[v] + pick_ref[e, v] * warped

    @pl.when(e == pl.num_programs(0) - 1)
    def _():
        out_ref[...] = acc_ref[...].astype(jnp.bfloat16)


def warp_tiles(choose, plane, picked, xrow, ycol, matched, bank):
    exp_dev, tile_len = matched.shape[0], matched.shape[1]
    patches = picked.shape[1]
    grid_spec = pltpu.PrefetchScalarGridSpec(
        num_scalar_prefetch=1,
        grid=(exp_dev,),
        in_specs=[
            pl.BlockSpec(memory_space=pltpu.SMEM),
            pl.BlockSpec(memory_space=pltpu.SMEM),
            pl.BlockSpec((1, tile_len), lambda e, idx: (0, 0)),
            pl.BlockSpec((tile_len, 1), lambda e, idx: (0, 0)),
            pl.BlockSpec((1, tile_len, tile_len), lambda e, idx: (e, 0, 0)),
            pl.BlockSpec((1, tile_len, tile_len), lambda e, idx: (idx[e, 0], 0, 0)),
            pl.BlockSpec((1, tile_len, tile_len), lambda e, idx: (idx[e, 1], 0, 0)),
        ],
        out_specs=pl.BlockSpec((patches, tile_len, tile_len), lambda e, idx: (0, 0, 0)),
        scratch_shapes=[pltpu.VMEM((patches, tile_len, tile_len), jnp.float32)],
    )
    flops = exp_dev * 4 * tile_len ** 3
    moved = exp_dev * tile_len * tile_len * (4 + 2 + 2) + patches * tile_len * tile_len * 2
    vmem = 60 * 1024 * 1024
    return pl.pallas_call(
        warp_body,
        grid_spec=grid_spec,
        out_shape=jax.ShapeDtypeStruct((patches, tile_len, tile_len), jnp.bfloat16),
        compiler_params=pltpu.CompilerParams(
            dimension_semantics=("arbitrary",), vmem_limit_bytes=vmem
        ),
        cost_estimate=pl.CostEstimate(flops=flops, bytes_accessed=moved, transcendentals=0),
    )(choose, plane, picked, xrow, ycol, matched, bank, bank)


def rows_from(source, anchor):
    return lax.dynamic_slice_in_dim(source, anchor, STRIP, 0)


def shards(images, coeffs, pair_list, weights, resample_bank, warp_index, destinations, counts):
    exp_dev = images.shape[0]
    tile_len = images.shape[1]
    row_count = lax.axis_size("row")
    col_count = lax.axis_size("col")
    visit_count = lax.axis_size("visit")
    row_pos = lax.axis_index("row")
    col_pos = lax.axis_index("col")
    visit_pos = lax.axis_index("visit")
    height = row_count * tile_len
    breadth = col_count * tile_len
    padded = extended(images, (("col", 2), ("row", 1)), HALO)
    own_ids = visit_pos * exp_dev + jnp.arange(exp_dev, dtype=jnp.int32)
    first_col = pair_list[:, 0]
    second_col = pair_list[:, 1]
    offsets = pair_list[:, 2]
    hit_first = first_col[None, :] == own_ids[:, None]
    hit_second = second_col[None, :] == own_ids[:, None]
    partner = jnp.sum(
        jnp.where(hit_first, second_col[None, :], 0) + jnp.where(hit_second, first_col[None, :], 0),
        axis=1,
    )
    offset = jnp.sum(jnp.where(hit_first | hit_second, offsets[None, :], 0), axis=1)
    pick_rows = (
        lax.broadcasted_iota(jnp.int32, (exp_dev, STRIP, tile_len), 2)
        == offset[:, None, None] + lax.broadcasted_iota(jnp.int32, (exp_dev, STRIP, tile_len), 1)
    ).astype(jnp.bfloat16)
    own_strip = jnp.einsum(
        "esr,erl->esl", pick_rows, images, preferred_element_type=jnp.float32
    ).astype(jnp.bfloat16)
    listed = destinations[:, 0, 0, :]
    how_many = counts[:, 0, 0]
    usable = jnp.arange(MAXD, dtype=jnp.int32)[None, :] < how_many[:, None]
    owners = jnp.arange(visit_count, dtype=jnp.int32)
    member = jnp.any(usable[:, :, None] & (listed[:, :, None] == owners[None, None, :]), axis=1)
    tile_weight = weights[:, 0, 0]
    nothing = jnp.zeros((), jnp.bfloat16)
    picked = jnp.where(member, tile_weight[:, None], nothing)
    strip_rows_n = exp_dev * STRIP
    extra = -(-(exp_dev * visit_count) // tile_len)
    extra = -(-extra // 16) * 16
    tail = jnp.zeros((extra * tile_len,), jnp.bfloat16)
    tail = tail.at[: exp_dev * visit_count].set(picked.reshape(-1)).reshape(extra, tile_len)
    payload = jnp.concatenate([own_strip.reshape(strip_rows_n, tile_len), tail], axis=0)
    received = [payload]
    for shift in range(1, visit_count):
        pairs = [(i, (i + shift) % visit_count) for i in range(visit_count)]
        received.append(lax.ppermute(payload, "visit", pairs))
    stacked = jnp.stack(received, 0)
    strips_all = stacked[:, :strip_rows_n].reshape(visit_count * exp_dev, STRIP, tile_len)
    picked_all = stacked[:, strip_rows_n:].reshape(visit_count, -1)[:, : exp_dev * visit_count]
    picked_all = picked_all.reshape(visit_count, exp_dev, visit_count)
    partner_visit = partner // exp_dev
    slot = (visit_pos - partner_visit) % visit_count
    source = slot * exp_dev + partner % exp_dev
    choose_strip = (
        lax.broadcasted_iota(jnp.int32, (exp_dev, visit_count * exp_dev), 1) == source[:, None]
    ).astype(jnp.bfloat16)
    theirs = jnp.einsum(
        "ej,jsl->esl", choose_strip, strips_all, preferred_element_type=jnp.float32
    )
    own_patch = jnp.take(picked_all, visit_pos, axis=2).astype(jnp.float32)
    denominator = jnp.sum(own_patch).reshape(1)
    stacked_tables = jnp.stack([band_table(tile_len, HALO, HALO * part) for part in SIGMA_PARTS])
    strip_tables = jnp.einsum(
        "esr,krj->eksj", pick_rows, stacked_tables, preferred_element_type=jnp.float32
    ).astype(jnp.bfloat16)
    nearby = conv_tiles(coeffs, strip_tables, stacked_tables, padded, True)
    spare = 2 * BLOCK + tile_len - BLOCK - padded.shape[1]
    roomy = jnp.pad(padded, ((0, 0), (0, spare), (0, spare)))
    blocks = stacked_tables[:, :BLOCK, : 2 * BLOCK]
    half = exp_dev // 2
    matched = band_tiles(coeffs, blocks, roomy, tile_len, 0, half, None)
    matched = band_tiles(coeffs, blocks, roomy, tile_len, half, exp_dev - half, matched)
    difference = nearby - theirs
    pixel_weight = 1.0 / (1.0 + theirs * theirs)
    strip_rows = row_pos * tile_len + offset[:, None] + jnp.arange(STRIP, dtype=jnp.int32)[None, :]
    ycoord = centred(strip_rows, height)[:, :, None]
    xcoord = centred(col_pos * tile_len + jnp.arange(tile_len, dtype=jnp.int32), breadth)
    xgrid = xcoord[None, None, :]
    weight_x = pixel_weight * xgrid
    weight_y = pixel_weight * ycoord
    sum_w = jnp.sum(pixel_weight, axis=(1, 2))
    sum_x = jnp.sum(weight_x, axis=(1, 2))
    sum_y = jnp.sum(weight_y, axis=(1, 2))
    sum_xx = jnp.sum(weight_x * xgrid, axis=(1, 2))
    sum_xy = jnp.sum(weight_x * ycoord, axis=(1, 2))
    sum_yy = jnp.sum(weight_y * ycoord, axis=(1, 2))
    normal = jnp.stack(
        [
            jnp.stack([sum_w, sum_x, sum_y], -1),
            jnp.stack([sum_x, sum_xx, sum_xy], -1),
            jnp.stack([sum_y, sum_xy, sum_yy], -1),
        ],
        1,
    )
    moments = jnp.stack(
        [
            jnp.sum(pixel_weight * difference, axis=(1, 2)),
            jnp.sum(weight_x * difference, axis=(1, 2)),
            jnp.sum(weight_y * difference, axis=(1, 2)),
        ],
        -1,
    )
    packed = jnp.concatenate([normal.reshape(exp_dev, 9), moments], axis=1)
    packed = butterfly_sum(packed, (("row", row_count), ("col", col_count)))
    normal = packed[:, :9].reshape(exp_dev, 3, 3)
    moments = packed[:, 9:]
    plane_fit = solve_three(normal, moments)
    row_coord = centred(row_pos * tile_len + jnp.arange(tile_len, dtype=jnp.int32), height)
    choose = warp_index[:, 0, 0, :]
    partial_sum = warp_tiles(
        choose, plane_fit, picked.astype(jnp.float32), xcoord.reshape(1, tile_len),
        row_coord.reshape(tile_len, 1), matched, resample_bank,
    )
    numerator = lax.psum_scatter(
        partial_sum, "visit", scatter_dimension=0, tiled=True
    ).astype(jnp.float32)
    coadd_patch = numerator / denominator[:, None, None]
    return (coadd_patch, plane_fit)


def solution(mesh):
    in_specs = (
        P("visit", "row", "col"),
        P("visit", None),
        P(),
        P("visit", "row", "col"),
        P(),
        P("visit", "row", "col", None),
        P("visit", "row", "col", None),
        P("visit", "row", "col"),
    )
    out_specs = (P("visit", "row", "col"), P("visit", None))
    return jax.shard_map(shards, mesh=mesh, in_specs=in_specs, out_specs=out_specs, check_vma=False)
```

```python
import functools

import jax
import jax.numpy as jnp
import ml_dtypes
import numpy as np
from jax import lax
from jax.sharding import PartitionSpec as P
from jax.experimental import pallas as pl
from jax.experimental.pallas import tpu as pltpu

HALO = 16
STRIP = 32
MAXD = 4


SIGMA_PARTS = (0.0625, 0.125, 0.25)


def extended(value, sides, width):
    for axis, dim in sides:
        devices, length = (lax.axis_size(axis), value.shape[dim])
        last = lax.slice_in_dim(value, length - width, length, axis=dim)
        initial = lax.slice_in_dim(value, 0, width, axis=dim)
        minor = dim == value.ndim - 1
        if minor:
            flat = value.shape[:-2] + (-1,)
            turned = jnp.swapaxes(last, -1, -2).shape
            last = jnp.swapaxes(last, -1, -2).reshape(flat)
            initial = jnp.swapaxes(initial, -1, -2).reshape(flat)
        if devices == 2:
            position = lax.axis_index(axis)
            facing = jnp.where(position == 0, last, initial)
            arrived = lax.ppermute(facing, axis, [(0, 1), (1, 0)])
            empty = jnp.zeros_like(arrived)
            before = jnp.where(position == 1, arrived, empty)
            after = jnp.where(position == 0, arrived, empty)
        else:
            up = [(i, (i + 1) % devices) for i in range(devices - 1)]
            down = [(j, i) for i, j in up]
            before = lax.ppermute(last, axis, up)
            after = lax.ppermute(initial, axis, down)
        if minor:
            before = jnp.swapaxes(before.reshape(turned), -1, -2)
            after = jnp.swapaxes(after.reshape(turned), -1, -2)
        value = jnp.concatenate([before, value, after], axis=dim)
    return value


def toeplitz_block(size, width, sigma):
    spread = (np.arange(2 * width + 1) - width).astype(np.float32)
    scale = np.float32(2.0) * np.float32(sigma) * np.float32(sigma)
    total = np.float32(np.exp(-spread * spread / scale).astype(np.float32).sum(dtype=np.float32))
    offset = (np.arange(size)[None, :] - np.arange(size)[:, None] - width).astype(np.float32)
    values = (np.exp(-offset * offset / scale).astype(np.float32) / total).astype(np.float32)
    values = np.where(np.abs(offset) <= width, values, np.float32(0.0))
    return values.astype(ml_dtypes.bfloat16)


def band_table(length, width, sigma):
    spread = (jnp.arange(2 * width + 1) - width).astype(jnp.float32)
    curve = jnp.exp(-spread * spread / (2.0 * sigma * sigma))
    total = jnp.sum(curve)
    rows_grid = lax.broadcasted_iota(jnp.int32, (length, length + 2 * width), 0)
    cols_grid = lax.broadcasted_iota(jnp.int32, (length, length + 2 * width), 1)
    offset = (cols_grid - rows_grid - width).astype(jnp.float32)
    values = jnp.exp(-offset * offset / (2.0 * sigma * sigma)) / total
    return jnp.where(jnp.abs(offset) <= width, values, 0.0).astype(jnp.bfloat16)


def centred(index, length):
    return (index.astype(jnp.float32) + 0.5) / length * 2.0 - 1.0


def solve_three(normal, moments):
    lower = jnp.linalg.cholesky(normal)
    first = moments[..., 0] / lower[..., 0, 0]
    second = (moments[..., 1] - lower[..., 1, 0] * first) / lower[..., 1, 1]
    third = (moments[..., 2] - lower[..., 2, 0] * first - lower[..., 2, 1] * second) / lower[
        ..., 2, 2
    ]
    upper_top = third / lower[..., 2, 2]
    upper_mid = (second - lower[..., 2, 1] * upper_top) / lower[..., 1, 1]
    upper_low = (first - lower[..., 1, 0] * upper_mid - lower[..., 2, 0] * upper_top) / lower[
        ..., 0, 0
    ]
    return jnp.stack([upper_low, upper_mid, upper_top], -1)


def butterfly_sum(values, axes):
    for axis, size in axes:
        if size & (size - 1) == 0:
            bit = 1
            while bit < size:
                pairs = [(i, i ^ bit) for i in range(size)]
                values = jax.tree.map(lambda v: v + lax.ppermute(v, axis, pairs), values)
                bit *= 2
        else:
            position = lax.axis_index(axis)
            def gathered(v):
                parts = [v]
                for shift in range(1, size):
                    pairs = [(i, (i + shift) % size) for i in range(size)]
                    parts.append(lax.ppermute(v, axis, pairs))
                stacked = jnp.stack(parts, 0)
                order = (position - jnp.arange(size)) % size
                canonical = jnp.zeros_like(stacked).at[order].set(stacked)
                return jnp.sum(canonical, axis=0)
            values = jax.tree.map(gathered, values)
    return values


def conv_body(coef_ref, vt_ref, ht_ref, padded_ref, out_ref):
    e = pl.program_id(0)
    image = padded_ref[0]
    total = None
    for kernel in range(len(SIGMA_PARTS)):
        across = jnp.dot(vt_ref[0, kernel], image, preferred_element_type=jnp.float32)
        smoothed = lax.dot_general(
            across.astype(jnp.bfloat16), ht_ref[kernel], (((1,), (1,)), ((), ())),
            preferred_element_type=jnp.float32,
        )
        term = coef_ref[e, kernel] * smoothed
        total = term if total is None else total + term
    out_ref[0] = total


def conv_tiles(coeffs, vtables, htables, padded, per_exposure):
    exp_dev, wide = padded.shape[0], padded.shape[1]
    nk, out_rows = vtables.shape[-3], vtables.shape[-2]
    tile_len = htables.shape[1]
    if per_exposure:
        vspec = pl.BlockSpec((1, nk, out_rows, wide), lambda e: (e, 0, 0, 0))
    else:
        vtables = vtables[None]
        vspec = pl.BlockSpec((1, nk, out_rows, wide), lambda e: (0, 0, 0, 0))
    flops = exp_dev * nk * 2 * out_rows * wide * (wide + tile_len)
    moved = exp_dev * wide * wide * 2 + exp_dev * out_rows * tile_len * 4
    return pl.pallas_call(
        conv_body,
        grid=(exp_dev,),
        in_specs=[
            pl.BlockSpec(memory_space=pltpu.SMEM),
            vspec,
            pl.BlockSpec((nk, tile_len, wide), lambda e: (0, 0, 0)),
            pl.BlockSpec((1, wide, wide), lambda e: (e, 0, 0)),
        ],
        out_specs=pl.BlockSpec((1, out_rows, tile_len), lambda e: (e, 0, 0)),
        out_shape=jax.ShapeDtypeStruct((exp_dev, out_rows, tile_len), jnp.float32),
        compiler_params=pltpu.CompilerParams(
            dimension_semantics=("arbitrary",), vmem_limit_bytes=48 * 1024 * 1024
        ),
        cost_estimate=pl.CostEstimate(flops=flops, bytes_accessed=moved, transcendentals=0),
    )(coeffs, vtables, htables, padded)


BLOCK = 128


def strip_body(off_ref, coef_ref, tb_ref, padded_ref, out_ref):
    e = pl.program_id(0)
    rows, tile_len = out_ref.shape[1], out_ref.shape[2]
    anchor = off_ref[e]
    base = (anchor // BLOCK) * BLOCK
    shift = anchor - base
    window = padded_ref[0, pl.ds(pl.multiple_of(base, BLOCK), 2 * BLOCK), :]
    pick = (
        lax.broadcasted_iota(jnp.int32, (rows, 2 * BLOCK), 1)
        == lax.broadcasted_iota(jnp.int32, (rows, 2 * BLOCK), 0) + shift
    ).astype(jnp.bfloat16)
    total = None
    for kernel in range(len(SIGMA_PARTS)):
        table = tb_ref[kernel]
        strip_rows = jnp.dot(pick, table, preferred_element_type=jnp.float32).astype(jnp.bfloat16)
        across = jnp.dot(strip_rows, window, preferred_element_type=jnp.float32)
        across = across.astype(jnp.bfloat16)
        block = table[:BLOCK]
        cols = [
            lax.dot_general(
                across[:, start:start + 2 * BLOCK], block, (((1,), (1,)), ((), ())),
                preferred_element_type=jnp.float32,
            )
            for start in range(0, tile_len, BLOCK)
        ]
        term = coef_ref[e, kernel] * jnp.concatenate(cols, 1)
        total = term if total is None else total + term
    out_ref[0] = total


def strip_tiles(offset, coeffs, tb, padded, tile_len):
    exp_dev, wide = padded.shape[0], padded.shape[1]
    nk = tb.shape[0]
    grid_spec = pltpu.PrefetchScalarGridSpec(
        num_scalar_prefetch=1,
        grid=(exp_dev,),
        in_specs=[
            pl.BlockSpec(memory_space=pltpu.SMEM),
            pl.BlockSpec((nk, 2 * BLOCK, 2 * BLOCK), lambda e, off: (0, 0, 0)),
            pl.BlockSpec((1, wide, wide), lambda e, off: (e, 0, 0)),
        ],
        out_specs=pl.BlockSpec((1, STRIP, tile_len), lambda e, off: (e, 0, 0)),
    )
    flops = exp_dev * nk * 2 * STRIP * 2 * BLOCK * (2 * BLOCK + wide + tile_len)
    moved = exp_dev * wide * wide * 2 + exp_dev * STRIP * tile_len * 4
    return pl.pallas_call(
        strip_body,
        grid_spec=grid_spec,
        out_shape=jax.ShapeDtypeStruct((exp_dev, STRIP, tile_len), jnp.float32),
        compiler_params=pltpu.CompilerParams(
            dimension_semantics=("arbitrary",), vmem_limit_bytes=48 * 1024 * 1024
        ),
        cost_estimate=pl.CostEstimate(flops=flops, bytes_accessed=moved, transcendentals=0),
    )(offset, coeffs, tb, padded)


def band_body(first, coef_ref, blk_ref, padded_ref, *rest):
    out_ref = rest[-1]
    e = pl.program_id(0) + first
    tile_len = out_ref.shape[1]
    total = None
    for kernel in range(len(SIGMA_PARTS)):
        block = blk_ref[kernel][:BLOCK]
        rows = [
            jnp.dot(block, padded_ref[0, start:start + 2 * BLOCK, :], preferred_element_type=jnp.float32)
            for start in range(0, tile_len, BLOCK)
        ]
        across = jnp.concatenate(rows, 0).astype(jnp.bfloat16)
        cols = [
            lax.dot_general(
                across[:, start:start + 2 * BLOCK], block, (((1,), (1,)), ((), ())),
                preferred_element_type=jnp.float32,
            )
            for start in range(0, tile_len, BLOCK)
        ]
        term = coef_ref[e, kernel] * jnp.concatenate(cols, 1)
        total = term if total is None else total + term
    out_ref[0] = total


def band_tiles(coeffs, blocks, padded, tile_len, first, count, into):
    exp_dev, wide = padded.shape[0], padded.shape[1]
    nk = blocks.shape[0]
    steps = tile_len // BLOCK
    flops = count * nk * steps * 2 * BLOCK * 2 * BLOCK * (wide + tile_len)
    moved = count * wide * wide * 2 + count * tile_len * tile_len * 4
    in_specs = [
        pl.BlockSpec(memory_space=pltpu.SMEM),
        pl.BlockSpec((nk, 2 * BLOCK, 2 * BLOCK), lambda e: (0, 0, 0)),
        pl.BlockSpec((1, wide, wide), lambda e: (e + first, 0, 0)),
    ]
    operands = [coeffs, blocks, padded]
    aliases = {}
    if into is not None:
        in_specs.append(pl.BlockSpec(memory_space=pl.ANY))
        operands.append(into)
        aliases = {3: 0}
    return pl.pallas_call(
        functools.partial(band_body, first),
        grid=(count,),
        in_specs=in_specs,
        out_specs=pl.BlockSpec((1, tile_len, tile_len), lambda e: (e + first, 0, 0)),
        out_shape=jax.ShapeDtypeStruct((exp_dev, tile_len, tile_len), jnp.float32),
        input_output_aliases=aliases,
        compiler_params=pltpu.CompilerParams(
            dimension_semantics=("arbitrary",), vmem_limit_bytes=48 * 1024 * 1024
        ),
        cost_estimate=pl.CostEstimate(flops=flops, bytes_accessed=moved, transcendentals=0),
    )(*operands)


def warp_body(idx_ref, plane_ref, pick_ref, xrow_ref, ycol_ref, matched_ref, rmap_ref, cmap_ref,
              out_ref, acc_ref):
    e = pl.program_id(0)
    background = (
        plane_ref[e, 0] + plane_ref[e, 1] * xrow_ref[...]
    ) + plane_ref[e, 2] * ycol_ref[...]
    corrected = (matched_ref[0] - background).astype(jnp.bfloat16)
    halfway = jnp.dot(rmap_ref[0], corrected, preferred_element_type=jnp.float32)
    warped = lax.dot_general(
        halfway.astype(jnp.bfloat16), cmap_ref[0], (((1,), (1,)), ((), ())),
        preferred_element_type=jnp.float32,
    )
    warped = warped.astype(jnp.bfloat16).astype(jnp.float32)
    patches = acc_ref.shape[0]

    @pl.when(e == 0)
    def _():
        for v in range(patches):
            acc_ref[v] = pick_ref[e, v] * warped

    @pl.when(e > 0)
    def _():
        for v in range(patches):
            acc_ref[v] = acc_ref[v] + pick_ref[e, v] * warped

    @pl.when(e == pl.num_programs(0) - 1)
    def _():
        out_ref[...] = acc_ref[...].astype(jnp.bfloat16)


def warp_tiles(choose, plane, picked, xrow, ycol, matched, bank):
    exp_dev, tile_len = matched.shape[0], matched.shape[1]
    patches = picked.shape[1]
    grid_spec = pltpu.PrefetchScalarGridSpec(
        num_scalar_prefetch=1,
        grid=(exp_dev,),
        in_specs=[
            pl.BlockSpec(memory_space=pltpu.SMEM),
            pl.BlockSpec(memory_space=pltpu.SMEM),
            pl.BlockSpec((1, tile_len), lambda e, idx: (0, 0)),
            pl.BlockSpec((tile_len, 1), lambda e, idx: (0, 0)),
            pl.BlockSpec((1, tile_len, tile_len), lambda e, idx: (e, 0, 0)),
            pl.BlockSpec((1, tile_len, tile_len), lambda e, idx: (idx[e, 0], 0, 0)),
            pl.BlockSpec((1, tile_len, tile_len), lambda e, idx: (idx[e, 1], 0, 0)),
        ],
        out_specs=pl.BlockSpec((patches, tile_len, tile_len), lambda e, idx: (0, 0, 0)),
        scratch_shapes=[pltpu.VMEM((patches, tile_len, tile_len), jnp.float32)],
    )
    flops = exp_dev * 4 * tile_len ** 3
    moved = exp_dev * tile_len * tile_len * (4 + 2 + 2) + patches * tile_len * tile_len * 2
    vmem = 60 * 1024 * 1024
    return pl.pallas_call(
        warp_body,
        grid_spec=grid_spec,
        out_shape=jax.ShapeDtypeStruct((patches, tile_len, tile_len), jnp.bfloat16),
        compiler_params=pltpu.CompilerParams(
            dimension_semantics=("arbitrary",), vmem_limit_bytes=vmem
        ),
        cost_estimate=pl.CostEstimate(flops=flops, bytes_accessed=moved, transcendentals=0),
    )(choose, plane, picked, xrow, ycol, matched, bank, bank)


def rows_from(source, anchor):
    return lax.dynamic_slice_in_dim(source, anchor, STRIP, 0)


def shards(images, coeffs, pair_list, weights, resample_bank, warp_index, destinations, counts):
    exp_dev = images.shape[0]
    tile_len = images.shape[1]
    row_count = lax.axis_size("row")
    col_count = lax.axis_size("col")
    visit_count = lax.axis_size("visit")
    row_pos = lax.axis_index("row")
    col_pos = lax.axis_index("col")
    visit_pos = lax.axis_index("visit")
    height = row_count * tile_len
    breadth = col_count * tile_len
    padded = extended(images, (("col", 2), ("row", 1)), HALO)
    own_ids = visit_pos * exp_dev + jnp.arange(exp_dev, dtype=jnp.int32)
    first_col = pair_list[:, 0]
    second_col = pair_list[:, 1]
    offsets = pair_list[:, 2]
    hit_first = first_col[None, :] == own_ids[:, None]
    hit_second = second_col[None, :] == own_ids[:, None]
    partner = jnp.sum(
        jnp.where(hit_first, second_col[None, :], 0) + jnp.where(hit_second, first_col[None, :], 0),
        axis=1,
    )
    offset = jnp.sum(jnp.where(hit_first | hit_second, offsets[None, :], 0), axis=1)
    pick_rows = (
        lax.broadcasted_iota(jnp.int32, (exp_dev, STRIP, tile_len), 2)
        == offset[:, None, None] + lax.broadcasted_iota(jnp.int32, (exp_dev, STRIP, tile_len), 1)
    ).astype(jnp.bfloat16)
    own_strip = jnp.einsum(
        "esr,erl->esl", pick_rows, images, preferred_element_type=jnp.float32
    ).astype(jnp.bfloat16)
    listed = destinations[:, 0, 0, :]
    how_many = counts[:, 0, 0]
    usable = jnp.arange(MAXD, dtype=jnp.int32)[None, :] < how_many[:, None]
    owners = jnp.arange(visit_count, dtype=jnp.int32)
    member = jnp.any(usable[:, :, None] & (listed[:, :, None] == owners[None, None, :]), axis=1)
    tile_weight = weights[:, 0, 0]
    nothing = jnp.zeros((), jnp.bfloat16)
    picked = jnp.where(member, tile_weight[:, None], nothing)
    strip_rows_n = exp_dev * STRIP
    extra = -(-(exp_dev * visit_count) // tile_len)
    extra = -(-extra // 16) * 16
    tail = jnp.zeros((extra * tile_len,), jnp.bfloat16)
    tail = tail.at[: exp_dev * visit_count].set(picked.reshape(-1)).reshape(extra, tile_len)
    payload = jnp.concatenate([own_strip.reshape(strip_rows_n, tile_len), tail], axis=0)
    received = [payload]
    for shift in range(1, visit_count):
        pairs = [(i, (i + shift) % visit_count) for i in range(visit_count)]
        received.append(lax.ppermute(payload, "visit", pairs))
    stacked = jnp.stack(received, 0)
    strips_all = stacked[:, :strip_rows_n].reshape(visit_count * exp_dev, STRIP, tile_len)
    picked_all = stacked[:, strip_rows_n:].reshape(visit_count, -1)[:, : exp_dev * visit_count]
    picked_all = picked_all.reshape(visit_count, exp_dev, visit_count)
    partner_visit = partner // exp_dev
    slot = (visit_pos - partner_visit) % visit_count
    source = slot * exp_dev + partner % exp_dev
    choose_strip = (
        lax.broadcasted_iota(jnp.int32, (exp_dev, visit_count * exp_dev), 1) == source[:, None]
    ).astype(jnp.bfloat16)
    theirs = jnp.einsum(
        "ej,jsl->esl", choose_strip, strips_all, preferred_element_type=jnp.float32
    )
    own_patch = jnp.take(picked_all, visit_pos, axis=2).astype(jnp.float32)
    denominator = jnp.sum(own_patch).reshape(1)
    spare = 2 * BLOCK + tile_len - BLOCK - padded.shape[1]
    roomy = jnp.pad(padded, ((0, 0), (0, spare), (0, spare)))
    blocks = jnp.asarray(
        np.stack([toeplitz_block(2 * BLOCK, HALO, HALO * part) for part in SIGMA_PARTS])
    )
    nearby = strip_tiles(offset, coeffs, blocks, roomy, tile_len)
    half = exp_dev // 2
    matched = band_tiles(coeffs, blocks, roomy, tile_len, 0, half, None)
    matched = band_tiles(coeffs, blocks, roomy, tile_len, half, exp_dev - half, matched)
    difference = nearby - theirs
    pixel_weight = 1.0 / (1.0 + theirs * theirs)
    strip_rows = row_pos * tile_len + offset[:, None] + jnp.arange(STRIP, dtype=jnp.int32)[None, :]
    ycoord = centred(strip_rows, height)[:, :, None]
    xcoord = centred(col_pos * tile_len + jnp.arange(tile_len, dtype=jnp.int32), breadth)
    xgrid = xcoord[None, None, :]
    weight_x = pixel_weight * xgrid
    weight_y = pixel_weight * ycoord
    sum_w = jnp.sum(pixel_weight, axis=(1, 2))
    sum_x = jnp.sum(weight_x, axis=(1, 2))
    sum_y = jnp.sum(weight_y, axis=(1, 2))
    sum_xx = jnp.sum(weight_x * xgrid, axis=(1, 2))
    sum_xy = jnp.sum(weight_x * ycoord, axis=(1, 2))
    sum_yy = jnp.sum(weight_y * ycoord, axis=(1, 2))
    normal = jnp.stack(
        [
            jnp.stack([sum_w, sum_x, sum_y], -1),
            jnp.stack([sum_x, sum_xx, sum_xy], -1),
            jnp.stack([sum_y, sum_xy, sum_yy], -1),
        ],
        1,
    )
    moments = jnp.stack(
        [
            jnp.sum(pixel_weight * difference, axis=(1, 2)),
            jnp.sum(weight_x * difference, axis=(1, 2)),
            jnp.sum(weight_y * difference, axis=(1, 2)),
        ],
        -1,
    )
    packed = jnp.concatenate([normal.reshape(exp_dev, 9), moments], axis=1)
    packed = butterfly_sum(packed, (("row", row_count), ("col", col_count)))
    normal = packed[:, :9].reshape(exp_dev, 3, 3)
    moments = packed[:, 9:]
    plane_fit = solve_three(normal, moments)
    row_coord = centred(row_pos * tile_len + jnp.arange(tile_len, dtype=jnp.int32), height)
    choose = warp_index[:, 0, 0, :]
    partial_sum = warp_tiles(
        choose, plane_fit, picked.astype(jnp.float32), xcoord.reshape(1, tile_len),
        row_coord.reshape(tile_len, 1), matched, resample_bank,
    )
    numerator = lax.psum_scatter(
        partial_sum, "visit", scatter_dimension=0, tiled=True
    ).astype(jnp.float32)
    coadd_patch = numerator / denominator[:, None, None]
    return (coadd_patch, plane_fit)


def solution(mesh):
    in_specs = (
        P("visit", "row", "col"),
        P("visit", None),
        P(),
        P("visit", "row", "col"),
        P(),
        P("visit", "row", "col", None),
        P("visit", "row", "col", None),
        P("visit", "row", "col"),
    )
    out_specs = (P("visit", "row", "col"), P("visit", None))
    return jax.shard_map(shards, mesh=mesh, in_specs=in_specs, out_specs=out_specs, check_vma=False)
```

```python
import functools

import jax
import jax.numpy as jnp
import ml_dtypes
import numpy as np
from jax import lax
from jax.sharding import PartitionSpec as P
from jax.experimental import pallas as pl
from jax.experimental.pallas import tpu as pltpu

HALO = 16
STRIP = 32
MAXD = 4


SIGMA_PARTS = (0.0625, 0.125, 0.25)


def extended(value, sides, width):
    for axis, dim in sides:
        devices, length = (lax.axis_size(axis), value.shape[dim])
        last = lax.slice_in_dim(value, length - width, length, axis=dim)
        initial = lax.slice_in_dim(value, 0, width, axis=dim)
        minor = dim == value.ndim - 1
        if minor:
            flat = value.shape[:-2] + (-1,)
            turned = jnp.swapaxes(last, -1, -2).shape
            last = jnp.swapaxes(last, -1, -2).reshape(flat)
            initial = jnp.swapaxes(initial, -1, -2).reshape(flat)
        if devices == 2:
            position = lax.axis_index(axis)
            facing = jnp.where(position == 0, last, initial)
            arrived = lax.ppermute(facing, axis, [(0, 1), (1, 0)])
            empty = jnp.zeros_like(arrived)
            before = jnp.where(position == 1, arrived, empty)
            after = jnp.where(position == 0, arrived, empty)
        else:
            up = [(i, (i + 1) % devices) for i in range(devices - 1)]
            down = [(j, i) for i, j in up]
            before = lax.ppermute(last, axis, up)
            after = lax.ppermute(initial, axis, down)
        if minor:
            before = jnp.swapaxes(before.reshape(turned), -1, -2)
            after = jnp.swapaxes(after.reshape(turned), -1, -2)
        value = jnp.concatenate([before, value, after], axis=dim)
    return value


def toeplitz_block(size, width, sigma):
    spread = (np.arange(2 * width + 1) - width).astype(np.float32)
    scale = np.float32(2.0) * np.float32(sigma) * np.float32(sigma)
    total = np.float32(np.exp(-spread * spread / scale).astype(np.float32).sum(dtype=np.float32))
    offset = (np.arange(size)[None, :] - np.arange(size)[:, None] - width).astype(np.float32)
    values = (np.exp(-offset * offset / scale).astype(np.float32) / total).astype(np.float32)
    values = np.where(np.abs(offset) <= width, values, np.float32(0.0))
    return values.astype(ml_dtypes.bfloat16)


def band_table(length, width, sigma):
    spread = (jnp.arange(2 * width + 1) - width).astype(jnp.float32)
    curve = jnp.exp(-spread * spread / (2.0 * sigma * sigma))
    total = jnp.sum(curve)
    rows_grid = lax.broadcasted_iota(jnp.int32, (length, length + 2 * width), 0)
    cols_grid = lax.broadcasted_iota(jnp.int32, (length, length + 2 * width), 1)
    offset = (cols_grid - rows_grid - width).astype(jnp.float32)
    values = jnp.exp(-offset * offset / (2.0 * sigma * sigma)) / total
    return jnp.where(jnp.abs(offset) <= width, values, 0.0).astype(jnp.bfloat16)


def centred(index, length):
    return (index.astype(jnp.float32) + 0.5) / length * 2.0 - 1.0


def solve_three(normal, moments):
    lower = jnp.linalg.cholesky(normal)
    first = moments[..., 0] / lower[..., 0, 0]
    second = (moments[..., 1] - lower[..., 1, 0] * first) / lower[..., 1, 1]
    third = (moments[..., 2] - lower[..., 2, 0] * first - lower[..., 2, 1] * second) / lower[
        ..., 2, 2
    ]
    upper_top = third / lower[..., 2, 2]
    upper_mid = (second - lower[..., 2, 1] * upper_top) / lower[..., 1, 1]
    upper_low = (first - lower[..., 1, 0] * upper_mid - lower[..., 2, 0] * upper_top) / lower[
        ..., 0, 0
    ]
    return jnp.stack([upper_low, upper_mid, upper_top], -1)


def butterfly_sum(values, axes):
    for axis, size in axes:
        if size & (size - 1) == 0:
            bit = 1
            while bit < size:
                pairs = [(i, i ^ bit) for i in range(size)]
                values = jax.tree.map(lambda v: v + lax.ppermute(v, axis, pairs), values)
                bit *= 2
        else:
            position = lax.axis_index(axis)
            def gathered(v):
                parts = [v]
                for shift in range(1, size):
                    pairs = [(i, (i + shift) % size) for i in range(size)]
                    parts.append(lax.ppermute(v, axis, pairs))
                stacked = jnp.stack(parts, 0)
                order = (position - jnp.arange(size)) % size
                canonical = jnp.zeros_like(stacked).at[order].set(stacked)
                return jnp.sum(canonical, axis=0)
            values = jax.tree.map(gathered, values)
    return values


def conv_body(coef_ref, vt_ref, ht_ref, padded_ref, out_ref):
    e = pl.program_id(0)
    image = padded_ref[0]
    total = None
    for kernel in range(len(SIGMA_PARTS)):
        across = jnp.dot(vt_ref[0, kernel], image, preferred_element_type=jnp.float32)
        smoothed = lax.dot_general(
            across.astype(jnp.bfloat16), ht_ref[kernel], (((1,), (1,)), ((), ())),
            preferred_element_type=jnp.float32,
        )
        term = coef_ref[e, kernel] * smoothed
        total = term if total is None else total + term
    out_ref[0] = total


def conv_tiles(coeffs, vtables, htables, padded, per_exposure):
    exp_dev, wide = padded.shape[0], padded.shape[1]
    nk, out_rows = vtables.shape[-3], vtables.shape[-2]
    tile_len = htables.shape[1]
    if per_exposure:
        vspec = pl.BlockSpec((1, nk, out_rows, wide), lambda e: (e, 0, 0, 0))
    else:
        vtables = vtables[None]
        vspec = pl.BlockSpec((1, nk, out_rows, wide), lambda e: (0, 0, 0, 0))
    flops = exp_dev * nk * 2 * out_rows * wide * (wide + tile_len)
    moved = exp_dev * wide * wide * 2 + exp_dev * out_rows * tile_len * 4
    return pl.pallas_call(
        conv_body,
        grid=(exp_dev,),
        in_specs=[
            pl.BlockSpec(memory_space=pltpu.SMEM),
            vspec,
            pl.BlockSpec((nk, tile_len, wide), lambda e: (0, 0, 0)),
            pl.BlockSpec((1, wide, wide), lambda e: (e, 0, 0)),
        ],
        out_specs=pl.BlockSpec((1, out_rows, tile_len), lambda e: (e, 0, 0)),
        out_shape=jax.ShapeDtypeStruct((exp_dev, out_rows, tile_len), jnp.float32),
        compiler_params=pltpu.CompilerParams(
            dimension_semantics=("arbitrary",), vmem_limit_bytes=48 * 1024 * 1024
        ),
        cost_estimate=pl.CostEstimate(flops=flops, bytes_accessed=moved, transcendentals=0),
    )(coeffs, vtables, htables, padded)


BLOCK = 128


def strip_body(off_ref, coef_ref, tb_ref, padded_ref, out_ref):
    e = pl.program_id(0)
    rows, tile_len = out_ref.shape[1], out_ref.shape[2]
    wide = padded_ref.shape[1]
    windows = [(start, min(2 * BLOCK, wide - start)) for start in range(0, tile_len, BLOCK)]
    anchor = off_ref[e]
    base = jnp.minimum((anchor // BLOCK) * BLOCK, wide - 2 * BLOCK)
    shift = anchor - base
    window = padded_ref[0, pl.ds(pl.multiple_of(base, 16), 2 * BLOCK), :]
    pick = (
        lax.broadcasted_iota(jnp.int32, (rows, 2 * BLOCK), 1)
        == lax.broadcasted_iota(jnp.int32, (rows, 2 * BLOCK), 0) + shift
    ).astype(jnp.bfloat16)
    total = None
    for kernel in range(len(SIGMA_PARTS)):
        table = tb_ref[kernel]
        strip_rows = jnp.dot(pick, table, preferred_element_type=jnp.float32).astype(jnp.bfloat16)
        across = jnp.dot(strip_rows, window, preferred_element_type=jnp.float32)
        across = across.astype(jnp.bfloat16)
        block = table[:BLOCK]
        cols = [
            lax.dot_general(
                across[:, start:start + reach], block[:, :reach], (((1,), (1,)), ((), ())),
                preferred_element_type=jnp.float32,
            )
            for start, reach in windows
        ]
        term = coef_ref[e, kernel] * jnp.concatenate(cols, 1)
        total = term if total is None else total + term
    out_ref[0] = total


def strip_tiles(offset, coeffs, tb, padded, tile_len):
    exp_dev, wide = padded.shape[0], padded.shape[1]
    nk = tb.shape[0]
    grid_spec = pltpu.PrefetchScalarGridSpec(
        num_scalar_prefetch=1,
        grid=(exp_dev,),
        in_specs=[
            pl.BlockSpec(memory_space=pltpu.SMEM),
            pl.BlockSpec((nk, 2 * BLOCK, 2 * BLOCK), lambda e, off: (0, 0, 0)),
            pl.BlockSpec((1, wide, wide), lambda e, off: (e, 0, 0)),
        ],
        out_specs=pl.BlockSpec((1, STRIP, tile_len), lambda e, off: (e, 0, 0)),
    )
    flops = exp_dev * nk * 2 * STRIP * 2 * BLOCK * (2 * BLOCK + wide + tile_len)
    moved = exp_dev * wide * wide * 2 + exp_dev * STRIP * tile_len * 4
    return pl.pallas_call(
        strip_body,
        grid_spec=grid_spec,
        out_shape=jax.ShapeDtypeStruct((exp_dev, STRIP, tile_len), jnp.float32),
        compiler_params=pltpu.CompilerParams(
            dimension_semantics=("arbitrary",), vmem_limit_bytes=48 * 1024 * 1024
        ),
        cost_estimate=pl.CostEstimate(flops=flops, bytes_accessed=moved, transcendentals=0),
    )(offset, coeffs, tb, padded)


def band_body(first, coef_ref, blk_ref, padded_ref, *rest):
    out_ref = rest[-1]
    e = pl.program_id(0) + first
    tile_len = out_ref.shape[1]
    wide = padded_ref.shape[1]
    windows = [(start, min(2 * BLOCK, wide - start)) for start in range(0, tile_len, BLOCK)]
    total = None
    for kernel in range(len(SIGMA_PARTS)):
        block = blk_ref[kernel][:BLOCK]
        rows = [
            jnp.dot(
                block[:, :reach], padded_ref[0, start:start + reach, :],
                preferred_element_type=jnp.float32,
            )
            for start, reach in windows
        ]
        across = jnp.concatenate(rows, 0).astype(jnp.bfloat16)
        cols = [
            lax.dot_general(
                across[:, start:start + reach], block[:, :reach], (((1,), (1,)), ((), ())),
                preferred_element_type=jnp.float32,
            )
            for start, reach in windows
        ]
        term = coef_ref[e, kernel] * jnp.concatenate(cols, 1)
        total = term if total is None else total + term
    out_ref[0] = total


def band_tiles(coeffs, blocks, padded, tile_len, first, count, into):
    exp_dev, wide = padded.shape[0], padded.shape[1]
    nk = blocks.shape[0]
    steps = tile_len // BLOCK
    flops = count * nk * steps * 2 * BLOCK * 2 * BLOCK * (wide + tile_len)
    moved = count * wide * wide * 2 + count * tile_len * tile_len * 4
    in_specs = [
        pl.BlockSpec(memory_space=pltpu.SMEM),
        pl.BlockSpec((nk, 2 * BLOCK, 2 * BLOCK), lambda e: (0, 0, 0)),
        pl.BlockSpec((1, wide, wide), lambda e: (e + first, 0, 0)),
    ]
    operands = [coeffs, blocks, padded]
    aliases = {}
    if into is not None:
        in_specs.append(pl.BlockSpec(memory_space=pl.ANY))
        operands.append(into)
        aliases = {3: 0}
    return pl.pallas_call(
        functools.partial(band_body, first),
        grid=(count,),
        in_specs=in_specs,
        out_specs=pl.BlockSpec((1, tile_len, tile_len), lambda e: (e + first, 0, 0)),
        out_shape=jax.ShapeDtypeStruct((exp_dev, tile_len, tile_len), jnp.float32),
        input_output_aliases=aliases,
        compiler_params=pltpu.CompilerParams(
            dimension_semantics=("arbitrary",), vmem_limit_bytes=48 * 1024 * 1024
        ),
        cost_estimate=pl.CostEstimate(flops=flops, bytes_accessed=moved, transcendentals=0),
    )(*operands)


def warp_body(idx_ref, plane_ref, pick_ref, xrow_ref, ycol_ref, matched_ref, rmap_ref, cmap_ref,
              out_ref, acc_ref):
    e = pl.program_id(0)
    background = (
        plane_ref[e, 0] + plane_ref[e, 1] * xrow_ref[...]
    ) + plane_ref[e, 2] * ycol_ref[...]
    corrected = (matched_ref[0] - background).astype(jnp.bfloat16)
    halfway = jnp.dot(rmap_ref[0], corrected, preferred_element_type=jnp.float32)
    warped = lax.dot_general(
        halfway.astype(jnp.bfloat16), cmap_ref[0], (((1,), (1,)), ((), ())),
        preferred_element_type=jnp.float32,
    )
    warped = warped.astype(jnp.bfloat16).astype(jnp.float32)
    patches = acc_ref.shape[0]

    @pl.when(e == 0)
    def _():
        for v in range(patches):
            acc_ref[v] = pick_ref[e, v] * warped

    @pl.when(e > 0)
    def _():
        for v in range(patches):
            acc_ref[v] = acc_ref[v] + pick_ref[e, v] * warped

    @pl.when(e == pl.num_programs(0) - 1)
    def _():
        out_ref[...] = acc_ref[...].astype(jnp.bfloat16)


def warp_tiles(choose, plane, picked, xrow, ycol, matched, bank):
    exp_dev, tile_len = matched.shape[0], matched.shape[1]
    patches = picked.shape[1]
    grid_spec = pltpu.PrefetchScalarGridSpec(
        num_scalar_prefetch=1,
        grid=(exp_dev,),
        in_specs=[
            pl.BlockSpec(memory_space=pltpu.SMEM),
            pl.BlockSpec(memory_space=pltpu.SMEM),
            pl.BlockSpec((1, tile_len), lambda e, idx: (0, 0)),
            pl.BlockSpec((tile_len, 1), lambda e, idx: (0, 0)),
            pl.BlockSpec((1, tile_len, tile_len), lambda e, idx: (e, 0, 0)),
            pl.BlockSpec((1, tile_len, tile_len), lambda e, idx: (idx[e, 0], 0, 0)),
            pl.BlockSpec((1, tile_len, tile_len), lambda e, idx: (idx[e, 1], 0, 0)),
        ],
        out_specs=pl.BlockSpec((patches, tile_len, tile_len), lambda e, idx: (0, 0, 0)),
        scratch_shapes=[pltpu.VMEM((patches, tile_len, tile_len), jnp.float32)],
    )
    flops = exp_dev * 4 * tile_len ** 3
    moved = exp_dev * tile_len * tile_len * (4 + 2 + 2) + patches * tile_len * tile_len * 2
    vmem = 60 * 1024 * 1024
    return pl.pallas_call(
        warp_body,
        grid_spec=grid_spec,
        out_shape=jax.ShapeDtypeStruct((patches, tile_len, tile_len), jnp.bfloat16),
        compiler_params=pltpu.CompilerParams(
            dimension_semantics=("arbitrary",), vmem_limit_bytes=vmem
        ),
        cost_estimate=pl.CostEstimate(flops=flops, bytes_accessed=moved, transcendentals=0),
    )(choose, plane, picked, xrow, ycol, matched, bank, bank)


def rows_from(source, anchor):
    return lax.dynamic_slice_in_dim(source, anchor, STRIP, 0)


def shards(images, coeffs, pair_list, weights, resample_bank, warp_index, destinations, counts):
    exp_dev = images.shape[0]
    tile_len = images.shape[1]
    row_count = lax.axis_size("row")
    col_count = lax.axis_size("col")
    visit_count = lax.axis_size("visit")
    row_pos = lax.axis_index("row")
    col_pos = lax.axis_index("col")
    visit_pos = lax.axis_index("visit")
    height = row_count * tile_len
    breadth = col_count * tile_len
    padded = extended(images, (("col", 2), ("row", 1)), HALO)
    own_ids = visit_pos * exp_dev + jnp.arange(exp_dev, dtype=jnp.int32)
    first_col = pair_list[:, 0]
    second_col = pair_list[:, 1]
    offsets = pair_list[:, 2]
    hit_first = first_col[None, :] == own_ids[:, None]
    hit_second = second_col[None, :] == own_ids[:, None]
    partner = jnp.sum(
        jnp.where(hit_first, second_col[None, :], 0) + jnp.where(hit_second, first_col[None, :], 0),
        axis=1,
    )
    offset = jnp.sum(jnp.where(hit_first | hit_second, offsets[None, :], 0), axis=1)
    pick_rows = (
        lax.broadcasted_iota(jnp.int32, (exp_dev, STRIP, tile_len), 2)
        == offset[:, None, None] + lax.broadcasted_iota(jnp.int32, (exp_dev, STRIP, tile_len), 1)
    ).astype(jnp.bfloat16)
    own_strip = jnp.einsum(
        "esr,erl->esl", pick_rows, images, preferred_element_type=jnp.float32
    ).astype(jnp.bfloat16)
    listed = destinations[:, 0, 0, :]
    how_many = counts[:, 0, 0]
    usable = jnp.arange(MAXD, dtype=jnp.int32)[None, :] < how_many[:, None]
    owners = jnp.arange(visit_count, dtype=jnp.int32)
    member = jnp.any(usable[:, :, None] & (listed[:, :, None] == owners[None, None, :]), axis=1)
    tile_weight = weights[:, 0, 0]
    nothing = jnp.zeros((), jnp.bfloat16)
    picked = jnp.where(member, tile_weight[:, None], nothing)
    strip_rows_n = exp_dev * STRIP
    extra = -(-(exp_dev * visit_count) // tile_len)
    extra = -(-extra // 16) * 16
    tail = jnp.zeros((extra * tile_len,), jnp.bfloat16)
    tail = tail.at[: exp_dev * visit_count].set(picked.reshape(-1)).reshape(extra, tile_len)
    payload = jnp.concatenate([own_strip.reshape(strip_rows_n, tile_len), tail], axis=0)
    received = [payload]
    for shift in range(1, visit_count):
        pairs = [(i, (i + shift) % visit_count) for i in range(visit_count)]
        received.append(lax.ppermute(payload, "visit", pairs))
    stacked = jnp.stack(received, 0)
    strips_all = stacked[:, :strip_rows_n].reshape(visit_count * exp_dev, STRIP, tile_len)
    picked_all = stacked[:, strip_rows_n:].reshape(visit_count, -1)[:, : exp_dev * visit_count]
    picked_all = picked_all.reshape(visit_count, exp_dev, visit_count)
    partner_visit = partner // exp_dev
    slot = (visit_pos - partner_visit) % visit_count
    source = slot * exp_dev + partner % exp_dev
    choose_strip = (
        lax.broadcasted_iota(jnp.int32, (exp_dev, visit_count * exp_dev), 1) == source[:, None]
    ).astype(jnp.bfloat16)
    theirs = jnp.einsum(
        "ej,jsl->esl", choose_strip, strips_all, preferred_element_type=jnp.float32
    )
    own_patch = jnp.take(picked_all, visit_pos, axis=2).astype(jnp.float32)
    denominator = jnp.sum(own_patch).reshape(1)
    roomy = padded
    blocks = jnp.asarray(
        np.stack([toeplitz_block(2 * BLOCK, HALO, HALO * part) for part in SIGMA_PARTS])
    )
    nearby = strip_tiles(offset, coeffs, blocks, roomy, tile_len)
    half = exp_dev // 2
    matched = band_tiles(coeffs, blocks, roomy, tile_len, 0, half, None)
    matched = band_tiles(coeffs, blocks, roomy, tile_len, half, exp_dev - half, matched)
    difference = nearby - theirs
    pixel_weight = 1.0 / (1.0 + theirs * theirs)
    strip_rows = row_pos * tile_len + offset[:, None] + jnp.arange(STRIP, dtype=jnp.int32)[None, :]
    ycoord = centred(strip_rows, height)[:, :, None]
    xcoord = centred(col_pos * tile_len + jnp.arange(tile_len, dtype=jnp.int32), breadth)
    xgrid = xcoord[None, None, :]
    weight_x = pixel_weight * xgrid
    weight_y = pixel_weight * ycoord
    sum_w = jnp.sum(pixel_weight, axis=(1, 2))
    sum_x = jnp.sum(weight_x, axis=(1, 2))
    sum_y = jnp.sum(weight_y, axis=(1, 2))
    sum_xx = jnp.sum(weight_x * xgrid, axis=(1, 2))
    sum_xy = jnp.sum(weight_x * ycoord, axis=(1, 2))
    sum_yy = jnp.sum(weight_y * ycoord, axis=(1, 2))
    normal = jnp.stack(
        [
            jnp.stack([sum_w, sum_x, sum_y], -1),
            jnp.stack([sum_x, sum_xx, sum_xy], -1),
            jnp.stack([sum_y, sum_xy, sum_yy], -1),
        ],
        1,
    )
    moments = jnp.stack(
        [
            jnp.sum(pixel_weight * difference, axis=(1, 2)),
            jnp.sum(weight_x * difference, axis=(1, 2)),
            jnp.sum(weight_y * difference, axis=(1, 2)),
        ],
        -1,
    )
    packed = jnp.concatenate([normal.reshape(exp_dev, 9), moments], axis=1)
    packed = butterfly_sum(packed, (("row", row_count), ("col", col_count)))
    normal = packed[:, :9].reshape(exp_dev, 3, 3)
    moments = packed[:, 9:]
    plane_fit = solve_three(normal, moments)
    row_coord = centred(row_pos * tile_len + jnp.arange(tile_len, dtype=jnp.int32), height)
    choose = warp_index[:, 0, 0, :]
    partial_sum = warp_tiles(
        choose, plane_fit, picked.astype(jnp.float32), xcoord.reshape(1, tile_len),
        row_coord.reshape(tile_len, 1), matched, resample_bank,
    )
    numerator = lax.psum_scatter(
        partial_sum, "visit", scatter_dimension=0, tiled=True
    ).astype(jnp.float32)
    coadd_patch = numerator / denominator[:, None, None]
    return (coadd_patch, plane_fit)


def solution(mesh):
    in_specs = (
        P("visit", "row", "col"),
        P("visit", None),
        P(),
        P("visit", "row", "col"),
        P(),
        P("visit", "row", "col", None),
        P("visit", "row", "col", None),
        P("visit", "row", "col"),
    )
    out_specs = (P("visit", "row", "col"), P("visit", None))
    return jax.shard_map(shards, mesh=mesh, in_specs=in_specs, out_specs=out_specs, check_vma=False)
```

```python
import functools

import jax
import jax.numpy as jnp
import ml_dtypes
import numpy as np
from jax import lax
from jax.sharding import PartitionSpec as P
from jax.experimental import pallas as pl
from jax.experimental.pallas import tpu as pltpu

HALO = 16
STRIP = 32
MAXD = 4


SIGMA_PARTS = (0.0625, 0.125, 0.25)


def extended(value, sides, width):
    for axis, dim in sides:
        devices, length = (lax.axis_size(axis), value.shape[dim])
        last = lax.slice_in_dim(value, length - width, length, axis=dim)
        initial = lax.slice_in_dim(value, 0, width, axis=dim)
        minor = dim == value.ndim - 1
        if minor:
            flat = value.shape[:-2] + (-1,)
            turned = jnp.swapaxes(last, -1, -2).shape
            last = jnp.swapaxes(last, -1, -2).reshape(flat)
            initial = jnp.swapaxes(initial, -1, -2).reshape(flat)
        if devices == 2:
            position = lax.axis_index(axis)
            facing = jnp.where(position == 0, last, initial)
            arrived = lax.ppermute(facing, axis, [(0, 1), (1, 0)])
            empty = jnp.zeros_like(arrived)
            before = jnp.where(position == 1, arrived, empty)
            after = jnp.where(position == 0, arrived, empty)
        else:
            up = [(i, (i + 1) % devices) for i in range(devices - 1)]
            down = [(j, i) for i, j in up]
            before = lax.ppermute(last, axis, up)
            after = lax.ppermute(initial, axis, down)
        if minor:
            before = jnp.swapaxes(before.reshape(turned), -1, -2)
            after = jnp.swapaxes(after.reshape(turned), -1, -2)
        value = jnp.concatenate([before, value, after], axis=dim)
    return value


def toeplitz_block(size, width, sigma):
    spread = (np.arange(2 * width + 1) - width).astype(np.float32)
    scale = np.float32(2.0) * np.float32(sigma) * np.float32(sigma)
    total = np.float32(np.exp(-spread * spread / scale).astype(np.float32).sum(dtype=np.float32))
    offset = (np.arange(size)[None, :] - np.arange(size)[:, None] - width).astype(np.float32)
    values = (np.exp(-offset * offset / scale).astype(np.float32) / total).astype(np.float32)
    values = np.where(np.abs(offset) <= width, values, np.float32(0.0))
    return values.astype(ml_dtypes.bfloat16)


def band_table(length, width, sigma):
    spread = (jnp.arange(2 * width + 1) - width).astype(jnp.float32)
    curve = jnp.exp(-spread * spread / (2.0 * sigma * sigma))
    total = jnp.sum(curve)
    rows_grid = lax.broadcasted_iota(jnp.int32, (length, length + 2 * width), 0)
    cols_grid = lax.broadcasted_iota(jnp.int32, (length, length + 2 * width), 1)
    offset = (cols_grid - rows_grid - width).astype(jnp.float32)
    values = jnp.exp(-offset * offset / (2.0 * sigma * sigma)) / total
    return jnp.where(jnp.abs(offset) <= width, values, 0.0).astype(jnp.bfloat16)


def centred(index, length):
    return (index.astype(jnp.float32) + 0.5) / length * 2.0 - 1.0


def solve_three(normal, moments):
    lower = jnp.linalg.cholesky(normal)
    first = moments[..., 0] / lower[..., 0, 0]
    second = (moments[..., 1] - lower[..., 1, 0] * first) / lower[..., 1, 1]
    third = (moments[..., 2] - lower[..., 2, 0] * first - lower[..., 2, 1] * second) / lower[
        ..., 2, 2
    ]
    upper_top = third / lower[..., 2, 2]
    upper_mid = (second - lower[..., 2, 1] * upper_top) / lower[..., 1, 1]
    upper_low = (first - lower[..., 1, 0] * upper_mid - lower[..., 2, 0] * upper_top) / lower[
        ..., 0, 0
    ]
    return jnp.stack([upper_low, upper_mid, upper_top], -1)


def butterfly_sum(values, axes):
    for axis, size in axes:
        if size & (size - 1) == 0:
            bit = 1
            while bit < size:
                pairs = [(i, i ^ bit) for i in range(size)]
                values = jax.tree.map(lambda v: v + lax.ppermute(v, axis, pairs), values)
                bit *= 2
        else:
            position = lax.axis_index(axis)
            def gathered(v):
                parts = [v]
                for shift in range(1, size):
                    pairs = [(i, (i + shift) % size) for i in range(size)]
                    parts.append(lax.ppermute(v, axis, pairs))
                stacked = jnp.stack(parts, 0)
                order = (position - jnp.arange(size)) % size
                canonical = jnp.zeros_like(stacked).at[order].set(stacked)
                return jnp.sum(canonical, axis=0)
            values = jax.tree.map(gathered, values)
    return values


def conv_body(coef_ref, vt_ref, ht_ref, padded_ref, out_ref):
    e = pl.program_id(0)
    image = padded_ref[0]
    total = None
    for kernel in range(len(SIGMA_PARTS)):
        across = jnp.dot(vt_ref[0, kernel], image, preferred_element_type=jnp.float32)
        smoothed = lax.dot_general(
            across.astype(jnp.bfloat16), ht_ref[kernel], (((1,), (1,)), ((), ())),
            preferred_element_type=jnp.float32,
        )
        term = coef_ref[e, kernel] * smoothed
        total = term if total is None else total + term
    out_ref[0] = total


def conv_tiles(coeffs, vtables, htables, padded, per_exposure):
    exp_dev, wide = padded.shape[0], padded.shape[1]
    nk, out_rows = vtables.shape[-3], vtables.shape[-2]
    tile_len = htables.shape[1]
    if per_exposure:
        vspec = pl.BlockSpec((1, nk, out_rows, wide), lambda e: (e, 0, 0, 0))
    else:
        vtables = vtables[None]
        vspec = pl.BlockSpec((1, nk, out_rows, wide), lambda e: (0, 0, 0, 0))
    flops = exp_dev * nk * 2 * out_rows * wide * (wide + tile_len)
    moved = exp_dev * wide * wide * 2 + exp_dev * out_rows * tile_len * 4
    return pl.pallas_call(
        conv_body,
        grid=(exp_dev,),
        in_specs=[
            pl.BlockSpec(memory_space=pltpu.SMEM),
            vspec,
            pl.BlockSpec((nk, tile_len, wide), lambda e: (0, 0, 0)),
            pl.BlockSpec((1, wide, wide), lambda e: (e, 0, 0)),
        ],
        out_specs=pl.BlockSpec((1, out_rows, tile_len), lambda e: (e, 0, 0)),
        out_shape=jax.ShapeDtypeStruct((exp_dev, out_rows, tile_len), jnp.float32),
        compiler_params=pltpu.CompilerParams(
            dimension_semantics=("arbitrary",), vmem_limit_bytes=48 * 1024 * 1024
        ),
        cost_estimate=pl.CostEstimate(flops=flops, bytes_accessed=moved, transcendentals=0),
    )(coeffs, vtables, htables, padded)


BLOCK = 128


def strip_body(off_ref, coef_ref, tb_ref, padded_ref, out_ref):
    e = pl.program_id(0)
    rows, tile_len = out_ref.shape[1], out_ref.shape[2]
    wide = padded_ref.shape[1]
    windows = [(start, min(2 * BLOCK, wide - start)) for start in range(0, tile_len, BLOCK)]
    anchor = off_ref[e]
    base = jnp.minimum((anchor // BLOCK) * BLOCK, wide - 2 * BLOCK)
    shift = anchor - base
    window = padded_ref[0, pl.ds(pl.multiple_of(base, 16), 2 * BLOCK), :]
    pick = (
        lax.broadcasted_iota(jnp.int32, (rows, 2 * BLOCK), 1)
        == lax.broadcasted_iota(jnp.int32, (rows, 2 * BLOCK), 0) + shift
    ).astype(jnp.bfloat16)
    total = None
    for kernel in range(len(SIGMA_PARTS)):
        table = tb_ref[kernel]
        strip_rows = jnp.dot(pick, table, preferred_element_type=jnp.float32).astype(jnp.bfloat16)
        across = jnp.dot(strip_rows, window, preferred_element_type=jnp.float32)
        across = across.astype(jnp.bfloat16)
        block = table[:BLOCK]
        cols = [
            lax.dot_general(
                across[:, start:start + reach], block[:, :reach], (((1,), (1,)), ((), ())),
                preferred_element_type=jnp.float32,
            )
            for start, reach in windows
        ]
        term = coef_ref[e, kernel] * jnp.concatenate(cols, 1)
        total = term if total is None else total + term
    out_ref[0] = total


def strip_tiles(offset, coeffs, tb, padded, tile_len):
    exp_dev, wide = padded.shape[0], padded.shape[1]
    nk = tb.shape[0]
    grid_spec = pltpu.PrefetchScalarGridSpec(
        num_scalar_prefetch=1,
        grid=(exp_dev,),
        in_specs=[
            pl.BlockSpec(memory_space=pltpu.SMEM),
            pl.BlockSpec((nk, 2 * BLOCK, 2 * BLOCK), lambda e, off: (0, 0, 0)),
            pl.BlockSpec((1, wide, wide), lambda e, off: (e, 0, 0)),
        ],
        out_specs=pl.BlockSpec((1, STRIP, tile_len), lambda e, off: (e, 0, 0)),
    )
    flops = exp_dev * nk * 2 * STRIP * 2 * BLOCK * (2 * BLOCK + wide + tile_len)
    moved = exp_dev * wide * wide * 2 + exp_dev * STRIP * tile_len * 4
    return pl.pallas_call(
        strip_body,
        grid_spec=grid_spec,
        out_shape=jax.ShapeDtypeStruct((exp_dev, STRIP, tile_len), jnp.float32),
        compiler_params=pltpu.CompilerParams(
            dimension_semantics=("arbitrary",), vmem_limit_bytes=48 * 1024 * 1024
        ),
        cost_estimate=pl.CostEstimate(flops=flops, bytes_accessed=moved, transcendentals=0),
    )(offset, coeffs, tb, padded)


def band_body(first, coef_ref, blk_ref, padded_ref, *rest):
    out_ref = rest[-1]
    e = pl.program_id(0) + first
    tile_len = out_ref.shape[1]
    wide = padded_ref.shape[1]
    windows = [(start, min(2 * BLOCK, wide - start)) for start in range(0, tile_len, BLOCK)]
    total = None
    for kernel in range(len(SIGMA_PARTS)):
        block = blk_ref[kernel][:BLOCK]
        rows = [
            jnp.dot(
                block[:, :reach], padded_ref[0, start:start + reach, :],
                preferred_element_type=jnp.float32,
            )
            for start, reach in windows
        ]
        across = jnp.concatenate(rows, 0).astype(jnp.bfloat16)
        cols = [
            lax.dot_general(
                across[:, start:start + reach], block[:, :reach], (((1,), (1,)), ((), ())),
                preferred_element_type=jnp.float32,
            )
            for start, reach in windows
        ]
        term = coef_ref[e, kernel] * jnp.concatenate(cols, 1)
        total = term if total is None else total + term
    out_ref[0] = total


def band_tiles(coeffs, blocks, padded, tile_len, first, count, into):
    exp_dev, wide = padded.shape[0], padded.shape[1]
    nk = blocks.shape[0]
    steps = tile_len // BLOCK
    flops = count * nk * steps * 2 * BLOCK * 2 * BLOCK * (wide + tile_len)
    moved = count * wide * wide * 2 + count * tile_len * tile_len * 4
    in_specs = [
        pl.BlockSpec(memory_space=pltpu.SMEM),
        pl.BlockSpec((nk, 2 * BLOCK, 2 * BLOCK), lambda e: (0, 0, 0)),
        pl.BlockSpec((1, wide, wide), lambda e: (e + first, 0, 0)),
    ]
    operands = [coeffs, blocks, padded]
    aliases = {}
    if into is not None:
        in_specs.append(pl.BlockSpec(memory_space=pl.ANY))
        operands.append(into)
        aliases = {3: 0}
    return pl.pallas_call(
        functools.partial(band_body, first),
        grid=(count,),
        in_specs=in_specs,
        out_specs=pl.BlockSpec((1, tile_len, tile_len), lambda e: (e + first, 0, 0)),
        out_shape=jax.ShapeDtypeStruct((exp_dev, tile_len, tile_len), jnp.float32),
        input_output_aliases=aliases,
        compiler_params=pltpu.CompilerParams(
            dimension_semantics=("arbitrary",), vmem_limit_bytes=48 * 1024 * 1024
        ),
        cost_estimate=pl.CostEstimate(flops=flops, bytes_accessed=moved, transcendentals=0),
    )(*operands)


def warp_body(idx_ref, plane_ref, pick_ref, xrow_ref, ycol_ref, matched_ref, rmap_ref, cmap_ref,
              out_ref, acc_ref):
    e = pl.program_id(0)
    background = (
        plane_ref[e, 0] + plane_ref[e, 1] * xrow_ref[...]
    ) + plane_ref[e, 2] * ycol_ref[...]
    corrected = (matched_ref[0] - background).astype(jnp.bfloat16)
    halfway = jnp.dot(rmap_ref[0], corrected, preferred_element_type=jnp.float32)
    warped = lax.dot_general(
        halfway.astype(jnp.bfloat16), cmap_ref[0], (((1,), (1,)), ((), ())),
        preferred_element_type=jnp.float32,
    )
    warped = warped.astype(jnp.bfloat16).astype(jnp.float32)
    patches = acc_ref.shape[0]

    @pl.when(e == 0)
    def _():
        for v in range(patches):
            acc_ref[v] = pick_ref[e, v] * warped

    @pl.when(e > 0)
    def _():
        for v in range(patches):
            acc_ref[v] = acc_ref[v] + pick_ref[e, v] * warped

    @pl.when(e == pl.num_programs(0) - 1)
    def _():
        out_ref[...] = acc_ref[...].astype(jnp.bfloat16)


def warp_tiles(choose, plane, picked, xrow, ycol, matched, bank):
    exp_dev, tile_len = matched.shape[0], matched.shape[1]
    patches = picked.shape[1]
    grid_spec = pltpu.PrefetchScalarGridSpec(
        num_scalar_prefetch=1,
        grid=(exp_dev,),
        in_specs=[
            pl.BlockSpec(memory_space=pltpu.SMEM),
            pl.BlockSpec(memory_space=pltpu.SMEM),
            pl.BlockSpec((1, tile_len), lambda e, idx: (0, 0)),
            pl.BlockSpec((tile_len, 1), lambda e, idx: (0, 0)),
            pl.BlockSpec((1, tile_len, tile_len), lambda e, idx: (e, 0, 0)),
            pl.BlockSpec((1, tile_len, tile_len), lambda e, idx: (idx[e, 0], 0, 0)),
            pl.BlockSpec((1, tile_len, tile_len), lambda e, idx: (idx[e, 1], 0, 0)),
        ],
        out_specs=pl.BlockSpec((patches, tile_len, tile_len), lambda e, idx: (0, 0, 0)),
        scratch_shapes=[pltpu.VMEM((patches, tile_len, tile_len), jnp.float32)],
    )
    flops = exp_dev * 4 * tile_len ** 3
    moved = exp_dev * tile_len * tile_len * (4 + 2 + 2) + patches * tile_len * tile_len * 2
    vmem = 60 * 1024 * 1024
    return pl.pallas_call(
        warp_body,
        grid_spec=grid_spec,
        out_shape=jax.ShapeDtypeStruct((patches, tile_len, tile_len), jnp.bfloat16),
        compiler_params=pltpu.CompilerParams(
            dimension_semantics=("arbitrary",), vmem_limit_bytes=vmem
        ),
        cost_estimate=pl.CostEstimate(flops=flops, bytes_accessed=moved, transcendentals=0),
    )(choose, plane, picked, xrow, ycol, matched, bank, bank)


def ring_scatter(parts, axis, size, position):
    ring = [(i, (i + 1) % size) for i in range(size)]
    travelling = None
    for step in range(size - 1):
        block = (position - step - 1) % size
        own = lax.dynamic_index_in_dim(parts, block, 0, False).astype(jnp.float32)
        outgoing = own if travelling is None else travelling + own
        travelling = lax.ppermute(outgoing.astype(jnp.bfloat16), axis, ring).astype(jnp.float32)
    own = lax.dynamic_index_in_dim(parts, position, 0, False).astype(jnp.float32)
    return own if travelling is None else travelling + own


def rows_from(source, anchor):
    return lax.dynamic_slice_in_dim(source, anchor, STRIP, 0)


def shards(images, coeffs, pair_list, weights, resample_bank, warp_index, destinations, counts):
    exp_dev = images.shape[0]
    tile_len = images.shape[1]
    row_count = lax.axis_size("row")
    col_count = lax.axis_size("col")
    visit_count = lax.axis_size("visit")
    row_pos = lax.axis_index("row")
    col_pos = lax.axis_index("col")
    visit_pos = lax.axis_index("visit")
    height = row_count * tile_len
    breadth = col_count * tile_len
    padded = extended(images, (("col", 2), ("row", 1)), HALO)
    own_ids = visit_pos * exp_dev + jnp.arange(exp_dev, dtype=jnp.int32)
    first_col = pair_list[:, 0]
    second_col = pair_list[:, 1]
    offsets = pair_list[:, 2]
    hit_first = first_col[None, :] == own_ids[:, None]
    hit_second = second_col[None, :] == own_ids[:, None]
    partner = jnp.sum(
        jnp.where(hit_first, second_col[None, :], 0) + jnp.where(hit_second, first_col[None, :], 0),
        axis=1,
    )
    offset = jnp.sum(jnp.where(hit_first | hit_second, offsets[None, :], 0), axis=1)
    pick_rows = (
        lax.broadcasted_iota(jnp.int32, (exp_dev, STRIP, tile_len), 2)
        == offset[:, None, None] + lax.broadcasted_iota(jnp.int32, (exp_dev, STRIP, tile_len), 1)
    ).astype(jnp.bfloat16)
    own_strip = jnp.einsum(
        "esr,erl->esl", pick_rows, images, preferred_element_type=jnp.float32
    ).astype(jnp.bfloat16)
    listed = destinations[:, 0, 0, :]
    how_many = counts[:, 0, 0]
    usable = jnp.arange(MAXD, dtype=jnp.int32)[None, :] < how_many[:, None]
    owners = jnp.arange(visit_count, dtype=jnp.int32)
    member = jnp.any(usable[:, :, None] & (listed[:, :, None] == owners[None, None, :]), axis=1)
    tile_weight = weights[:, 0, 0]
    nothing = jnp.zeros((), jnp.bfloat16)
    picked = jnp.where(member, tile_weight[:, None], nothing)
    strip_rows_n = exp_dev * STRIP
    extra = -(-(exp_dev * visit_count) // tile_len)
    extra = -(-extra // 16) * 16
    tail = jnp.zeros((extra * tile_len,), jnp.bfloat16)
    tail = tail.at[: exp_dev * visit_count].set(picked.reshape(-1)).reshape(extra, tile_len)
    payload = jnp.concatenate([own_strip.reshape(strip_rows_n, tile_len), tail], axis=0)
    received = [payload]
    for shift in range(1, visit_count):
        pairs = [(i, (i + shift) % visit_count) for i in range(visit_count)]
        received.append(lax.ppermute(payload, "visit", pairs))
    stacked = jnp.stack(received, 0)
    strips_all = stacked[:, :strip_rows_n].reshape(visit_count * exp_dev, STRIP, tile_len)
    picked_all = stacked[:, strip_rows_n:].reshape(visit_count, -1)[:, : exp_dev * visit_count]
    picked_all = picked_all.reshape(visit_count, exp_dev, visit_count)
    partner_visit = partner // exp_dev
    slot = (visit_pos - partner_visit) % visit_count
    source = slot * exp_dev + partner % exp_dev
    choose_strip = (
        lax.broadcasted_iota(jnp.int32, (exp_dev, visit_count * exp_dev), 1) == source[:, None]
    ).astype(jnp.bfloat16)
    theirs = jnp.einsum(
        "ej,jsl->esl", choose_strip, strips_all, preferred_element_type=jnp.float32
    )
    own_patch = jnp.take(picked_all, visit_pos, axis=2).astype(jnp.float32)
    denominator = jnp.sum(own_patch).reshape(1)
    roomy = padded
    blocks = jnp.asarray(
        np.stack([toeplitz_block(2 * BLOCK, HALO, HALO * part) for part in SIGMA_PARTS])
    )
    nearby = strip_tiles(offset, coeffs, blocks, roomy, tile_len)
    half = exp_dev // 2
    matched = band_tiles(coeffs, blocks, roomy, tile_len, 0, half, None)
    matched = band_tiles(coeffs, blocks, roomy, tile_len, half, exp_dev - half, matched)
    difference = nearby - theirs
    pixel_weight = 1.0 / (1.0 + theirs * theirs)
    strip_rows = row_pos * tile_len + offset[:, None] + jnp.arange(STRIP, dtype=jnp.int32)[None, :]
    ycoord = centred(strip_rows, height)[:, :, None]
    xcoord = centred(col_pos * tile_len + jnp.arange(tile_len, dtype=jnp.int32), breadth)
    xgrid = xcoord[None, None, :]
    weight_x = pixel_weight * xgrid
    weight_y = pixel_weight * ycoord
    sum_w = jnp.sum(pixel_weight, axis=(1, 2))
    sum_x = jnp.sum(weight_x, axis=(1, 2))
    sum_y = jnp.sum(weight_y, axis=(1, 2))
    sum_xx = jnp.sum(weight_x * xgrid, axis=(1, 2))
    sum_xy = jnp.sum(weight_x * ycoord, axis=(1, 2))
    sum_yy = jnp.sum(weight_y * ycoord, axis=(1, 2))
    normal = jnp.stack(
        [
            jnp.stack([sum_w, sum_x, sum_y], -1),
            jnp.stack([sum_x, sum_xx, sum_xy], -1),
            jnp.stack([sum_y, sum_xy, sum_yy], -1),
        ],
        1,
    )
    moments = jnp.stack(
        [
            jnp.sum(pixel_weight * difference, axis=(1, 2)),
            jnp.sum(weight_x * difference, axis=(1, 2)),
            jnp.sum(weight_y * difference, axis=(1, 2)),
        ],
        -1,
    )
    packed = jnp.concatenate([normal.reshape(exp_dev, 9), moments], axis=1)
    packed = butterfly_sum(packed, (("row", row_count), ("col", col_count)))
    normal = packed[:, :9].reshape(exp_dev, 3, 3)
    moments = packed[:, 9:]
    plane_fit = solve_three(normal, moments)
    row_coord = centred(row_pos * tile_len + jnp.arange(tile_len, dtype=jnp.int32), height)
    choose = warp_index[:, 0, 0, :]
    partial_sum = warp_tiles(
        choose, plane_fit, picked.astype(jnp.float32), xcoord.reshape(1, tile_len),
        row_coord.reshape(tile_len, 1), matched, resample_bank,
    )
    numerator = ring_scatter(partial_sum, "visit", visit_count, visit_pos)[None]
    coadd_patch = numerator / denominator[:, None, None]
    return (coadd_patch, plane_fit)


def solution(mesh):
    in_specs = (
        P("visit", "row", "col"),
        P("visit", None),
        P(),
        P("visit", "row", "col"),
        P(),
        P("visit", "row", "col", None),
        P("visit", "row", "col", None),
        P("visit", "row", "col"),
    )
    out_specs = (P("visit", "row", "col"), P("visit", None))
    return jax.shard_map(shards, mesh=mesh, in_specs=in_specs, out_specs=out_specs, check_vma=False)
```

```python
import functools

import jax
import jax.numpy as jnp
import ml_dtypes
import numpy as np
from jax import lax
from jax.sharding import PartitionSpec as P
from jax.experimental import pallas as pl
from jax.experimental.pallas import tpu as pltpu

HALO = 16
STRIP = 32
MAXD = 4


SIGMA_PARTS = (0.0625, 0.125, 0.25)


def extended(value, sides, width):
    for axis, dim in sides:
        devices, length = (lax.axis_size(axis), value.shape[dim])
        last = lax.slice_in_dim(value, length - width, length, axis=dim)
        initial = lax.slice_in_dim(value, 0, width, axis=dim)
        minor = dim == value.ndim - 1
        if minor:
            flat = value.shape[:-2] + (-1,)
            turned = jnp.swapaxes(last, -1, -2).shape
            last = jnp.swapaxes(last, -1, -2).reshape(flat)
            initial = jnp.swapaxes(initial, -1, -2).reshape(flat)
        if devices == 2:
            position = lax.axis_index(axis)
            facing = jnp.where(position == 0, last, initial)
            arrived = lax.ppermute(facing, axis, [(0, 1), (1, 0)])
            empty = jnp.zeros_like(arrived)
            before = jnp.where(position == 1, arrived, empty)
            after = jnp.where(position == 0, arrived, empty)
        else:
            up = [(i, (i + 1) % devices) for i in range(devices - 1)]
            down = [(j, i) for i, j in up]
            before = lax.ppermute(last, axis, up)
            after = lax.ppermute(initial, axis, down)
        if minor:
            before = jnp.swapaxes(before.reshape(turned), -1, -2)
            after = jnp.swapaxes(after.reshape(turned), -1, -2)
        value = jnp.concatenate([before, value, after], axis=dim)
    return value


def toeplitz_block(size, width, sigma):
    spread = (np.arange(2 * width + 1) - width).astype(np.float32)
    scale = np.float32(2.0) * np.float32(sigma) * np.float32(sigma)
    total = np.float32(np.exp(-spread * spread / scale).astype(np.float32).sum(dtype=np.float32))
    offset = (np.arange(size)[None, :] - np.arange(size)[:, None] - width).astype(np.float32)
    values = (np.exp(-offset * offset / scale).astype(np.float32) / total).astype(np.float32)
    values = np.where(np.abs(offset) <= width, values, np.float32(0.0))
    return values.astype(ml_dtypes.bfloat16)


def band_table(length, width, sigma):
    spread = (jnp.arange(2 * width + 1) - width).astype(jnp.float32)
    curve = jnp.exp(-spread * spread / (2.0 * sigma * sigma))
    total = jnp.sum(curve)
    rows_grid = lax.broadcasted_iota(jnp.int32, (length, length + 2 * width), 0)
    cols_grid = lax.broadcasted_iota(jnp.int32, (length, length + 2 * width), 1)
    offset = (cols_grid - rows_grid - width).astype(jnp.float32)
    values = jnp.exp(-offset * offset / (2.0 * sigma * sigma)) / total
    return jnp.where(jnp.abs(offset) <= width, values, 0.0).astype(jnp.bfloat16)


def centred(index, length):
    return (index.astype(jnp.float32) + 0.5) / length * 2.0 - 1.0


def solve_three(normal, moments):
    lower = jnp.linalg.cholesky(normal)
    first = moments[..., 0] / lower[..., 0, 0]
    second = (moments[..., 1] - lower[..., 1, 0] * first) / lower[..., 1, 1]
    third = (moments[..., 2] - lower[..., 2, 0] * first - lower[..., 2, 1] * second) / lower[
        ..., 2, 2
    ]
    upper_top = third / lower[..., 2, 2]
    upper_mid = (second - lower[..., 2, 1] * upper_top) / lower[..., 1, 1]
    upper_low = (first - lower[..., 1, 0] * upper_mid - lower[..., 2, 0] * upper_top) / lower[
        ..., 0, 0
    ]
    return jnp.stack([upper_low, upper_mid, upper_top], -1)


def butterfly_sum(values, axes):
    for axis, size in axes:
        if size & (size - 1) == 0:
            bit = 1
            while bit < size:
                pairs = [(i, i ^ bit) for i in range(size)]
                values = jax.tree.map(lambda v: v + lax.ppermute(v, axis, pairs), values)
                bit *= 2
        else:
            position = lax.axis_index(axis)
            def gathered(v):
                parts = [v]
                for shift in range(1, size):
                    pairs = [(i, (i + shift) % size) for i in range(size)]
                    parts.append(lax.ppermute(v, axis, pairs))
                stacked = jnp.stack(parts, 0)
                order = (position - jnp.arange(size)) % size
                canonical = jnp.zeros_like(stacked).at[order].set(stacked)
                return jnp.sum(canonical, axis=0)
            values = jax.tree.map(gathered, values)
    return values


def conv_body(coef_ref, vt_ref, ht_ref, padded_ref, out_ref):
    e = pl.program_id(0)
    image = padded_ref[0]
    total = None
    for kernel in range(len(SIGMA_PARTS)):
        across = jnp.dot(vt_ref[0, kernel], image, preferred_element_type=jnp.float32)
        smoothed = lax.dot_general(
            across.astype(jnp.bfloat16), ht_ref[kernel], (((1,), (1,)), ((), ())),
            preferred_element_type=jnp.float32,
        )
        term = coef_ref[e, kernel] * smoothed
        total = term if total is None else total + term
    out_ref[0] = total


def conv_tiles(coeffs, vtables, htables, padded, per_exposure):
    exp_dev, wide = padded.shape[0], padded.shape[1]
    nk, out_rows = vtables.shape[-3], vtables.shape[-2]
    tile_len = htables.shape[1]
    if per_exposure:
        vspec = pl.BlockSpec((1, nk, out_rows, wide), lambda e: (e, 0, 0, 0))
    else:
        vtables = vtables[None]
        vspec = pl.BlockSpec((1, nk, out_rows, wide), lambda e: (0, 0, 0, 0))
    flops = exp_dev * nk * 2 * out_rows * wide * (wide + tile_len)
    moved = exp_dev * wide * wide * 2 + exp_dev * out_rows * tile_len * 4
    return pl.pallas_call(
        conv_body,
        grid=(exp_dev,),
        in_specs=[
            pl.BlockSpec(memory_space=pltpu.SMEM),
            vspec,
            pl.BlockSpec((nk, tile_len, wide), lambda e: (0, 0, 0)),
            pl.BlockSpec((1, wide, wide), lambda e: (e, 0, 0)),
        ],
        out_specs=pl.BlockSpec((1, out_rows, tile_len), lambda e: (e, 0, 0)),
        out_shape=jax.ShapeDtypeStruct((exp_dev, out_rows, tile_len), jnp.float32),
        compiler_params=pltpu.CompilerParams(
            dimension_semantics=("arbitrary",), vmem_limit_bytes=48 * 1024 * 1024
        ),
        cost_estimate=pl.CostEstimate(flops=flops, bytes_accessed=moved, transcendentals=0),
    )(coeffs, vtables, htables, padded)


BLOCK = 128


def strip_body(off_ref, coef_ref, tb_ref, padded_ref, out_ref):
    e = pl.program_id(0)
    rows, tile_len = out_ref.shape[1], out_ref.shape[2]
    wide = padded_ref.shape[1]
    windows = [(start, min(2 * BLOCK, wide - start)) for start in range(0, tile_len, BLOCK)]
    anchor = off_ref[e]
    base = jnp.minimum((anchor // BLOCK) * BLOCK, wide - 2 * BLOCK)
    shift = anchor - base
    window = padded_ref[0, pl.ds(pl.multiple_of(base, 16), 2 * BLOCK), :]
    pick = (
        lax.broadcasted_iota(jnp.int32, (rows, 2 * BLOCK), 1)
        == lax.broadcasted_iota(jnp.int32, (rows, 2 * BLOCK), 0) + shift
    ).astype(jnp.bfloat16)
    total = None
    for kernel in range(len(SIGMA_PARTS)):
        table = tb_ref[kernel]
        strip_rows = jnp.dot(pick, table, preferred_element_type=jnp.float32).astype(jnp.bfloat16)
        across = jnp.dot(strip_rows, window, preferred_element_type=jnp.float32)
        across = across.astype(jnp.bfloat16)
        block = table[:BLOCK]
        cols = [
            lax.dot_general(
                across[:, start:start + reach], block[:, :reach], (((1,), (1,)), ((), ())),
                preferred_element_type=jnp.float32,
            )
            for start, reach in windows
        ]
        term = coef_ref[e, kernel] * jnp.concatenate(cols, 1)
        total = term if total is None else total + term
    out_ref[0] = total


def strip_tiles(offset, coeffs, tb, padded, tile_len):
    exp_dev, wide = padded.shape[0], padded.shape[1]
    nk = tb.shape[0]
    grid_spec = pltpu.PrefetchScalarGridSpec(
        num_scalar_prefetch=1,
        grid=(exp_dev,),
        in_specs=[
            pl.BlockSpec(memory_space=pltpu.SMEM),
            pl.BlockSpec((nk, 2 * BLOCK, 2 * BLOCK), lambda e, off: (0, 0, 0)),
            pl.BlockSpec((1, wide, wide), lambda e, off: (e, 0, 0)),
        ],
        out_specs=pl.BlockSpec((1, STRIP, tile_len), lambda e, off: (e, 0, 0)),
    )
    flops = exp_dev * nk * 2 * STRIP * 2 * BLOCK * (2 * BLOCK + wide + tile_len)
    moved = exp_dev * wide * wide * 2 + exp_dev * STRIP * tile_len * 4
    return pl.pallas_call(
        strip_body,
        grid_spec=grid_spec,
        out_shape=jax.ShapeDtypeStruct((exp_dev, STRIP, tile_len), jnp.float32),
        compiler_params=pltpu.CompilerParams(
            dimension_semantics=("arbitrary",), vmem_limit_bytes=48 * 1024 * 1024
        ),
        cost_estimate=pl.CostEstimate(flops=flops, bytes_accessed=moved, transcendentals=0),
    )(offset, coeffs, tb, padded)


def band_body(first, coef_ref, blk_ref, padded_ref, *rest):
    out_ref = rest[-1]
    e = pl.program_id(0) + first
    tile_len = out_ref.shape[1]
    wide = padded_ref.shape[1]
    windows = [(start, min(2 * BLOCK, wide - start)) for start in range(0, tile_len, BLOCK)]
    total = None
    for kernel in range(len(SIGMA_PARTS)):
        block = blk_ref[kernel][:BLOCK]
        rows = [
            jnp.dot(
                block[:, :reach], padded_ref[0, start:start + reach, :],
                preferred_element_type=jnp.float32,
            )
            for start, reach in windows
        ]
        across = jnp.concatenate(rows, 0).astype(jnp.bfloat16)
        cols = [
            lax.dot_general(
                across[:, start:start + reach], block[:, :reach], (((1,), (1,)), ((), ())),
                preferred_element_type=jnp.float32,
            )
            for start, reach in windows
        ]
        term = coef_ref[e, kernel] * jnp.concatenate(cols, 1)
        total = term if total is None else total + term
    out_ref[0] = total


def band_tiles(coeffs, blocks, padded, tile_len, first, count, into):
    exp_dev, wide = padded.shape[0], padded.shape[1]
    nk = blocks.shape[0]
    steps = tile_len // BLOCK
    flops = count * nk * steps * 2 * BLOCK * 2 * BLOCK * (wide + tile_len)
    moved = count * wide * wide * 2 + count * tile_len * tile_len * 4
    in_specs = [
        pl.BlockSpec(memory_space=pltpu.SMEM),
        pl.BlockSpec((nk, 2 * BLOCK, 2 * BLOCK), lambda e: (0, 0, 0)),
        pl.BlockSpec((1, wide, wide), lambda e: (e + first, 0, 0)),
    ]
    operands = [coeffs, blocks, padded]
    aliases = {}
    if into is not None:
        in_specs.append(pl.BlockSpec(memory_space=pl.ANY))
        operands.append(into)
        aliases = {3: 0}
    return pl.pallas_call(
        functools.partial(band_body, first),
        grid=(count,),
        in_specs=in_specs,
        out_specs=pl.BlockSpec((1, tile_len, tile_len), lambda e: (e + first, 0, 0)),
        out_shape=jax.ShapeDtypeStruct((exp_dev, tile_len, tile_len), jnp.float32),
        input_output_aliases=aliases,
        compiler_params=pltpu.CompilerParams(
            dimension_semantics=("arbitrary",), vmem_limit_bytes=48 * 1024 * 1024
        ),
        cost_estimate=pl.CostEstimate(flops=flops, bytes_accessed=moved, transcendentals=0),
    )(*operands)


def warp_body(idx_ref, plane_ref, pick_ref, xrow_ref, ycol_ref, matched_ref, rmap_ref, cmap_ref,
              out_ref, acc_ref):
    e = pl.program_id(0)
    background = (
        plane_ref[e, 0] + plane_ref[e, 1] * xrow_ref[...]
    ) + plane_ref[e, 2] * ycol_ref[...]
    corrected = (matched_ref[0] - background).astype(jnp.bfloat16)
    halfway = jnp.dot(rmap_ref[0], corrected, preferred_element_type=jnp.float32)
    warped = lax.dot_general(
        halfway.astype(jnp.bfloat16), cmap_ref[0], (((1,), (1,)), ((), ())),
        preferred_element_type=jnp.float32,
    )
    warped = warped.astype(jnp.bfloat16).astype(jnp.float32)
    patches = acc_ref.shape[0]

    @pl.when(e == 0)
    def _():
        for v in range(patches):
            acc_ref[v] = pick_ref[e, v] * warped

    @pl.when(e > 0)
    def _():
        for v in range(patches):
            acc_ref[v] = acc_ref[v] + pick_ref[e, v] * warped

    @pl.when(e == pl.num_programs(0) - 1)
    def _():
        out_ref[...] = acc_ref[...].astype(jnp.bfloat16)


def warp_tiles(choose, plane, picked, xrow, ycol, matched, bank):
    exp_dev, tile_len = matched.shape[0], matched.shape[1]
    patches = picked.shape[1]
    grid_spec = pltpu.PrefetchScalarGridSpec(
        num_scalar_prefetch=1,
        grid=(exp_dev,),
        in_specs=[
            pl.BlockSpec(memory_space=pltpu.SMEM),
            pl.BlockSpec(memory_space=pltpu.SMEM),
            pl.BlockSpec((1, tile_len), lambda e, idx: (0, 0)),
            pl.BlockSpec((tile_len, 1), lambda e, idx: (0, 0)),
            pl.BlockSpec((1, tile_len, tile_len), lambda e, idx: (e, 0, 0)),
            pl.BlockSpec((1, tile_len, tile_len), lambda e, idx: (idx[e, 0], 0, 0)),
            pl.BlockSpec((1, tile_len, tile_len), lambda e, idx: (idx[e, 1], 0, 0)),
        ],
        out_specs=pl.BlockSpec((patches, tile_len, tile_len), lambda e, idx: (0, 0, 0)),
        scratch_shapes=[pltpu.VMEM((patches, tile_len, tile_len), jnp.float32)],
    )
    flops = exp_dev * 4 * tile_len ** 3
    moved = exp_dev * tile_len * tile_len * (4 + 2 + 2) + patches * tile_len * tile_len * 2
    vmem = 60 * 1024 * 1024
    return pl.pallas_call(
        warp_body,
        grid_spec=grid_spec,
        out_shape=jax.ShapeDtypeStruct((patches, tile_len, tile_len), jnp.bfloat16),
        compiler_params=pltpu.CompilerParams(
            dimension_semantics=("arbitrary",), vmem_limit_bytes=vmem
        ),
        cost_estimate=pl.CostEstimate(flops=flops, bytes_accessed=moved, transcendentals=0),
    )(choose, plane, picked, xrow, ycol, matched, bank, bank)


def ring_scatter(parts, axis, size):
    ring = [(i, (i + 1) % size) for i in range(size)]
    travelling = None
    for step in range(size - 1):
        own = parts[step].astype(jnp.float32)
        outgoing = own if travelling is None else travelling + own
        travelling = lax.ppermute(outgoing.astype(jnp.bfloat16), axis, ring).astype(jnp.float32)
    own = parts[size - 1].astype(jnp.float32)
    return own if travelling is None else travelling + own


def rows_from(source, anchor):
    return lax.dynamic_slice_in_dim(source, anchor, STRIP, 0)


def shards(images, coeffs, pair_list, weights, resample_bank, warp_index, destinations, counts):
    exp_dev = images.shape[0]
    tile_len = images.shape[1]
    row_count = lax.axis_size("row")
    col_count = lax.axis_size("col")
    visit_count = lax.axis_size("visit")
    row_pos = lax.axis_index("row")
    col_pos = lax.axis_index("col")
    visit_pos = lax.axis_index("visit")
    height = row_count * tile_len
    breadth = col_count * tile_len
    padded = extended(images, (("col", 2), ("row", 1)), HALO)
    own_ids = visit_pos * exp_dev + jnp.arange(exp_dev, dtype=jnp.int32)
    first_col = pair_list[:, 0]
    second_col = pair_list[:, 1]
    offsets = pair_list[:, 2]
    hit_first = first_col[None, :] == own_ids[:, None]
    hit_second = second_col[None, :] == own_ids[:, None]
    partner = jnp.sum(
        jnp.where(hit_first, second_col[None, :], 0) + jnp.where(hit_second, first_col[None, :], 0),
        axis=1,
    )
    offset = jnp.sum(jnp.where(hit_first | hit_second, offsets[None, :], 0), axis=1)
    pick_rows = (
        lax.broadcasted_iota(jnp.int32, (exp_dev, STRIP, tile_len), 2)
        == offset[:, None, None] + lax.broadcasted_iota(jnp.int32, (exp_dev, STRIP, tile_len), 1)
    ).astype(jnp.bfloat16)
    own_strip = jnp.einsum(
        "esr,erl->esl", pick_rows, images, preferred_element_type=jnp.float32
    ).astype(jnp.bfloat16)
    listed = destinations[:, 0, 0, :]
    how_many = counts[:, 0, 0]
    usable = jnp.arange(MAXD, dtype=jnp.int32)[None, :] < how_many[:, None]
    owners = jnp.arange(visit_count, dtype=jnp.int32)
    member = jnp.any(usable[:, :, None] & (listed[:, :, None] == owners[None, None, :]), axis=1)
    tile_weight = weights[:, 0, 0]
    nothing = jnp.zeros((), jnp.bfloat16)
    picked = jnp.where(member, tile_weight[:, None], nothing)
    strip_rows_n = exp_dev * STRIP
    extra = -(-(exp_dev * visit_count) // tile_len)
    extra = -(-extra // 16) * 16
    tail = jnp.zeros((extra * tile_len,), jnp.bfloat16)
    tail = tail.at[: exp_dev * visit_count].set(picked.reshape(-1)).reshape(extra, tile_len)
    payload = jnp.concatenate([own_strip.reshape(strip_rows_n, tile_len), tail], axis=0)
    received = [payload]
    for shift in range(1, visit_count):
        pairs = [(i, (i + shift) % visit_count) for i in range(visit_count)]
        received.append(lax.ppermute(payload, "visit", pairs))
    stacked = jnp.stack(received, 0)
    strips_all = stacked[:, :strip_rows_n].reshape(visit_count * exp_dev, STRIP, tile_len)
    picked_all = stacked[:, strip_rows_n:].reshape(visit_count, -1)[:, : exp_dev * visit_count]
    picked_all = picked_all.reshape(visit_count, exp_dev, visit_count)
    partner_visit = partner // exp_dev
    slot = (visit_pos - partner_visit) % visit_count
    source = slot * exp_dev + partner % exp_dev
    choose_strip = (
        lax.broadcasted_iota(jnp.int32, (exp_dev, visit_count * exp_dev), 1) == source[:, None]
    ).astype(jnp.bfloat16)
    theirs = jnp.einsum(
        "ej,jsl->esl", choose_strip, strips_all, preferred_element_type=jnp.float32
    )
    own_patch = jnp.take(picked_all, visit_pos, axis=2).astype(jnp.float32)
    denominator = jnp.sum(own_patch).reshape(1)
    roomy = padded
    blocks = jnp.asarray(
        np.stack([toeplitz_block(2 * BLOCK, HALO, HALO * part) for part in SIGMA_PARTS])
    )
    nearby = strip_tiles(offset, coeffs, blocks, roomy, tile_len)
    half = exp_dev // 2
    matched = band_tiles(coeffs, blocks, roomy, tile_len, 0, half, None)
    matched = band_tiles(coeffs, blocks, roomy, tile_len, half, exp_dev - half, matched)
    difference = nearby - theirs
    pixel_weight = 1.0 / (1.0 + theirs * theirs)
    strip_rows = row_pos * tile_len + offset[:, None] + jnp.arange(STRIP, dtype=jnp.int32)[None, :]
    ycoord = centred(strip_rows, height)[:, :, None]
    xcoord = centred(col_pos * tile_len + jnp.arange(tile_len, dtype=jnp.int32), breadth)
    xgrid = xcoord[None, None, :]
    weight_x = pixel_weight * xgrid
    weight_y = pixel_weight * ycoord
    sum_w = jnp.sum(pixel_weight, axis=(1, 2))
    sum_x = jnp.sum(weight_x, axis=(1, 2))
    sum_y = jnp.sum(weight_y, axis=(1, 2))
    sum_xx = jnp.sum(weight_x * xgrid, axis=(1, 2))
    sum_xy = jnp.sum(weight_x * ycoord, axis=(1, 2))
    sum_yy = jnp.sum(weight_y * ycoord, axis=(1, 2))
    normal = jnp.stack(
        [
            jnp.stack([sum_w, sum_x, sum_y], -1),
            jnp.stack([sum_x, sum_xx, sum_xy], -1),
            jnp.stack([sum_y, sum_xy, sum_yy], -1),
        ],
        1,
    )
    moments = jnp.stack(
        [
            jnp.sum(pixel_weight * difference, axis=(1, 2)),
            jnp.sum(weight_x * difference, axis=(1, 2)),
            jnp.sum(weight_y * difference, axis=(1, 2)),
        ],
        -1,
    )
    packed = jnp.concatenate([normal.reshape(exp_dev, 9), moments], axis=1)
    packed = butterfly_sum(packed, (("row", row_count), ("col", col_count)))
    normal = packed[:, :9].reshape(exp_dev, 3, 3)
    moments = packed[:, 9:]
    plane_fit = solve_three(normal, moments)
    row_coord = centred(row_pos * tile_len + jnp.arange(tile_len, dtype=jnp.int32), height)
    choose = warp_index[:, 0, 0, :]
    ring_order = (
        lax.broadcasted_iota(jnp.int32, (visit_count, visit_count), 0)
        == (visit_pos - lax.broadcasted_iota(jnp.int32, (visit_count, visit_count), 1) - 1)
        % visit_count
    ).astype(jnp.float32)
    picked_ring = jnp.dot(picked.astype(jnp.float32), ring_order, precision=lax.Precision.HIGHEST)
    partial_sum = warp_tiles(
        choose, plane_fit, picked_ring, xcoord.reshape(1, tile_len),
        row_coord.reshape(tile_len, 1), matched, resample_bank,
    )
    numerator = ring_scatter(partial_sum, "visit", visit_count)[None]
    coadd_patch = numerator / denominator[:, None, None]
    return (coadd_patch, plane_fit)


def solution(mesh):
    in_specs = (
        P("visit", "row", "col"),
        P("visit", None),
        P(),
        P("visit", "row", "col"),
        P(),
        P("visit", "row", "col", None),
        P("visit", "row", "col", None),
        P("visit", "row", "col"),
    )
    out_specs = (P("visit", "row", "col"), P("visit", None))
    return jax.shard_map(shards, mesh=mesh, in_specs=in_specs, out_specs=out_specs, check_vma=False)
```

```python
import functools

import jax
import jax.numpy as jnp
import ml_dtypes
import numpy as np
from jax import lax
from jax.sharding import PartitionSpec as P
from jax.experimental import pallas as pl
from jax.experimental.pallas import tpu as pltpu

HALO = 16
STRIP = 32
MAXD = 4


SIGMA_PARTS = (0.0625, 0.125, 0.25)


def extended(value, sides, width):
    for axis, dim in sides:
        devices, length = (lax.axis_size(axis), value.shape[dim])
        last = lax.slice_in_dim(value, length - width, length, axis=dim)
        initial = lax.slice_in_dim(value, 0, width, axis=dim)
        minor = dim == value.ndim - 1
        if minor:
            flat = value.shape[:-2] + (-1,)
            turned = jnp.swapaxes(last, -1, -2).shape
            last = jnp.swapaxes(last, -1, -2).reshape(flat)
            initial = jnp.swapaxes(initial, -1, -2).reshape(flat)
        if devices == 2:
            position = lax.axis_index(axis)
            facing = jnp.where(position == 0, last, initial)
            arrived = lax.ppermute(facing, axis, [(0, 1), (1, 0)])
            empty = jnp.zeros_like(arrived)
            before = jnp.where(position == 1, arrived, empty)
            after = jnp.where(position == 0, arrived, empty)
        else:
            up = [(i, (i + 1) % devices) for i in range(devices - 1)]
            down = [(j, i) for i, j in up]
            before = lax.ppermute(last, axis, up)
            after = lax.ppermute(initial, axis, down)
        if minor:
            before = jnp.swapaxes(before.reshape(turned), -1, -2)
            after = jnp.swapaxes(after.reshape(turned), -1, -2)
        value = jnp.concatenate([before, value, after], axis=dim)
    return value


def toeplitz_block(size, width, sigma):
    spread = (np.arange(2 * width + 1) - width).astype(np.float32)
    scale = np.float32(2.0) * np.float32(sigma) * np.float32(sigma)
    total = np.float32(np.exp(-spread * spread / scale).astype(np.float32).sum(dtype=np.float32))
    offset = (np.arange(size)[None, :] - np.arange(size)[:, None] - width).astype(np.float32)
    values = (np.exp(-offset * offset / scale).astype(np.float32) / total).astype(np.float32)
    values = np.where(np.abs(offset) <= width, values, np.float32(0.0))
    return values.astype(ml_dtypes.bfloat16)


def band_table(length, width, sigma):
    spread = (jnp.arange(2 * width + 1) - width).astype(jnp.float32)
    curve = jnp.exp(-spread * spread / (2.0 * sigma * sigma))
    total = jnp.sum(curve)
    rows_grid = lax.broadcasted_iota(jnp.int32, (length, length + 2 * width), 0)
    cols_grid = lax.broadcasted_iota(jnp.int32, (length, length + 2 * width), 1)
    offset = (cols_grid - rows_grid - width).astype(jnp.float32)
    values = jnp.exp(-offset * offset / (2.0 * sigma * sigma)) / total
    return jnp.where(jnp.abs(offset) <= width, values, 0.0).astype(jnp.bfloat16)


def centred(index, length):
    return (index.astype(jnp.float32) + 0.5) / length * 2.0 - 1.0


def solve_three(normal, moments):
    lower = jnp.linalg.cholesky(normal)
    first = moments[..., 0] / lower[..., 0, 0]
    second = (moments[..., 1] - lower[..., 1, 0] * first) / lower[..., 1, 1]
    third = (moments[..., 2] - lower[..., 2, 0] * first - lower[..., 2, 1] * second) / lower[
        ..., 2, 2
    ]
    upper_top = third / lower[..., 2, 2]
    upper_mid = (second - lower[..., 2, 1] * upper_top) / lower[..., 1, 1]
    upper_low = (first - lower[..., 1, 0] * upper_mid - lower[..., 2, 0] * upper_top) / lower[
        ..., 0, 0
    ]
    return jnp.stack([upper_low, upper_mid, upper_top], -1)


def butterfly_sum(values, axes):
    for axis, size in axes:
        if size & (size - 1) == 0:
            bit = 1
            while bit < size:
                pairs = [(i, i ^ bit) for i in range(size)]
                values = jax.tree.map(lambda v: v + lax.ppermute(v, axis, pairs), values)
                bit *= 2
        else:
            position = lax.axis_index(axis)
            def gathered(v):
                parts = [v]
                for shift in range(1, size):
                    pairs = [(i, (i + shift) % size) for i in range(size)]
                    parts.append(lax.ppermute(v, axis, pairs))
                stacked = jnp.stack(parts, 0)
                order = (position - jnp.arange(size)) % size
                canonical = jnp.zeros_like(stacked).at[order].set(stacked)
                return jnp.sum(canonical, axis=0)
            values = jax.tree.map(gathered, values)
    return values


def conv_body(coef_ref, vt_ref, ht_ref, padded_ref, out_ref):
    e = pl.program_id(0)
    image = padded_ref[0]
    total = None
    for kernel in range(len(SIGMA_PARTS)):
        across = jnp.dot(vt_ref[0, kernel], image, preferred_element_type=jnp.float32)
        smoothed = lax.dot_general(
            across.astype(jnp.bfloat16), ht_ref[kernel], (((1,), (1,)), ((), ())),
            preferred_element_type=jnp.float32,
        )
        term = coef_ref[e, kernel] * smoothed
        total = term if total is None else total + term
    out_ref[0] = total


def conv_tiles(coeffs, vtables, htables, padded, per_exposure):
    exp_dev, wide = padded.shape[0], padded.shape[1]
    nk, out_rows = vtables.shape[-3], vtables.shape[-2]
    tile_len = htables.shape[1]
    if per_exposure:
        vspec = pl.BlockSpec((1, nk, out_rows, wide), lambda e: (e, 0, 0, 0))
    else:
        vtables = vtables[None]
        vspec = pl.BlockSpec((1, nk, out_rows, wide), lambda e: (0, 0, 0, 0))
    flops = exp_dev * nk * 2 * out_rows * wide * (wide + tile_len)
    moved = exp_dev * wide * wide * 2 + exp_dev * out_rows * tile_len * 4
    return pl.pallas_call(
        conv_body,
        grid=(exp_dev,),
        in_specs=[
            pl.BlockSpec(memory_space=pltpu.SMEM),
            vspec,
            pl.BlockSpec((nk, tile_len, wide), lambda e: (0, 0, 0)),
            pl.BlockSpec((1, wide, wide), lambda e: (e, 0, 0)),
        ],
        out_specs=pl.BlockSpec((1, out_rows, tile_len), lambda e: (e, 0, 0)),
        out_shape=jax.ShapeDtypeStruct((exp_dev, out_rows, tile_len), jnp.float32),
        compiler_params=pltpu.CompilerParams(
            dimension_semantics=("arbitrary",), vmem_limit_bytes=48 * 1024 * 1024
        ),
        cost_estimate=pl.CostEstimate(flops=flops, bytes_accessed=moved, transcendentals=0),
    )(coeffs, vtables, htables, padded)


BLOCK = 128


def strip_body(off_ref, coef_ref, tb_ref, padded_ref, out_ref):
    e = pl.program_id(0)
    rows, tile_len = out_ref.shape[1], out_ref.shape[2]
    wide = padded_ref.shape[1]
    windows = [(start, min(2 * BLOCK, wide - start)) for start in range(0, tile_len, BLOCK)]
    anchor = off_ref[e]
    base = jnp.minimum((anchor // BLOCK) * BLOCK, wide - 2 * BLOCK)
    shift = anchor - base
    window = padded_ref[0, pl.ds(pl.multiple_of(base, 16), 2 * BLOCK), :]
    pick = (
        lax.broadcasted_iota(jnp.int32, (rows, 2 * BLOCK), 1)
        == lax.broadcasted_iota(jnp.int32, (rows, 2 * BLOCK), 0) + shift
    ).astype(jnp.bfloat16)
    total = None
    for kernel in range(len(SIGMA_PARTS)):
        table = tb_ref[kernel]
        strip_rows = jnp.dot(pick, table, preferred_element_type=jnp.float32).astype(jnp.bfloat16)
        across = jnp.dot(strip_rows, window, preferred_element_type=jnp.float32)
        across = across.astype(jnp.bfloat16)
        block = table[:BLOCK]
        cols = [
            lax.dot_general(
                across[:, start:start + reach], block[:, :reach], (((1,), (1,)), ((), ())),
                preferred_element_type=jnp.float32,
            )
            for start, reach in windows
        ]
        term = coef_ref[e, kernel] * jnp.concatenate(cols, 1)
        total = term if total is None else total + term
    out_ref[0] = total


def strip_tiles(offset, coeffs, tb, padded, tile_len):
    exp_dev, wide = padded.shape[0], padded.shape[1]
    nk = tb.shape[0]
    grid_spec = pltpu.PrefetchScalarGridSpec(
        num_scalar_prefetch=1,
        grid=(exp_dev,),
        in_specs=[
            pl.BlockSpec(memory_space=pltpu.SMEM),
            pl.BlockSpec((nk, 2 * BLOCK, 2 * BLOCK), lambda e, off: (0, 0, 0)),
            pl.BlockSpec((1, wide, wide), lambda e, off: (e, 0, 0)),
        ],
        out_specs=pl.BlockSpec((1, STRIP, tile_len), lambda e, off: (e, 0, 0)),
    )
    flops = exp_dev * nk * 2 * STRIP * 2 * BLOCK * (2 * BLOCK + wide + tile_len)
    moved = exp_dev * wide * wide * 2 + exp_dev * STRIP * tile_len * 4
    return pl.pallas_call(
        strip_body,
        grid_spec=grid_spec,
        out_shape=jax.ShapeDtypeStruct((exp_dev, STRIP, tile_len), jnp.float32),
        compiler_params=pltpu.CompilerParams(
            dimension_semantics=("arbitrary",), vmem_limit_bytes=48 * 1024 * 1024
        ),
        cost_estimate=pl.CostEstimate(flops=flops, bytes_accessed=moved, transcendentals=0),
    )(offset, coeffs, tb, padded)


def band_body(first, coef_ref, blk_ref, padded_ref, *rest):
    out_ref = rest[-1]
    e = pl.program_id(0) + first
    tile_len = out_ref.shape[1]
    wide = padded_ref.shape[1]
    windows = [(start, min(2 * BLOCK, wide - start)) for start in range(0, tile_len, BLOCK)]
    total = None
    for kernel in range(len(SIGMA_PARTS)):
        block = blk_ref[kernel][:BLOCK]
        rows = [
            jnp.dot(
                block[:, :reach], padded_ref[0, start:start + reach, :],
                preferred_element_type=jnp.float32,
            )
            for start, reach in windows
        ]
        across = jnp.concatenate(rows, 0).astype(jnp.bfloat16)
        cols = [
            lax.dot_general(
                across[:, start:start + reach], block[:, :reach], (((1,), (1,)), ((), ())),
                preferred_element_type=jnp.float32,
            )
            for start, reach in windows
        ]
        term = coef_ref[e, kernel] * jnp.concatenate(cols, 1)
        total = term if total is None else total + term
    out_ref[0] = total


def band_tiles(coeffs, blocks, padded, tile_len, first, count, into):
    exp_dev, wide = padded.shape[0], padded.shape[1]
    nk = blocks.shape[0]
    steps = tile_len // BLOCK
    flops = count * nk * steps * 2 * BLOCK * 2 * BLOCK * (wide + tile_len)
    moved = count * wide * wide * 2 + count * tile_len * tile_len * 4
    in_specs = [
        pl.BlockSpec(memory_space=pltpu.SMEM),
        pl.BlockSpec((nk, 2 * BLOCK, 2 * BLOCK), lambda e: (0, 0, 0)),
        pl.BlockSpec((1, wide, wide), lambda e: (e + first, 0, 0)),
    ]
    operands = [coeffs, blocks, padded]
    aliases = {}
    if into is not None:
        in_specs.append(pl.BlockSpec(memory_space=pl.ANY))
        operands.append(into)
        aliases = {3: 0}
    return pl.pallas_call(
        functools.partial(band_body, first),
        grid=(count,),
        in_specs=in_specs,
        out_specs=pl.BlockSpec((1, tile_len, tile_len), lambda e: (e + first, 0, 0)),
        out_shape=jax.ShapeDtypeStruct((exp_dev, tile_len, tile_len), jnp.float32),
        input_output_aliases=aliases,
        compiler_params=pltpu.CompilerParams(
            dimension_semantics=("arbitrary",), vmem_limit_bytes=48 * 1024 * 1024
        ),
        cost_estimate=pl.CostEstimate(flops=flops, bytes_accessed=moved, transcendentals=0),
    )(*operands)


def warp_body(idx_ref, plane_ref, pick_ref, xrow_ref, ycol_ref, matched_ref, rmap_ref, cmap_ref,
              out_ref, acc_ref):
    e = pl.program_id(0)
    background = (
        plane_ref[e, 0] + plane_ref[e, 1] * xrow_ref[...]
    ) + plane_ref[e, 2] * ycol_ref[...]
    corrected = (matched_ref[0] - background).astype(jnp.bfloat16)
    halfway = jnp.dot(rmap_ref[0], corrected, preferred_element_type=jnp.float32)
    warped = lax.dot_general(
        halfway.astype(jnp.bfloat16), cmap_ref[0], (((1,), (1,)), ((), ())),
        preferred_element_type=jnp.float32,
    )
    warped = warped.astype(jnp.bfloat16).astype(jnp.float32)
    patches = acc_ref.shape[0]

    @pl.when(e == 0)
    def _():
        for v in range(patches):
            acc_ref[v] = pick_ref[e, v] * warped

    @pl.when(e > 0)
    def _():
        for v in range(patches):
            acc_ref[v] = acc_ref[v] + pick_ref[e, v] * warped

    @pl.when(e == pl.num_programs(0) - 1)
    def _():
        out_ref[...] = acc_ref[...].astype(jnp.bfloat16)


def warp_tiles(choose, plane, picked, xrow, ycol, matched, bank, part, pieces):
    exp_dev, tile_len = matched.shape[0], matched.shape[1]
    patches = picked.shape[1]
    rows = tile_len // pieces
    grid_spec = pltpu.PrefetchScalarGridSpec(
        num_scalar_prefetch=1,
        grid=(exp_dev,),
        in_specs=[
            pl.BlockSpec(memory_space=pltpu.SMEM),
            pl.BlockSpec(memory_space=pltpu.SMEM),
            pl.BlockSpec((1, tile_len), lambda e, idx: (0, 0)),
            pl.BlockSpec((tile_len, 1), lambda e, idx: (0, 0)),
            pl.BlockSpec((1, tile_len, tile_len), lambda e, idx: (e, 0, 0)),
            pl.BlockSpec((1, rows, tile_len), lambda e, idx: (idx[e, 0], part, 0)),
            pl.BlockSpec((1, tile_len, tile_len), lambda e, idx: (idx[e, 1], 0, 0)),
        ],
        out_specs=pl.BlockSpec((patches, rows, tile_len), lambda e, idx: (0, 0, 0)),
        scratch_shapes=[pltpu.VMEM((patches, rows, tile_len), jnp.float32)],
    )
    flops = exp_dev * 4 * rows * tile_len * tile_len
    moved = exp_dev * tile_len * tile_len * (4 + 2) + exp_dev * rows * tile_len * 2
    moved = moved + patches * rows * tile_len * 2
    vmem = 60 * 1024 * 1024
    return pl.pallas_call(
        warp_body,
        grid_spec=grid_spec,
        out_shape=jax.ShapeDtypeStruct((patches, rows, tile_len), jnp.bfloat16),
        compiler_params=pltpu.CompilerParams(
            dimension_semantics=("arbitrary",), vmem_limit_bytes=vmem
        ),
        cost_estimate=pl.CostEstimate(flops=flops, bytes_accessed=moved, transcendentals=0),
    )(choose, plane, picked, xrow, ycol, matched, bank, bank)


def ring_scatter(parts, axis, size):
    ring = [(i, (i + 1) % size) for i in range(size)]
    travelling = None
    for step in range(size - 1):
        own = parts[step].astype(jnp.float32)
        outgoing = own if travelling is None else travelling + own
        travelling = lax.ppermute(outgoing.astype(jnp.bfloat16), axis, ring).astype(jnp.float32)
    own = parts[size - 1].astype(jnp.float32)
    return own if travelling is None else travelling + own


def rows_from(source, anchor):
    return lax.dynamic_slice_in_dim(source, anchor, STRIP, 0)


def shards(images, coeffs, pair_list, weights, resample_bank, warp_index, destinations, counts):
    exp_dev = images.shape[0]
    tile_len = images.shape[1]
    row_count = lax.axis_size("row")
    col_count = lax.axis_size("col")
    visit_count = lax.axis_size("visit")
    row_pos = lax.axis_index("row")
    col_pos = lax.axis_index("col")
    visit_pos = lax.axis_index("visit")
    height = row_count * tile_len
    breadth = col_count * tile_len
    padded = extended(images, (("col", 2), ("row", 1)), HALO)
    own_ids = visit_pos * exp_dev + jnp.arange(exp_dev, dtype=jnp.int32)
    first_col = pair_list[:, 0]
    second_col = pair_list[:, 1]
    offsets = pair_list[:, 2]
    hit_first = first_col[None, :] == own_ids[:, None]
    hit_second = second_col[None, :] == own_ids[:, None]
    partner = jnp.sum(
        jnp.where(hit_first, second_col[None, :], 0) + jnp.where(hit_second, first_col[None, :], 0),
        axis=1,
    )
    offset = jnp.sum(jnp.where(hit_first | hit_second, offsets[None, :], 0), axis=1)
    pick_rows = (
        lax.broadcasted_iota(jnp.int32, (exp_dev, STRIP, tile_len), 2)
        == offset[:, None, None] + lax.broadcasted_iota(jnp.int32, (exp_dev, STRIP, tile_len), 1)
    ).astype(jnp.bfloat16)
    own_strip = jnp.einsum(
        "esr,erl->esl", pick_rows, images, preferred_element_type=jnp.float32
    ).astype(jnp.bfloat16)
    listed = destinations[:, 0, 0, :]
    how_many = counts[:, 0, 0]
    usable = jnp.arange(MAXD, dtype=jnp.int32)[None, :] < how_many[:, None]
    owners = jnp.arange(visit_count, dtype=jnp.int32)
    member = jnp.any(usable[:, :, None] & (listed[:, :, None] == owners[None, None, :]), axis=1)
    tile_weight = weights[:, 0, 0]
    nothing = jnp.zeros((), jnp.bfloat16)
    picked = jnp.where(member, tile_weight[:, None], nothing)
    strip_rows_n = exp_dev * STRIP
    extra = -(-(exp_dev * visit_count) // tile_len)
    extra = -(-extra // 16) * 16
    tail = jnp.zeros((extra * tile_len,), jnp.bfloat16)
    tail = tail.at[: exp_dev * visit_count].set(picked.reshape(-1)).reshape(extra, tile_len)
    payload = jnp.concatenate([own_strip.reshape(strip_rows_n, tile_len), tail], axis=0)
    received = [payload]
    for shift in range(1, visit_count):
        pairs = [(i, (i + shift) % visit_count) for i in range(visit_count)]
        received.append(lax.ppermute(payload, "visit", pairs))
    stacked = jnp.stack(received, 0)
    strips_all = stacked[:, :strip_rows_n].reshape(visit_count * exp_dev, STRIP, tile_len)
    picked_all = stacked[:, strip_rows_n:].reshape(visit_count, -1)[:, : exp_dev * visit_count]
    picked_all = picked_all.reshape(visit_count, exp_dev, visit_count)
    partner_visit = partner // exp_dev
    slot = (visit_pos - partner_visit) % visit_count
    source = slot * exp_dev + partner % exp_dev
    choose_strip = (
        lax.broadcasted_iota(jnp.int32, (exp_dev, visit_count * exp_dev), 1) == source[:, None]
    ).astype(jnp.bfloat16)
    theirs = jnp.einsum(
        "ej,jsl->esl", choose_strip, strips_all, preferred_element_type=jnp.float32
    )
    own_patch = jnp.take(picked_all, visit_pos, axis=2).astype(jnp.float32)
    denominator = jnp.sum(own_patch).reshape(1)
    roomy = padded
    blocks = jnp.asarray(
        np.stack([toeplitz_block(2 * BLOCK, HALO, HALO * part) for part in SIGMA_PARTS])
    )
    nearby = strip_tiles(offset, coeffs, blocks, roomy, tile_len)
    half = exp_dev // 2
    matched = band_tiles(coeffs, blocks, roomy, tile_len, 0, half, None)
    matched = band_tiles(coeffs, blocks, roomy, tile_len, half, exp_dev - half, matched)
    difference = nearby - theirs
    pixel_weight = 1.0 / (1.0 + theirs * theirs)
    strip_rows = row_pos * tile_len + offset[:, None] + jnp.arange(STRIP, dtype=jnp.int32)[None, :]
    ycoord = centred(strip_rows, height)[:, :, None]
    xcoord = centred(col_pos * tile_len + jnp.arange(tile_len, dtype=jnp.int32), breadth)
    xgrid = xcoord[None, None, :]
    weight_x = pixel_weight * xgrid
    weight_y = pixel_weight * ycoord
    sum_w = jnp.sum(pixel_weight, axis=(1, 2))
    sum_x = jnp.sum(weight_x, axis=(1, 2))
    sum_y = jnp.sum(weight_y, axis=(1, 2))
    sum_xx = jnp.sum(weight_x * xgrid, axis=(1, 2))
    sum_xy = jnp.sum(weight_x * ycoord, axis=(1, 2))
    sum_yy = jnp.sum(weight_y * ycoord, axis=(1, 2))
    normal = jnp.stack(
        [
            jnp.stack([sum_w, sum_x, sum_y], -1),
            jnp.stack([sum_x, sum_xx, sum_xy], -1),
            jnp.stack([sum_y, sum_xy, sum_yy], -1),
        ],
        1,
    )
    moments = jnp.stack(
        [
            jnp.sum(pixel_weight * difference, axis=(1, 2)),
            jnp.sum(weight_x * difference, axis=(1, 2)),
            jnp.sum(weight_y * difference, axis=(1, 2)),
        ],
        -1,
    )
    packed = jnp.concatenate([normal.reshape(exp_dev, 9), moments], axis=1)
    packed = butterfly_sum(packed, (("row", row_count), ("col", col_count)))
    normal = packed[:, :9].reshape(exp_dev, 3, 3)
    moments = packed[:, 9:]
    plane_fit = solve_three(normal, moments)
    row_coord = centred(row_pos * tile_len + jnp.arange(tile_len, dtype=jnp.int32), height)
    choose = warp_index[:, 0, 0, :]
    ring_order = (
        lax.broadcasted_iota(jnp.int32, (visit_count, visit_count), 0)
        == (visit_pos - lax.broadcasted_iota(jnp.int32, (visit_count, visit_count), 1) - 1)
        % visit_count
    ).astype(jnp.float32)
    picked_ring = jnp.dot(picked.astype(jnp.float32), ring_order, precision=lax.Precision.HIGHEST)
    halves = [warp_tiles(
        choose, plane_fit, picked_ring, xcoord.reshape(1, tile_len),
        row_coord.reshape(tile_len, 1), matched, resample_bank, part, 2) for part in range(2)]
    numerator = jnp.concatenate(
        [ring_scatter(piece, "visit", visit_count) for piece in halves], 0
    )[None]
    coadd_patch = numerator / denominator[:, None, None]
    return (coadd_patch, plane_fit)


def solution(mesh):
    in_specs = (
        P("visit", "row", "col"),
        P("visit", None),
        P(),
        P("visit", "row", "col"),
        P(),
        P("visit", "row", "col", None),
        P("visit", "row", "col", None),
        P("visit", "row", "col"),
    )
    out_specs = (P("visit", "row", "col"), P("visit", None))
    return jax.shard_map(shards, mesh=mesh, in_specs=in_specs, out_specs=out_specs, check_vma=False)
```

```python
import functools

import jax
import jax.numpy as jnp
import ml_dtypes
import numpy as np
from jax import lax
from jax.sharding import PartitionSpec as P
from jax.experimental import pallas as pl
from jax.experimental.pallas import tpu as pltpu

HALO = 16
STRIP = 32
MAXD = 4


SIGMA_PARTS = (0.0625, 0.125, 0.25)


def extended(value, sides, width):
    for axis, dim in sides:
        devices, length = (lax.axis_size(axis), value.shape[dim])
        last = lax.slice_in_dim(value, length - width, length, axis=dim)
        initial = lax.slice_in_dim(value, 0, width, axis=dim)
        minor = dim == value.ndim - 1
        if minor:
            flat = value.shape[:-2] + (-1,)
            turned = jnp.swapaxes(last, -1, -2).shape
            last = jnp.swapaxes(last, -1, -2).reshape(flat)
            initial = jnp.swapaxes(initial, -1, -2).reshape(flat)
        if devices == 2:
            position = lax.axis_index(axis)
            facing = jnp.where(position == 0, last, initial)
            arrived = lax.ppermute(facing, axis, [(0, 1), (1, 0)])
            empty = jnp.zeros_like(arrived)
            before = jnp.where(position == 1, arrived, empty)
            after = jnp.where(position == 0, arrived, empty)
        else:
            up = [(i, (i + 1) % devices) for i in range(devices - 1)]
            down = [(j, i) for i, j in up]
            before = lax.ppermute(last, axis, up)
            after = lax.ppermute(initial, axis, down)
        if minor:
            before = jnp.swapaxes(before.reshape(turned), -1, -2)
            after = jnp.swapaxes(after.reshape(turned), -1, -2)
        value = jnp.concatenate([before, value, after], axis=dim)
    return value


def toeplitz_block(size, width, sigma):
    spread = (np.arange(2 * width + 1) - width).astype(np.float32)
    scale = np.float32(2.0) * np.float32(sigma) * np.float32(sigma)
    total = np.float32(np.exp(-spread * spread / scale).astype(np.float32).sum(dtype=np.float32))
    offset = (np.arange(size)[None, :] - np.arange(size)[:, None] - width).astype(np.float32)
    values = (np.exp(-offset * offset / scale).astype(np.float32) / total).astype(np.float32)
    values = np.where(np.abs(offset) <= width, values, np.float32(0.0))
    return values.astype(ml_dtypes.bfloat16)


def band_table(length, width, sigma):
    spread = (jnp.arange(2 * width + 1) - width).astype(jnp.float32)
    curve = jnp.exp(-spread * spread / (2.0 * sigma * sigma))
    total = jnp.sum(curve)
    rows_grid = lax.broadcasted_iota(jnp.int32, (length, length + 2 * width), 0)
    cols_grid = lax.broadcasted_iota(jnp.int32, (length, length + 2 * width), 1)
    offset = (cols_grid - rows_grid - width).astype(jnp.float32)
    values = jnp.exp(-offset * offset / (2.0 * sigma * sigma)) / total
    return jnp.where(jnp.abs(offset) <= width, values, 0.0).astype(jnp.bfloat16)


def centred(index, length):
    return (index.astype(jnp.float32) + 0.5) / length * 2.0 - 1.0


def solve_three(normal, moments):
    lower = jnp.linalg.cholesky(normal)
    first = moments[..., 0] / lower[..., 0, 0]
    second = (moments[..., 1] - lower[..., 1, 0] * first) / lower[..., 1, 1]
    third = (moments[..., 2] - lower[..., 2, 0] * first - lower[..., 2, 1] * second) / lower[
        ..., 2, 2
    ]
    upper_top = third / lower[..., 2, 2]
    upper_mid = (second - lower[..., 2, 1] * upper_top) / lower[..., 1, 1]
    upper_low = (first - lower[..., 1, 0] * upper_mid - lower[..., 2, 0] * upper_top) / lower[
        ..., 0, 0
    ]
    return jnp.stack([upper_low, upper_mid, upper_top], -1)


def butterfly_sum(values, axes):
    for axis, size in axes:
        if size & (size - 1) == 0:
            bit = 1
            while bit < size:
                pairs = [(i, i ^ bit) for i in range(size)]
                values = jax.tree.map(lambda v: v + lax.ppermute(v, axis, pairs), values)
                bit *= 2
        else:
            position = lax.axis_index(axis)
            def gathered(v):
                parts = [v]
                for shift in range(1, size):
                    pairs = [(i, (i + shift) % size) for i in range(size)]
                    parts.append(lax.ppermute(v, axis, pairs))
                stacked = jnp.stack(parts, 0)
                order = (position - jnp.arange(size)) % size
                canonical = jnp.zeros_like(stacked).at[order].set(stacked)
                return jnp.sum(canonical, axis=0)
            values = jax.tree.map(gathered, values)
    return values


def conv_body(coef_ref, vt_ref, ht_ref, padded_ref, out_ref):
    e = pl.program_id(0)
    image = padded_ref[0]
    total = None
    for kernel in range(len(SIGMA_PARTS)):
        across = jnp.dot(vt_ref[0, kernel], image, preferred_element_type=jnp.float32)
        smoothed = lax.dot_general(
            across.astype(jnp.bfloat16), ht_ref[kernel], (((1,), (1,)), ((), ())),
            preferred_element_type=jnp.float32,
        )
        term = coef_ref[e, kernel] * smoothed
        total = term if total is None else total + term
    out_ref[0] = total


def conv_tiles(coeffs, vtables, htables, padded, per_exposure):
    exp_dev, wide = padded.shape[0], padded.shape[1]
    nk, out_rows = vtables.shape[-3], vtables.shape[-2]
    tile_len = htables.shape[1]
    if per_exposure:
        vspec = pl.BlockSpec((1, nk, out_rows, wide), lambda e: (e, 0, 0, 0))
    else:
        vtables = vtables[None]
        vspec = pl.BlockSpec((1, nk, out_rows, wide), lambda e: (0, 0, 0, 0))
    flops = exp_dev * nk * 2 * out_rows * wide * (wide + tile_len)
    moved = exp_dev * wide * wide * 2 + exp_dev * out_rows * tile_len * 4
    return pl.pallas_call(
        conv_body,
        grid=(exp_dev,),
        in_specs=[
            pl.BlockSpec(memory_space=pltpu.SMEM),
            vspec,
            pl.BlockSpec((nk, tile_len, wide), lambda e: (0, 0, 0)),
            pl.BlockSpec((1, wide, wide), lambda e: (e, 0, 0)),
        ],
        out_specs=pl.BlockSpec((1, out_rows, tile_len), lambda e: (e, 0, 0)),
        out_shape=jax.ShapeDtypeStruct((exp_dev, out_rows, tile_len), jnp.float32),
        compiler_params=pltpu.CompilerParams(
            dimension_semantics=("arbitrary",), vmem_limit_bytes=48 * 1024 * 1024
        ),
        cost_estimate=pl.CostEstimate(flops=flops, bytes_accessed=moved, transcendentals=0),
    )(coeffs, vtables, htables, padded)


BLOCK = 128


def strip_body(off_ref, coef_ref, tb_ref, padded_ref, out_ref):
    e = pl.program_id(0)
    rows, tile_len = out_ref.shape[1], out_ref.shape[2]
    wide = padded_ref.shape[1]
    windows = [(start, min(2 * BLOCK, wide - start)) for start in range(0, tile_len, BLOCK)]
    anchor = off_ref[e]
    base = jnp.minimum((anchor // BLOCK) * BLOCK, wide - 2 * BLOCK)
    shift = anchor - base
    window = padded_ref[0, pl.ds(pl.multiple_of(base, 16), 2 * BLOCK), :]
    pick = (
        lax.broadcasted_iota(jnp.int32, (rows, 2 * BLOCK), 1)
        == lax.broadcasted_iota(jnp.int32, (rows, 2 * BLOCK), 0) + shift
    ).astype(jnp.bfloat16)
    total = None
    for kernel in range(len(SIGMA_PARTS)):
        table = tb_ref[kernel]
        strip_rows = jnp.dot(pick, table, preferred_element_type=jnp.float32).astype(jnp.bfloat16)
        across = jnp.dot(strip_rows, window, preferred_element_type=jnp.float32)
        across = across.astype(jnp.bfloat16)
        block = table[:BLOCK]
        cols = [
            lax.dot_general(
                across[:, start:start + reach], block[:, :reach], (((1,), (1,)), ((), ())),
                preferred_element_type=jnp.float32,
            )
            for start, reach in windows
        ]
        term = coef_ref[e, kernel] * jnp.concatenate(cols, 1)
        total = term if total is None else total + term
    out_ref[0] = total


def strip_tiles(offset, coeffs, tb, padded, tile_len):
    exp_dev, wide = padded.shape[0], padded.shape[1]
    nk = tb.shape[0]
    grid_spec = pltpu.PrefetchScalarGridSpec(
        num_scalar_prefetch=1,
        grid=(exp_dev,),
        in_specs=[
            pl.BlockSpec(memory_space=pltpu.SMEM),
            pl.BlockSpec((nk, 2 * BLOCK, 2 * BLOCK), lambda e, off: (0, 0, 0)),
            pl.BlockSpec((1, wide, wide), lambda e, off: (e, 0, 0)),
        ],
        out_specs=pl.BlockSpec((1, STRIP, tile_len), lambda e, off: (e, 0, 0)),
    )
    flops = exp_dev * nk * 2 * STRIP * 2 * BLOCK * (2 * BLOCK + wide + tile_len)
    moved = exp_dev * wide * wide * 2 + exp_dev * STRIP * tile_len * 4
    return pl.pallas_call(
        strip_body,
        grid_spec=grid_spec,
        out_shape=jax.ShapeDtypeStruct((exp_dev, STRIP, tile_len), jnp.float32),
        compiler_params=pltpu.CompilerParams(
            dimension_semantics=("arbitrary",), vmem_limit_bytes=48 * 1024 * 1024
        ),
        cost_estimate=pl.CostEstimate(flops=flops, bytes_accessed=moved, transcendentals=0),
    )(offset, coeffs, tb, padded)


def band_body(first, coef_ref, blk_ref, padded_ref, *rest):
    out_ref = rest[-1]
    e = pl.program_id(0) + first
    tile_len = out_ref.shape[1]
    wide = padded_ref.shape[1]
    windows = [(start, min(2 * BLOCK, wide - start)) for start in range(0, tile_len, BLOCK)]
    total = None
    for kernel in range(len(SIGMA_PARTS)):
        block = blk_ref[kernel][:BLOCK]
        rows = [
            jnp.dot(
                block[:, :reach], padded_ref[0, start:start + reach, :],
                preferred_element_type=jnp.float32,
            )
            for start, reach in windows
        ]
        across = jnp.concatenate(rows, 0).astype(jnp.bfloat16)
        cols = [
            lax.dot_general(
                across[:, start:start + reach], block[:, :reach], (((1,), (1,)), ((), ())),
                preferred_element_type=jnp.float32,
            )
            for start, reach in windows
        ]
        term = coef_ref[e, kernel] * jnp.concatenate(cols, 1)
        total = term if total is None else total + term
    out_ref[0] = total


def band_tiles(coeffs, blocks, padded, tile_len, first, count, into):
    exp_dev, wide = padded.shape[0], padded.shape[1]
    nk = blocks.shape[0]
    steps = tile_len // BLOCK
    flops = count * nk * steps * 2 * BLOCK * 2 * BLOCK * (wide + tile_len)
    moved = count * wide * wide * 2 + count * tile_len * tile_len * 4
    in_specs = [
        pl.BlockSpec(memory_space=pltpu.SMEM),
        pl.BlockSpec((nk, 2 * BLOCK, 2 * BLOCK), lambda e: (0, 0, 0)),
        pl.BlockSpec((1, wide, wide), lambda e: (e + first, 0, 0)),
    ]
    operands = [coeffs, blocks, padded]
    aliases = {}
    if into is not None:
        in_specs.append(pl.BlockSpec(memory_space=pl.ANY))
        operands.append(into)
        aliases = {3: 0}
    return pl.pallas_call(
        functools.partial(band_body, first),
        grid=(count,),
        in_specs=in_specs,
        out_specs=pl.BlockSpec((1, tile_len, tile_len), lambda e: (e + first, 0, 0)),
        out_shape=jax.ShapeDtypeStruct((exp_dev, tile_len, tile_len), jnp.float32),
        input_output_aliases=aliases,
        compiler_params=pltpu.CompilerParams(
            dimension_semantics=("arbitrary",), vmem_limit_bytes=48 * 1024 * 1024
        ),
        cost_estimate=pl.CostEstimate(flops=flops, bytes_accessed=moved, transcendentals=0),
    )(*operands)


def warp_body(idx_ref, plane_ref, pick_ref, xrow_ref, ycol_ref, matched_ref, rmap_ref, cmap_ref,
              out_ref, acc_ref):
    e = pl.program_id(0)
    background = (
        plane_ref[e, 0] + plane_ref[e, 1] * xrow_ref[...]
    ) + plane_ref[e, 2] * ycol_ref[...]
    corrected = (matched_ref[0] - background).astype(jnp.bfloat16)
    halfway = jnp.dot(rmap_ref[0], corrected, preferred_element_type=jnp.float32)
    warped = lax.dot_general(
        halfway.astype(jnp.bfloat16), cmap_ref[0], (((1,), (1,)), ((), ())),
        preferred_element_type=jnp.float32,
    )
    warped = warped.astype(jnp.bfloat16).astype(jnp.float32)
    patches = acc_ref.shape[0]

    @pl.when(e == 0)
    def _():
        for v in range(patches):
            acc_ref[v] = pick_ref[e, v] * warped

    @pl.when(e > 0)
    def _():
        for v in range(patches):
            acc_ref[v] = acc_ref[v] + pick_ref[e, v] * warped

    @pl.when(e == pl.num_programs(0) - 1)
    def _():
        out_ref[...] = acc_ref[...].astype(jnp.bfloat16)


def warp_tiles(choose, plane, picked, xrow, ycol, matched, bank, part, pieces):
    exp_dev, tile_len = matched.shape[0], matched.shape[1]
    patches = picked.shape[1]
    rows = tile_len // pieces
    grid_spec = pltpu.PrefetchScalarGridSpec(
        num_scalar_prefetch=1,
        grid=(exp_dev,),
        in_specs=[
            pl.BlockSpec(memory_space=pltpu.SMEM),
            pl.BlockSpec(memory_space=pltpu.SMEM),
            pl.BlockSpec((1, tile_len), lambda e, idx: (0, 0)),
            pl.BlockSpec((tile_len, 1), lambda e, idx: (0, 0)),
            pl.BlockSpec((1, tile_len, tile_len), lambda e, idx: (e, 0, 0)),
            pl.BlockSpec((1, rows, tile_len), lambda e, idx: (idx[e, 0], part, 0)),
            pl.BlockSpec((1, tile_len, tile_len), lambda e, idx: (idx[e, 1], 0, 0)),
        ],
        out_specs=pl.BlockSpec((patches, rows, tile_len), lambda e, idx: (0, 0, 0)),
        scratch_shapes=[pltpu.VMEM((patches, rows, tile_len), jnp.float32)],
    )
    flops = exp_dev * 4 * rows * tile_len * tile_len
    moved = exp_dev * tile_len * tile_len * (4 + 2) + exp_dev * rows * tile_len * 2
    moved = moved + patches * rows * tile_len * 2
    vmem = 60 * 1024 * 1024
    return pl.pallas_call(
        warp_body,
        grid_spec=grid_spec,
        out_shape=jax.ShapeDtypeStruct((patches, rows, tile_len), jnp.bfloat16),
        compiler_params=pltpu.CompilerParams(
            dimension_semantics=("arbitrary",), vmem_limit_bytes=vmem
        ),
        cost_estimate=pl.CostEstimate(flops=flops, bytes_accessed=moved, transcendentals=0),
    )(choose, plane, picked, xrow, ycol, matched, bank, bank)


def ring_scatter(parts, axis, size):
    ring = [(i, (i + 1) % size) for i in range(size)]
    travelling = None
    for step in range(size - 1):
        own = parts[step].astype(jnp.float32)
        outgoing = own if travelling is None else travelling + own
        travelling = lax.ppermute(outgoing.astype(jnp.bfloat16), axis, ring).astype(jnp.float32)
    own = parts[size - 1].astype(jnp.float32)
    return own if travelling is None else travelling + own


def rows_from(source, anchor):
    return lax.dynamic_slice_in_dim(source, anchor, STRIP, 0)


def shards(images, coeffs, pair_list, weights, resample_bank, warp_index, destinations, counts):
    exp_dev = images.shape[0]
    tile_len = images.shape[1]
    row_count = lax.axis_size("row")
    col_count = lax.axis_size("col")
    visit_count = lax.axis_size("visit")
    row_pos = lax.axis_index("row")
    col_pos = lax.axis_index("col")
    visit_pos = lax.axis_index("visit")
    height = row_count * tile_len
    breadth = col_count * tile_len
    padded = extended(images, (("col", 2), ("row", 1)), HALO)
    own_ids = visit_pos * exp_dev + jnp.arange(exp_dev, dtype=jnp.int32)
    first_col = pair_list[:, 0]
    second_col = pair_list[:, 1]
    offsets = pair_list[:, 2]
    hit_first = first_col[None, :] == own_ids[:, None]
    hit_second = second_col[None, :] == own_ids[:, None]
    partner = jnp.sum(
        jnp.where(hit_first, second_col[None, :], 0) + jnp.where(hit_second, first_col[None, :], 0),
        axis=1,
    )
    offset = jnp.sum(jnp.where(hit_first | hit_second, offsets[None, :], 0), axis=1)
    pick_rows = (
        lax.broadcasted_iota(jnp.int32, (exp_dev, STRIP, tile_len), 2)
        == offset[:, None, None] + lax.broadcasted_iota(jnp.int32, (exp_dev, STRIP, tile_len), 1)
    ).astype(jnp.bfloat16)
    own_strip = jnp.einsum(
        "esr,erl->esl", pick_rows, images, preferred_element_type=jnp.float32
    ).astype(jnp.bfloat16)
    listed = destinations[:, 0, 0, :]
    how_many = counts[:, 0, 0]
    usable = jnp.arange(MAXD, dtype=jnp.int32)[None, :] < how_many[:, None]
    owners = jnp.arange(visit_count, dtype=jnp.int32)
    member = jnp.any(usable[:, :, None] & (listed[:, :, None] == owners[None, None, :]), axis=1)
    tile_weight = weights[:, 0, 0]
    nothing = jnp.zeros((), jnp.bfloat16)
    picked = jnp.where(member, tile_weight[:, None], nothing)
    strip_rows_n = exp_dev * STRIP
    extra = -(-(exp_dev * visit_count) // tile_len)
    extra = -(-extra // 16) * 16
    tail = jnp.zeros((extra * tile_len,), jnp.bfloat16)
    tail = tail.at[: exp_dev * visit_count].set(picked.reshape(-1)).reshape(extra, tile_len)
    payload = jnp.concatenate([own_strip.reshape(strip_rows_n, tile_len), tail], axis=0)
    received = [payload]
    for shift in range(1, visit_count):
        pairs = [(i, (i + shift) % visit_count) for i in range(visit_count)]
        received.append(lax.ppermute(payload, "visit", pairs))
    stacked = jnp.stack(received, 0)
    strips_all = stacked[:, :strip_rows_n].reshape(visit_count * exp_dev, STRIP, tile_len)
    picked_all = stacked[:, strip_rows_n:].reshape(visit_count, -1)[:, : exp_dev * visit_count]
    picked_all = picked_all.reshape(visit_count, exp_dev, visit_count)
    partner_visit = partner // exp_dev
    slot = (visit_pos - partner_visit) % visit_count
    source = slot * exp_dev + partner % exp_dev
    choose_strip = (
        lax.broadcasted_iota(jnp.int32, (exp_dev, visit_count * exp_dev), 1) == source[:, None]
    ).astype(jnp.bfloat16)
    theirs = jnp.einsum(
        "ej,jsl->esl", choose_strip, strips_all, preferred_element_type=jnp.float32
    )
    own_patch = jnp.take(picked_all, visit_pos, axis=2).astype(jnp.float32)
    denominator = jnp.sum(own_patch).reshape(1)
    roomy = padded
    blocks = jnp.asarray(
        np.stack([toeplitz_block(2 * BLOCK, HALO, HALO * part) for part in SIGMA_PARTS])
    )
    nearby = strip_tiles(offset, coeffs, blocks, roomy, tile_len)
    half = exp_dev // 2
    matched = band_tiles(coeffs, blocks, roomy, tile_len, 0, half, None)
    matched = band_tiles(coeffs, blocks, roomy, tile_len, half, exp_dev - half, matched)
    difference = nearby - theirs
    pixel_weight = 1.0 / (1.0 + theirs * theirs)
    strip_rows = row_pos * tile_len + offset[:, None] + jnp.arange(STRIP, dtype=jnp.int32)[None, :]
    ycoord = centred(strip_rows, height)[:, :, None]
    xcoord = centred(col_pos * tile_len + jnp.arange(tile_len, dtype=jnp.int32), breadth)
    xgrid = xcoord[None, None, :]
    weight_x = pixel_weight * xgrid
    weight_y = pixel_weight * ycoord
    sum_w = jnp.sum(pixel_weight, axis=(1, 2))
    sum_x = jnp.sum(weight_x, axis=(1, 2))
    sum_y = jnp.sum(weight_y, axis=(1, 2))
    sum_xx = jnp.sum(weight_x * xgrid, axis=(1, 2))
    sum_xy = jnp.sum(weight_x * ycoord, axis=(1, 2))
    sum_yy = jnp.sum(weight_y * ycoord, axis=(1, 2))
    normal = jnp.stack(
        [
            jnp.stack([sum_w, sum_x, sum_y], -1),
            jnp.stack([sum_x, sum_xx, sum_xy], -1),
            jnp.stack([sum_y, sum_xy, sum_yy], -1),
        ],
        1,
    )
    moments = jnp.stack(
        [
            jnp.sum(pixel_weight * difference, axis=(1, 2)),
            jnp.sum(weight_x * difference, axis=(1, 2)),
            jnp.sum(weight_y * difference, axis=(1, 2)),
        ],
        -1,
    )
    packed = jnp.concatenate([normal.reshape(exp_dev, 9), moments], axis=1)
    packed = butterfly_sum(packed, (("row", row_count), ("col", col_count)))
    normal = packed[:, :9].reshape(exp_dev, 3, 3)
    moments = packed[:, 9:]
    plane_fit = solve_three(normal, moments)
    row_coord = centred(row_pos * tile_len + jnp.arange(tile_len, dtype=jnp.int32), height)
    choose = warp_index[:, 0, 0, :]
    ring_order = (
        lax.broadcasted_iota(jnp.int32, (visit_count, visit_count), 0)
        == (visit_pos - lax.broadcasted_iota(jnp.int32, (visit_count, visit_count), 1) - 1)
        % visit_count
    ).astype(jnp.float32)
    picked_ring = jnp.dot(picked.astype(jnp.float32), ring_order, precision=lax.Precision.HIGHEST)
    halves = [warp_tiles(
        choose, plane_fit, picked_ring, xcoord.reshape(1, tile_len),
        row_coord.reshape(tile_len, 1), matched, resample_bank, part, 4) for part in range(4)]
    numerator = jnp.concatenate(
        [ring_scatter(piece, "visit", visit_count) for piece in halves], 0
    )[None]
    coadd_patch = numerator / denominator[:, None, None]
    return (coadd_patch, plane_fit)


def solution(mesh):
    in_specs = (
        P("visit", "row", "col"),
        P("visit", None),
        P(),
        P("visit", "row", "col"),
        P(),
        P("visit", "row", "col", None),
        P("visit", "row", "col", None),
        P("visit", "row", "col"),
    )
    out_specs = (P("visit", "row", "col"), P("visit", None))
    return jax.shard_map(shards, mesh=mesh, in_specs=in_specs, out_specs=out_specs, check_vma=False)
```

```python
import functools

import jax
import jax.numpy as jnp
import ml_dtypes
import numpy as np
from jax import lax
from jax.sharding import PartitionSpec as P
from jax.experimental import pallas as pl
from jax.experimental.pallas import tpu as pltpu

HALO = 16
STRIP = 32
MAXD = 4


SIGMA_PARTS = (0.0625, 0.125, 0.25)


def extended(value, sides, width):
    for axis, dim in sides:
        devices, length = (lax.axis_size(axis), value.shape[dim])
        last = lax.slice_in_dim(value, length - width, length, axis=dim)
        initial = lax.slice_in_dim(value, 0, width, axis=dim)
        minor = dim == value.ndim - 1
        if minor:
            flat = value.shape[:-2] + (-1,)
            turned = jnp.swapaxes(last, -1, -2).shape
            last = jnp.swapaxes(last, -1, -2).reshape(flat)
            initial = jnp.swapaxes(initial, -1, -2).reshape(flat)
        if devices == 2:
            position = lax.axis_index(axis)
            facing = jnp.where(position == 0, last, initial)
            arrived = lax.ppermute(facing, axis, [(0, 1), (1, 0)])
            empty = jnp.zeros_like(arrived)
            before = jnp.where(position == 1, arrived, empty)
            after = jnp.where(position == 0, arrived, empty)
        else:
            up = [(i, (i + 1) % devices) for i in range(devices - 1)]
            down = [(j, i) for i, j in up]
            before = lax.ppermute(last, axis, up)
            after = lax.ppermute(initial, axis, down)
        if minor:
            before = jnp.swapaxes(before.reshape(turned), -1, -2)
            after = jnp.swapaxes(after.reshape(turned), -1, -2)
        value = jnp.concatenate([before, value, after], axis=dim)
    return value


def toeplitz_block(size, width, sigma):
    spread = (np.arange(2 * width + 1) - width).astype(np.float32)
    scale = np.float32(2.0) * np.float32(sigma) * np.float32(sigma)
    total = np.float32(np.exp(-spread * spread / scale).astype(np.float32).sum(dtype=np.float32))
    offset = (np.arange(size)[None, :] - np.arange(size)[:, None] - width).astype(np.float32)
    values = (np.exp(-offset * offset / scale).astype(np.float32) / total).astype(np.float32)
    values = np.where(np.abs(offset) <= width, values, np.float32(0.0))
    return values.astype(ml_dtypes.bfloat16)


def band_table(length, width, sigma):
    spread = (jnp.arange(2 * width + 1) - width).astype(jnp.float32)
    curve = jnp.exp(-spread * spread / (2.0 * sigma * sigma))
    total = jnp.sum(curve)
    rows_grid = lax.broadcasted_iota(jnp.int32, (length, length + 2 * width), 0)
    cols_grid = lax.broadcasted_iota(jnp.int32, (length, length + 2 * width), 1)
    offset = (cols_grid - rows_grid - width).astype(jnp.float32)
    values = jnp.exp(-offset * offset / (2.0 * sigma * sigma)) / total
    return jnp.where(jnp.abs(offset) <= width, values, 0.0).astype(jnp.bfloat16)


def centred(index, length):
    return (index.astype(jnp.float32) + 0.5) / length * 2.0 - 1.0


def solve_three(normal, moments):
    l00 = jnp.sqrt(normal[..., 0, 0])
    l10 = normal[..., 1, 0] / l00
    l20 = normal[..., 2, 0] / l00
    l11 = jnp.sqrt(normal[..., 1, 1] - l10 * l10)
    l21 = (normal[..., 2, 1] - l20 * l10) / l11
    l22 = jnp.sqrt(normal[..., 2, 2] - l20 * l20 - l21 * l21)
    zero = jnp.zeros_like(l00)
    lower = jnp.stack(
        [jnp.stack([l00, zero, zero], -1), jnp.stack([l10, l11, zero], -1),
         jnp.stack([l20, l21, l22], -1)], -2,
    )
    first = moments[..., 0] / lower[..., 0, 0]
    second = (moments[..., 1] - lower[..., 1, 0] * first) / lower[..., 1, 1]
    third = (moments[..., 2] - lower[..., 2, 0] * first - lower[..., 2, 1] * second) / lower[
        ..., 2, 2
    ]
    upper_top = third / lower[..., 2, 2]
    upper_mid = (second - lower[..., 2, 1] * upper_top) / lower[..., 1, 1]
    upper_low = (first - lower[..., 1, 0] * upper_mid - lower[..., 2, 0] * upper_top) / lower[
        ..., 0, 0
    ]
    return jnp.stack([upper_low, upper_mid, upper_top], -1)


def butterfly_sum(values, axes):
    for axis, size in axes:
        if size & (size - 1) == 0:
            bit = 1
            while bit < size:
                pairs = [(i, i ^ bit) for i in range(size)]
                values = jax.tree.map(lambda v: v + lax.ppermute(v, axis, pairs), values)
                bit *= 2
        else:
            position = lax.axis_index(axis)
            def gathered(v):
                parts = [v]
                for shift in range(1, size):
                    pairs = [(i, (i + shift) % size) for i in range(size)]
                    parts.append(lax.ppermute(v, axis, pairs))
                stacked = jnp.stack(parts, 0)
                order = (position - jnp.arange(size)) % size
                canonical = jnp.zeros_like(stacked).at[order].set(stacked)
                return jnp.sum(canonical, axis=0)
            values = jax.tree.map(gathered, values)
    return values


def conv_body(coef_ref, vt_ref, ht_ref, padded_ref, out_ref):
    e = pl.program_id(0)
    image = padded_ref[0]
    total = None
    for kernel in range(len(SIGMA_PARTS)):
        across = jnp.dot(vt_ref[0, kernel], image, preferred_element_type=jnp.float32)
        smoothed = lax.dot_general(
            across.astype(jnp.bfloat16), ht_ref[kernel], (((1,), (1,)), ((), ())),
            preferred_element_type=jnp.float32,
        )
        term = coef_ref[e, kernel] * smoothed
        total = term if total is None else total + term
    out_ref[0] = total


def conv_tiles(coeffs, vtables, htables, padded, per_exposure):
    exp_dev, wide = padded.shape[0], padded.shape[1]
    nk, out_rows = vtables.shape[-3], vtables.shape[-2]
    tile_len = htables.shape[1]
    if per_exposure:
        vspec = pl.BlockSpec((1, nk, out_rows, wide), lambda e: (e, 0, 0, 0))
    else:
        vtables = vtables[None]
        vspec = pl.BlockSpec((1, nk, out_rows, wide), lambda e: (0, 0, 0, 0))
    flops = exp_dev * nk * 2 * out_rows * wide * (wide + tile_len)
    moved = exp_dev * wide * wide * 2 + exp_dev * out_rows * tile_len * 4
    return pl.pallas_call(
        conv_body,
        grid=(exp_dev,),
        in_specs=[
            pl.BlockSpec(memory_space=pltpu.SMEM),
            vspec,
            pl.BlockSpec((nk, tile_len, wide), lambda e: (0, 0, 0)),
            pl.BlockSpec((1, wide, wide), lambda e: (e, 0, 0)),
        ],
        out_specs=pl.BlockSpec((1, out_rows, tile_len), lambda e: (e, 0, 0)),
        out_shape=jax.ShapeDtypeStruct((exp_dev, out_rows, tile_len), jnp.float32),
        compiler_params=pltpu.CompilerParams(
            dimension_semantics=("arbitrary",), vmem_limit_bytes=48 * 1024 * 1024
        ),
        cost_estimate=pl.CostEstimate(flops=flops, bytes_accessed=moved, transcendentals=0),
    )(coeffs, vtables, htables, padded)


BLOCK = 128


def strip_body(off_ref, coef_ref, tb_ref, padded_ref, out_ref):
    e = pl.program_id(0)
    rows, tile_len = out_ref.shape[1], out_ref.shape[2]
    wide = padded_ref.shape[1]
    windows = [(start, min(2 * BLOCK, wide - start)) for start in range(0, tile_len, BLOCK)]
    anchor = off_ref[e]
    base = jnp.minimum((anchor // BLOCK) * BLOCK, wide - 2 * BLOCK)
    shift = anchor - base
    window = padded_ref[0, pl.ds(pl.multiple_of(base, 16), 2 * BLOCK), :]
    pick = (
        lax.broadcasted_iota(jnp.int32, (rows, 2 * BLOCK), 1)
        == lax.broadcasted_iota(jnp.int32, (rows, 2 * BLOCK), 0) + shift
    ).astype(jnp.bfloat16)
    total = None
    for kernel in range(len(SIGMA_PARTS)):
        table = tb_ref[kernel]
        strip_rows = jnp.dot(pick, table, preferred_element_type=jnp.float32).astype(jnp.bfloat16)
        across = jnp.dot(strip_rows, window, preferred_element_type=jnp.float32)
        across = across.astype(jnp.bfloat16)
        block = table[:BLOCK]
        cols = [
            lax.dot_general(
                across[:, start:start + reach], block[:, :reach], (((1,), (1,)), ((), ())),
                preferred_element_type=jnp.float32,
            )
            for start, reach in windows
        ]
        term = coef_ref[e, kernel] * jnp.concatenate(cols, 1)
        total = term if total is None else total + term
    out_ref[0] = total


def strip_tiles(offset, coeffs, tb, padded, tile_len):
    exp_dev, wide = padded.shape[0], padded.shape[1]
    nk = tb.shape[0]
    grid_spec = pltpu.PrefetchScalarGridSpec(
        num_scalar_prefetch=1,
        grid=(exp_dev,),
        in_specs=[
            pl.BlockSpec(memory_space=pltpu.SMEM),
            pl.BlockSpec((nk, 2 * BLOCK, 2 * BLOCK), lambda e, off: (0, 0, 0)),
            pl.BlockSpec((1, wide, wide), lambda e, off: (e, 0, 0)),
        ],
        out_specs=pl.BlockSpec((1, STRIP, tile_len), lambda e, off: (e, 0, 0)),
    )
    flops = exp_dev * nk * 2 * STRIP * 2 * BLOCK * (2 * BLOCK + wide + tile_len)
    moved = exp_dev * wide * wide * 2 + exp_dev * STRIP * tile_len * 4
    return pl.pallas_call(
        strip_body,
        grid_spec=grid_spec,
        out_shape=jax.ShapeDtypeStruct((exp_dev, STRIP, tile_len), jnp.float32),
        compiler_params=pltpu.CompilerParams(
            dimension_semantics=("arbitrary",), vmem_limit_bytes=48 * 1024 * 1024
        ),
        cost_estimate=pl.CostEstimate(flops=flops, bytes_accessed=moved, transcendentals=0),
    )(offset, coeffs, tb, padded)


def band_body(first, coef_ref, blk_ref, padded_ref, *rest):
    out_ref = rest[-1]
    e = pl.program_id(0) + first
    tile_len = out_ref.shape[1]
    wide = padded_ref.shape[1]
    windows = [(start, min(2 * BLOCK, wide - start)) for start in range(0, tile_len, BLOCK)]
    total = None
    for kernel in range(len(SIGMA_PARTS)):
        block = blk_ref[kernel][:BLOCK]
        rows = [
            jnp.dot(
                block[:, :reach], padded_ref[0, start:start + reach, :],
                preferred_element_type=jnp.float32,
            )
            for start, reach in windows
        ]
        across = jnp.concatenate(rows, 0).astype(jnp.bfloat16)
        cols = [
            lax.dot_general(
                across[:, start:start + reach], block[:, :reach], (((1,), (1,)), ((), ())),
                preferred_element_type=jnp.float32,
            )
            for start, reach in windows
        ]
        term = coef_ref[e, kernel] * jnp.concatenate(cols, 1)
        total = term if total is None else total + term
    out_ref[0] = total


def band_tiles(coeffs, blocks, padded, tile_len, first, count, into):
    exp_dev, wide = padded.shape[0], padded.shape[1]
    nk = blocks.shape[0]
    steps = tile_len // BLOCK
    flops = count * nk * steps * 2 * BLOCK * 2 * BLOCK * (wide + tile_len)
    moved = count * wide * wide * 2 + count * tile_len * tile_len * 4
    in_specs = [
        pl.BlockSpec(memory_space=pltpu.SMEM),
        pl.BlockSpec((nk, 2 * BLOCK, 2 * BLOCK), lambda e: (0, 0, 0)),
        pl.BlockSpec((1, wide, wide), lambda e: (e + first, 0, 0)),
    ]
    operands = [coeffs, blocks, padded]
    aliases = {}
    if into is not None:
        in_specs.append(pl.BlockSpec(memory_space=pl.ANY))
        operands.append(into)
        aliases = {3: 0}
    return pl.pallas_call(
        functools.partial(band_body, first),
        grid=(count,),
        in_specs=in_specs,
        out_specs=pl.BlockSpec((1, tile_len, tile_len), lambda e: (e + first, 0, 0)),
        out_shape=jax.ShapeDtypeStruct((exp_dev, tile_len, tile_len), jnp.float32),
        input_output_aliases=aliases,
        compiler_params=pltpu.CompilerParams(
            dimension_semantics=("arbitrary",), vmem_limit_bytes=48 * 1024 * 1024
        ),
        cost_estimate=pl.CostEstimate(flops=flops, bytes_accessed=moved, transcendentals=0),
    )(*operands)


def warp_body(idx_ref, plane_ref, pick_ref, xrow_ref, ycol_ref, matched_ref, rmap_ref, cmap_ref,
              out_ref, acc_ref):
    e = pl.program_id(0)
    background = (
        plane_ref[e, 0] + plane_ref[e, 1] * xrow_ref[...]
    ) + plane_ref[e, 2] * ycol_ref[...]
    corrected = (matched_ref[0] - background).astype(jnp.bfloat16)
    halfway = jnp.dot(rmap_ref[0], corrected, preferred_element_type=jnp.float32)
    warped = lax.dot_general(
        halfway.astype(jnp.bfloat16), cmap_ref[0], (((1,), (1,)), ((), ())),
        preferred_element_type=jnp.float32,
    )
    warped = warped.astype(jnp.bfloat16).astype(jnp.float32)
    patches = acc_ref.shape[0]

    @pl.when(e == 0)
    def _():
        for v in range(patches):
            acc_ref[v] = pick_ref[e, v] * warped

    @pl.when(e > 0)
    def _():
        for v in range(patches):
            acc_ref[v] = acc_ref[v] + pick_ref[e, v] * warped

    @pl.when(e == pl.num_programs(0) - 1)
    def _():
        out_ref[...] = acc_ref[...].astype(jnp.bfloat16)


def warp_tiles(choose, plane, picked, xrow, ycol, matched, bank, part, pieces):
    exp_dev, tile_len = matched.shape[0], matched.shape[1]
    patches = picked.shape[1]
    rows = tile_len // pieces
    grid_spec = pltpu.PrefetchScalarGridSpec(
        num_scalar_prefetch=1,
        grid=(exp_dev,),
        in_specs=[
            pl.BlockSpec(memory_space=pltpu.SMEM),
            pl.BlockSpec(memory_space=pltpu.SMEM),
            pl.BlockSpec((1, tile_len), lambda e, idx: (0, 0)),
            pl.BlockSpec((tile_len, 1), lambda e, idx: (0, 0)),
            pl.BlockSpec((1, tile_len, tile_len), lambda e, idx: (e, 0, 0)),
            pl.BlockSpec((1, rows, tile_len), lambda e, idx: (idx[e, 0], part, 0)),
            pl.BlockSpec((1, tile_len, tile_len), lambda e, idx: (idx[e, 1], 0, 0)),
        ],
        out_specs=pl.BlockSpec((patches, rows, tile_len), lambda e, idx: (0, 0, 0)),
        scratch_shapes=[pltpu.VMEM((patches, rows, tile_len), jnp.float32)],
    )
    flops = exp_dev * 4 * rows * tile_len * tile_len
    moved = exp_dev * tile_len * tile_len * (4 + 2) + exp_dev * rows * tile_len * 2
    moved = moved + patches * rows * tile_len * 2
    vmem = 60 * 1024 * 1024
    return pl.pallas_call(
        warp_body,
        grid_spec=grid_spec,
        out_shape=jax.ShapeDtypeStruct((patches, rows, tile_len), jnp.bfloat16),
        compiler_params=pltpu.CompilerParams(
            dimension_semantics=("arbitrary",), vmem_limit_bytes=vmem
        ),
        cost_estimate=pl.CostEstimate(flops=flops, bytes_accessed=moved, transcendentals=0),
    )(choose, plane, picked, xrow, ycol, matched, bank, bank)


def ring_scatter(parts, axis, size):
    ring = [(i, (i + 1) % size) for i in range(size)]
    travelling = None
    for step in range(size - 1):
        own = parts[step].astype(jnp.float32)
        outgoing = own if travelling is None else travelling + own
        travelling = lax.ppermute(outgoing.astype(jnp.bfloat16), axis, ring).astype(jnp.float32)
    own = parts[size - 1].astype(jnp.float32)
    return own if travelling is None else travelling + own


def rows_from(source, anchor):
    return lax.dynamic_slice_in_dim(source, anchor, STRIP, 0)


def shards(images, coeffs, pair_list, weights, resample_bank, warp_index, destinations, counts):
    exp_dev = images.shape[0]
    tile_len = images.shape[1]
    row_count = lax.axis_size("row")
    col_count = lax.axis_size("col")
    visit_count = lax.axis_size("visit")
    row_pos = lax.axis_index("row")
    col_pos = lax.axis_index("col")
    visit_pos = lax.axis_index("visit")
    height = row_count * tile_len
    breadth = col_count * tile_len
    padded = extended(images, (("col", 2), ("row", 1)), HALO)
    own_ids = visit_pos * exp_dev + jnp.arange(exp_dev, dtype=jnp.int32)
    first_col = pair_list[:, 0]
    second_col = pair_list[:, 1]
    offsets = pair_list[:, 2]
    hit_first = first_col[None, :] == own_ids[:, None]
    hit_second = second_col[None, :] == own_ids[:, None]
    partner = jnp.sum(
        jnp.where(hit_first, second_col[None, :], 0) + jnp.where(hit_second, first_col[None, :], 0),
        axis=1,
    )
    offset = jnp.sum(jnp.where(hit_first | hit_second, offsets[None, :], 0), axis=1)
    pick_rows = (
        lax.broadcasted_iota(jnp.int32, (exp_dev, STRIP, tile_len), 2)
        == offset[:, None, None] + lax.broadcasted_iota(jnp.int32, (exp_dev, STRIP, tile_len), 1)
    ).astype(jnp.bfloat16)
    own_strip = jnp.einsum(
        "esr,erl->esl", pick_rows, images, preferred_element_type=jnp.float32
    ).astype(jnp.bfloat16)
    listed = destinations[:, 0, 0, :]
    how_many = counts[:, 0, 0]
    usable = jnp.arange(MAXD, dtype=jnp.int32)[None, :] < how_many[:, None]
    owners = jnp.arange(visit_count, dtype=jnp.int32)
    member = jnp.any(usable[:, :, None] & (listed[:, :, None] == owners[None, None, :]), axis=1)
    tile_weight = weights[:, 0, 0]
    nothing = jnp.zeros((), jnp.bfloat16)
    picked = jnp.where(member, tile_weight[:, None], nothing)
    strip_rows_n = exp_dev * STRIP
    extra = -(-(exp_dev * visit_count) // tile_len)
    extra = -(-extra // 16) * 16
    tail = jnp.zeros((extra * tile_len,), jnp.bfloat16)
    tail = tail.at[: exp_dev * visit_count].set(picked.reshape(-1)).reshape(extra, tile_len)
    payload = jnp.concatenate([own_strip.reshape(strip_rows_n, tile_len), tail], axis=0)
    received = [payload]
    for shift in range(1, visit_count):
        pairs = [(i, (i + shift) % visit_count) for i in range(visit_count)]
        received.append(lax.ppermute(payload, "visit", pairs))
    stacked = jnp.stack(received, 0)
    strips_all = stacked[:, :strip_rows_n].reshape(visit_count * exp_dev, STRIP, tile_len)
    picked_all = stacked[:, strip_rows_n:].reshape(visit_count, -1)[:, : exp_dev * visit_count]
    picked_all = picked_all.reshape(visit_count, exp_dev, visit_count)
    partner_visit = partner // exp_dev
    slot = (visit_pos - partner_visit) % visit_count
    source = slot * exp_dev + partner % exp_dev
    choose_strip = (
        lax.broadcasted_iota(jnp.int32, (exp_dev, visit_count * exp_dev), 1) == source[:, None]
    ).astype(jnp.bfloat16)
    theirs = jnp.einsum(
        "ej,jsl->esl", choose_strip, strips_all, preferred_element_type=jnp.float32
    )
    own_patch = jnp.take(picked_all, visit_pos, axis=2).astype(jnp.float32)
    denominator = jnp.sum(own_patch).reshape(1)
    roomy = padded
    blocks = jnp.asarray(
        np.stack([toeplitz_block(2 * BLOCK, HALO, HALO * part) for part in SIGMA_PARTS])
    )
    nearby = strip_tiles(offset, coeffs, blocks, roomy, tile_len)
    half = exp_dev // 2
    matched = band_tiles(coeffs, blocks, roomy, tile_len, 0, half, None)
    matched = band_tiles(coeffs, blocks, roomy, tile_len, half, exp_dev - half, matched)
    difference = nearby - theirs
    pixel_weight = 1.0 / (1.0 + theirs * theirs)
    strip_rows = row_pos * tile_len + offset[:, None] + jnp.arange(STRIP, dtype=jnp.int32)[None, :]
    ycoord = centred(strip_rows, height)[:, :, None]
    xcoord = centred(col_pos * tile_len + jnp.arange(tile_len, dtype=jnp.int32), breadth)
    xgrid = xcoord[None, None, :]
    weight_x = pixel_weight * xgrid
    weight_y = pixel_weight * ycoord
    sum_w = jnp.sum(pixel_weight, axis=(1, 2))
    sum_x = jnp.sum(weight_x, axis=(1, 2))
    sum_y = jnp.sum(weight_y, axis=(1, 2))
    sum_xx = jnp.sum(weight_x * xgrid, axis=(1, 2))
    sum_xy = jnp.sum(weight_x * ycoord, axis=(1, 2))
    sum_yy = jnp.sum(weight_y * ycoord, axis=(1, 2))
    normal = jnp.stack(
        [
            jnp.stack([sum_w, sum_x, sum_y], -1),
            jnp.stack([sum_x, sum_xx, sum_xy], -1),
            jnp.stack([sum_y, sum_xy, sum_yy], -1),
        ],
        1,
    )
    moments = jnp.stack(
        [
            jnp.sum(pixel_weight * difference, axis=(1, 2)),
            jnp.sum(weight_x * difference, axis=(1, 2)),
            jnp.sum(weight_y * difference, axis=(1, 2)),
        ],
        -1,
    )
    packed = jnp.concatenate([normal.reshape(exp_dev, 9), moments], axis=1)
    packed = butterfly_sum(packed, (("row", row_count), ("col", col_count)))
    normal = packed[:, :9].reshape(exp_dev, 3, 3)
    moments = packed[:, 9:]
    plane_fit = solve_three(normal, moments)
    row_coord = centred(row_pos * tile_len + jnp.arange(tile_len, dtype=jnp.int32), height)
    choose = warp_index[:, 0, 0, :]
    ring_order = (
        lax.broadcasted_iota(jnp.int32, (visit_count, visit_count), 0)
        == (visit_pos - lax.broadcasted_iota(jnp.int32, (visit_count, visit_count), 1) - 1)
        % visit_count
    ).astype(jnp.float32)
    picked_ring = jnp.dot(picked.astype(jnp.float32), ring_order, precision=lax.Precision.HIGHEST)
    halves = [warp_tiles(
        choose, plane_fit, picked_ring, xcoord.reshape(1, tile_len),
        row_coord.reshape(tile_len, 1), matched, resample_bank, part, 2) for part in range(2)]
    numerator = jnp.concatenate(
        [ring_scatter(piece, "visit", visit_count) for piece in halves], 0
    )[None]
    coadd_patch = numerator / denominator[:, None, None]
    return (coadd_patch, plane_fit)


def solution(mesh):
    in_specs = (
        P("visit", "row", "col"),
        P("visit", None),
        P(),
        P("visit", "row", "col"),
        P(),
        P("visit", "row", "col", None),
        P("visit", "row", "col", None),
        P("visit", "row", "col"),
    )
    out_specs = (P("visit", "row", "col"), P("visit", None))
    return jax.shard_map(shards, mesh=mesh, in_specs=in_specs, out_specs=out_specs, check_vma=False)
```

```python
import functools

import jax
import jax.numpy as jnp
import ml_dtypes
import numpy as np
from jax import lax
from jax.sharding import PartitionSpec as P
from jax.experimental import pallas as pl
from jax.experimental.pallas import tpu as pltpu

HALO = 16
STRIP = 32
MAXD = 4


SIGMA_PARTS = (0.0625, 0.125, 0.25)


def extended(value, sides, width):
    for axis, dim in sides:
        devices, length = (lax.axis_size(axis), value.shape[dim])
        last = lax.slice_in_dim(value, length - width, length, axis=dim)
        initial = lax.slice_in_dim(value, 0, width, axis=dim)
        minor = dim == value.ndim - 1
        if minor:
            flat = value.shape[:-2] + (-1,)
            turned = jnp.swapaxes(last, -1, -2).shape
            last = jnp.swapaxes(last, -1, -2).reshape(flat)
            initial = jnp.swapaxes(initial, -1, -2).reshape(flat)
        if devices == 2:
            position = lax.axis_index(axis)
            facing = jnp.where(position == 0, last, initial)
            arrived = lax.ppermute(facing, axis, [(0, 1), (1, 0)])
            empty = jnp.zeros_like(arrived)
            before = jnp.where(position == 1, arrived, empty)
            after = jnp.where(position == 0, arrived, empty)
        else:
            up = [(i, (i + 1) % devices) for i in range(devices - 1)]
            down = [(j, i) for i, j in up]
            before = lax.ppermute(last, axis, up)
            after = lax.ppermute(initial, axis, down)
        if minor:
            before = jnp.swapaxes(before.reshape(turned), -1, -2)
            after = jnp.swapaxes(after.reshape(turned), -1, -2)
        value = jnp.concatenate([before, value, after], axis=dim)
    return value


def toeplitz_block(size, width, sigma):
    spread = (np.arange(2 * width + 1) - width).astype(np.float32)
    scale = np.float32(2.0) * np.float32(sigma) * np.float32(sigma)
    total = np.float32(np.exp(-spread * spread / scale).astype(np.float32).sum(dtype=np.float32))
    offset = (np.arange(size)[None, :] - np.arange(size)[:, None] - width).astype(np.float32)
    values = (np.exp(-offset * offset / scale).astype(np.float32) / total).astype(np.float32)
    values = np.where(np.abs(offset) <= width, values, np.float32(0.0))
    return values.astype(ml_dtypes.bfloat16)


def band_table(length, width, sigma):
    spread = (jnp.arange(2 * width + 1) - width).astype(jnp.float32)
    curve = jnp.exp(-spread * spread / (2.0 * sigma * sigma))
    total = jnp.sum(curve)
    rows_grid = lax.broadcasted_iota(jnp.int32, (length, length + 2 * width), 0)
    cols_grid = lax.broadcasted_iota(jnp.int32, (length, length + 2 * width), 1)
    offset = (cols_grid - rows_grid - width).astype(jnp.float32)
    values = jnp.exp(-offset * offset / (2.0 * sigma * sigma)) / total
    return jnp.where(jnp.abs(offset) <= width, values, 0.0).astype(jnp.bfloat16)


def centred(index, length):
    return (index.astype(jnp.float32) + 0.5) / length * 2.0 - 1.0


def solve_three(normal, moments):
    l00 = jnp.sqrt(normal[..., 0, 0])
    l10 = normal[..., 1, 0] / l00
    l20 = normal[..., 2, 0] / l00
    l11 = jnp.sqrt(normal[..., 1, 1] - l10 * l10)
    l21 = (normal[..., 2, 1] - l20 * l10) / l11
    l22 = jnp.sqrt(normal[..., 2, 2] - l20 * l20 - l21 * l21)
    zero = jnp.zeros_like(l00)
    lower = jnp.stack(
        [jnp.stack([l00, zero, zero], -1), jnp.stack([l10, l11, zero], -1),
         jnp.stack([l20, l21, l22], -1)], -2,
    )
    first = moments[..., 0] / lower[..., 0, 0]
    second = (moments[..., 1] - lower[..., 1, 0] * first) / lower[..., 1, 1]
    third = (moments[..., 2] - lower[..., 2, 0] * first - lower[..., 2, 1] * second) / lower[
        ..., 2, 2
    ]
    upper_top = third / lower[..., 2, 2]
    upper_mid = (second - lower[..., 2, 1] * upper_top) / lower[..., 1, 1]
    upper_low = (first - lower[..., 1, 0] * upper_mid - lower[..., 2, 0] * upper_top) / lower[
        ..., 0, 0
    ]
    return jnp.stack([upper_low, upper_mid, upper_top], -1)


def butterfly_sum(values, axes):
    for axis, size in axes:
        if size & (size - 1) == 0:
            bit = 1
            while bit < size:
                pairs = [(i, i ^ bit) for i in range(size)]
                values = jax.tree.map(lambda v: v + lax.ppermute(v, axis, pairs), values)
                bit *= 2
        else:
            position = lax.axis_index(axis)
            def gathered(v):
                parts = [v]
                for shift in range(1, size):
                    pairs = [(i, (i + shift) % size) for i in range(size)]
                    parts.append(lax.ppermute(v, axis, pairs))
                stacked = jnp.stack(parts, 0)
                order = (position - jnp.arange(size)) % size
                canonical = jnp.zeros_like(stacked).at[order].set(stacked)
                return jnp.sum(canonical, axis=0)
            values = jax.tree.map(gathered, values)
    return values


def conv_body(coef_ref, vt_ref, ht_ref, padded_ref, out_ref):
    e = pl.program_id(0)
    image = padded_ref[0]
    total = None
    for kernel in range(len(SIGMA_PARTS)):
        across = jnp.dot(vt_ref[0, kernel], image, preferred_element_type=jnp.float32)
        smoothed = lax.dot_general(
            across.astype(jnp.bfloat16), ht_ref[kernel], (((1,), (1,)), ((), ())),
            preferred_element_type=jnp.float32,
        )
        term = coef_ref[e, kernel] * smoothed
        total = term if total is None else total + term
    out_ref[0] = total


def conv_tiles(coeffs, vtables, htables, padded, per_exposure):
    exp_dev, wide = padded.shape[0], padded.shape[1]
    nk, out_rows = vtables.shape[-3], vtables.shape[-2]
    tile_len = htables.shape[1]
    if per_exposure:
        vspec = pl.BlockSpec((1, nk, out_rows, wide), lambda e: (e, 0, 0, 0))
    else:
        vtables = vtables[None]
        vspec = pl.BlockSpec((1, nk, out_rows, wide), lambda e: (0, 0, 0, 0))
    flops = exp_dev * nk * 2 * out_rows * wide * (wide + tile_len)
    moved = exp_dev * wide * wide * 2 + exp_dev * out_rows * tile_len * 4
    return pl.pallas_call(
        conv_body,
        grid=(exp_dev,),
        in_specs=[
            pl.BlockSpec(memory_space=pltpu.SMEM),
            vspec,
            pl.BlockSpec((nk, tile_len, wide), lambda e: (0, 0, 0)),
            pl.BlockSpec((1, wide, wide), lambda e: (e, 0, 0)),
        ],
        out_specs=pl.BlockSpec((1, out_rows, tile_len), lambda e: (e, 0, 0)),
        out_shape=jax.ShapeDtypeStruct((exp_dev, out_rows, tile_len), jnp.float32),
        compiler_params=pltpu.CompilerParams(
            dimension_semantics=("arbitrary",), vmem_limit_bytes=48 * 1024 * 1024
        ),
        cost_estimate=pl.CostEstimate(flops=flops, bytes_accessed=moved, transcendentals=0),
    )(coeffs, vtables, htables, padded)


BLOCK = 128


def strip_body(off_ref, coef_ref, tb_ref, padded_ref, out_ref):
    e = pl.program_id(0)
    rows, tile_len = out_ref.shape[1], out_ref.shape[2]
    wide = padded_ref.shape[1]
    windows = [(start, min(2 * BLOCK, wide - start)) for start in range(0, tile_len, BLOCK)]
    anchor = off_ref[e]
    base = jnp.minimum((anchor // BLOCK) * BLOCK, wide - 2 * BLOCK)
    shift = anchor - base
    window = padded_ref[0, pl.ds(pl.multiple_of(base, 16), 2 * BLOCK), :]
    pick = (
        lax.broadcasted_iota(jnp.int32, (rows, 2 * BLOCK), 1)
        == lax.broadcasted_iota(jnp.int32, (rows, 2 * BLOCK), 0) + shift
    ).astype(jnp.bfloat16)
    total = None
    for kernel in range(len(SIGMA_PARTS)):
        table = tb_ref[kernel]
        strip_rows = jnp.dot(pick, table, preferred_element_type=jnp.float32).astype(jnp.bfloat16)
        across = jnp.dot(strip_rows, window, preferred_element_type=jnp.float32)
        across = across.astype(jnp.bfloat16)
        block = table[:BLOCK]
        cols = [
            lax.dot_general(
                across[:, start:start + reach], block[:, :reach], (((1,), (1,)), ((), ())),
                preferred_element_type=jnp.float32,
            )
            for start, reach in windows
        ]
        term = coef_ref[e, kernel] * jnp.concatenate(cols, 1)
        total = term if total is None else total + term
    out_ref[0] = total


def strip_tiles(offset, coeffs, tb, padded, tile_len):
    exp_dev, wide = padded.shape[0], padded.shape[1]
    nk = tb.shape[0]
    grid_spec = pltpu.PrefetchScalarGridSpec(
        num_scalar_prefetch=1,
        grid=(exp_dev,),
        in_specs=[
            pl.BlockSpec(memory_space=pltpu.SMEM),
            pl.BlockSpec((nk, 2 * BLOCK, 2 * BLOCK), lambda e, off: (0, 0, 0)),
            pl.BlockSpec((1, wide, wide), lambda e, off: (e, 0, 0)),
        ],
        out_specs=pl.BlockSpec((1, STRIP, tile_len), lambda e, off: (e, 0, 0)),
    )
    flops = exp_dev * nk * 2 * STRIP * 2 * BLOCK * (2 * BLOCK + wide + tile_len)
    moved = exp_dev * wide * wide * 2 + exp_dev * STRIP * tile_len * 4
    return pl.pallas_call(
        strip_body,
        grid_spec=grid_spec,
        out_shape=jax.ShapeDtypeStruct((exp_dev, STRIP, tile_len), jnp.float32),
        compiler_params=pltpu.CompilerParams(
            dimension_semantics=("arbitrary",), vmem_limit_bytes=48 * 1024 * 1024
        ),
        cost_estimate=pl.CostEstimate(flops=flops, bytes_accessed=moved, transcendentals=0),
    )(offset, coeffs, tb, padded)


def band_body(first, coef_ref, blk_ref, padded_ref, *rest):
    out_ref = rest[-1]
    e = pl.program_id(0) + first
    tile_len = out_ref.shape[1]
    wide = padded_ref.shape[1]
    windows = [(start, min(2 * BLOCK, wide - start)) for start in range(0, tile_len, BLOCK)]
    total = None
    for kernel in range(len(SIGMA_PARTS)):
        block = blk_ref[kernel][:BLOCK]
        rows = [
            jnp.dot(
                block[:, :reach], padded_ref[0, start:start + reach, :],
                preferred_element_type=jnp.float32,
            )
            for start, reach in windows
        ]
        across = jnp.concatenate(rows, 0).astype(jnp.bfloat16)
        cols = [
            lax.dot_general(
                across[:, start:start + reach], block[:, :reach], (((1,), (1,)), ((), ())),
                preferred_element_type=jnp.float32,
            )
            for start, reach in windows
        ]
        term = coef_ref[e, kernel] * jnp.concatenate(cols, 1)
        total = term if total is None else total + term
    out_ref[0] = total


def band_tiles(coeffs, blocks, padded, tile_len, first, count, into):
    exp_dev, wide = padded.shape[0], padded.shape[1]
    nk = blocks.shape[0]
    steps = tile_len // BLOCK
    flops = count * nk * steps * 2 * BLOCK * 2 * BLOCK * (wide + tile_len)
    moved = count * wide * wide * 2 + count * tile_len * tile_len * 4
    in_specs = [
        pl.BlockSpec(memory_space=pltpu.SMEM),
        pl.BlockSpec((nk, 2 * BLOCK, 2 * BLOCK), lambda e: (0, 0, 0)),
        pl.BlockSpec((1, wide, wide), lambda e: (e + first, 0, 0)),
    ]
    operands = [coeffs, blocks, padded]
    aliases = {}
    if into is not None:
        in_specs.append(pl.BlockSpec(memory_space=pl.ANY))
        operands.append(into)
        aliases = {3: 0}
    return pl.pallas_call(
        functools.partial(band_body, first),
        grid=(count,),
        in_specs=in_specs,
        out_specs=pl.BlockSpec((1, tile_len, tile_len), lambda e: (e + first, 0, 0)),
        out_shape=jax.ShapeDtypeStruct((exp_dev, tile_len, tile_len), jnp.float32),
        input_output_aliases=aliases,
        compiler_params=pltpu.CompilerParams(
            dimension_semantics=("arbitrary",), vmem_limit_bytes=48 * 1024 * 1024
        ),
        cost_estimate=pl.CostEstimate(flops=flops, bytes_accessed=moved, transcendentals=0),
    )(*operands)


def warp_body(idx_ref, plane_ref, pick_ref, xrow_ref, ycol_ref, matched_ref, rmap_ref, cmap_ref,
              *rest):
    out_refs, acc_ref = rest[:-1], rest[-1]
    e = pl.program_id(0)
    background = (
        plane_ref[e, 0] + plane_ref[e, 1] * xrow_ref[...]
    ) + plane_ref[e, 2] * ycol_ref[...]
    corrected = (matched_ref[0] - background).astype(jnp.bfloat16)
    halfway = jnp.dot(rmap_ref[0], corrected, preferred_element_type=jnp.float32)
    warped = lax.dot_general(
        halfway.astype(jnp.bfloat16), cmap_ref[0], (((1,), (1,)), ((), ())),
        preferred_element_type=jnp.float32,
    )
    warped = warped.astype(jnp.bfloat16).astype(jnp.float32)
    patches = acc_ref.shape[0]

    @pl.when(e == 0)
    def _():
        for v in range(patches):
            acc_ref[v] = pick_ref[e, v] * warped

    @pl.when(e > 0)
    def _():
        for v in range(patches):
            acc_ref[v] = acc_ref[v] + pick_ref[e, v] * warped

    @pl.when(e == pl.num_programs(0) - 1)
    def _():
        for v in range(patches):
            out_refs[v][...] = acc_ref[v].astype(jnp.bfloat16)


def warp_tiles(choose, plane, picked, xrow, ycol, matched, bank, part, pieces):
    exp_dev, tile_len = matched.shape[0], matched.shape[1]
    patches = picked.shape[1]
    rows = tile_len // pieces
    grid_spec = pltpu.PrefetchScalarGridSpec(
        num_scalar_prefetch=1,
        grid=(exp_dev,),
        in_specs=[
            pl.BlockSpec(memory_space=pltpu.SMEM),
            pl.BlockSpec(memory_space=pltpu.SMEM),
            pl.BlockSpec((1, tile_len), lambda e, idx: (0, 0)),
            pl.BlockSpec((tile_len, 1), lambda e, idx: (0, 0)),
            pl.BlockSpec((1, tile_len, tile_len), lambda e, idx: (e, 0, 0)),
            pl.BlockSpec((1, rows, tile_len), lambda e, idx: (idx[e, 0], part, 0)),
            pl.BlockSpec((1, tile_len, tile_len), lambda e, idx: (idx[e, 1], 0, 0)),
        ],
        out_specs=[pl.BlockSpec((rows, tile_len), lambda e, idx: (0, 0)) for _ in range(patches)],
        scratch_shapes=[pltpu.VMEM((patches, rows, tile_len), jnp.float32)],
    )
    flops = exp_dev * 4 * rows * tile_len * tile_len
    moved = exp_dev * tile_len * tile_len * (4 + 2) + exp_dev * rows * tile_len * 2
    moved = moved + patches * rows * tile_len * 2
    vmem = 60 * 1024 * 1024
    return pl.pallas_call(
        warp_body,
        grid_spec=grid_spec,
        out_shape=[jax.ShapeDtypeStruct((rows, tile_len), jnp.bfloat16) for _ in range(patches)],
        compiler_params=pltpu.CompilerParams(
            dimension_semantics=("arbitrary",), vmem_limit_bytes=vmem
        ),
        cost_estimate=pl.CostEstimate(flops=flops, bytes_accessed=moved, transcendentals=0),
    )(choose, plane, picked, xrow, ycol, matched, bank, bank)


def ring_scatter(parts, axis, size):
    ring = [(i, (i + 1) % size) for i in range(size)]
    travelling = None
    for step in range(size - 1):
        own = parts[step].astype(jnp.float32)
        outgoing = own if travelling is None else travelling + own
        travelling = lax.ppermute(outgoing.astype(jnp.bfloat16), axis, ring).astype(jnp.float32)
    own = parts[size - 1].astype(jnp.float32)
    return own if travelling is None else travelling + own


def rows_from(source, anchor):
    return lax.dynamic_slice_in_dim(source, anchor, STRIP, 0)


def shards(images, coeffs, pair_list, weights, resample_bank, warp_index, destinations, counts):
    exp_dev = images.shape[0]
    tile_len = images.shape[1]
    row_count = lax.axis_size("row")
    col_count = lax.axis_size("col")
    visit_count = lax.axis_size("visit")
    row_pos = lax.axis_index("row")
    col_pos = lax.axis_index("col")
    visit_pos = lax.axis_index("visit")
    height = row_count * tile_len
    breadth = col_count * tile_len
    padded = extended(images, (("col", 2), ("row", 1)), HALO)
    own_ids = visit_pos * exp_dev + jnp.arange(exp_dev, dtype=jnp.int32)
    first_col = pair_list[:, 0]
    second_col = pair_list[:, 1]
    offsets = pair_list[:, 2]
    hit_first = first_col[None, :] == own_ids[:, None]
    hit_second = second_col[None, :] == own_ids[:, None]
    partner = jnp.sum(
        jnp.where(hit_first, second_col[None, :], 0) + jnp.where(hit_second, first_col[None, :], 0),
        axis=1,
    )
    offset = jnp.sum(jnp.where(hit_first | hit_second, offsets[None, :], 0), axis=1)
    pick_rows = (
        lax.broadcasted_iota(jnp.int32, (exp_dev, STRIP, tile_len), 2)
        == offset[:, None, None] + lax.broadcasted_iota(jnp.int32, (exp_dev, STRIP, tile_len), 1)
    ).astype(jnp.bfloat16)
    own_strip = jnp.einsum(
        "esr,erl->esl", pick_rows, images, preferred_element_type=jnp.float32
    ).astype(jnp.bfloat16)
    listed = destinations[:, 0, 0, :]
    how_many = counts[:, 0, 0]
    usable = jnp.arange(MAXD, dtype=jnp.int32)[None, :] < how_many[:, None]
    owners = jnp.arange(visit_count, dtype=jnp.int32)
    member = jnp.any(usable[:, :, None] & (listed[:, :, None] == owners[None, None, :]), axis=1)
    tile_weight = weights[:, 0, 0]
    nothing = jnp.zeros((), jnp.bfloat16)
    picked = jnp.where(member, tile_weight[:, None], nothing)
    strip_rows_n = exp_dev * STRIP
    extra = -(-(exp_dev * visit_count) // tile_len)
    extra = -(-extra // 16) * 16
    tail = jnp.zeros((extra * tile_len,), jnp.bfloat16)
    tail = tail.at[: exp_dev * visit_count].set(picked.reshape(-1)).reshape(extra, tile_len)
    payload = jnp.concatenate([own_strip.reshape(strip_rows_n, tile_len), tail], axis=0)
    received = [payload]
    for shift in range(1, visit_count):
        pairs = [(i, (i + shift) % visit_count) for i in range(visit_count)]
        received.append(lax.ppermute(payload, "visit", pairs))
    stacked = jnp.stack(received, 0)
    strips_all = stacked[:, :strip_rows_n].reshape(visit_count * exp_dev, STRIP, tile_len)
    picked_all = stacked[:, strip_rows_n:].reshape(visit_count, -1)[:, : exp_dev * visit_count]
    picked_all = picked_all.reshape(visit_count, exp_dev, visit_count)
    partner_visit = partner // exp_dev
    slot = (visit_pos - partner_visit) % visit_count
    source = slot * exp_dev + partner % exp_dev
    choose_strip = (
        lax.broadcasted_iota(jnp.int32, (exp_dev, visit_count * exp_dev), 1) == source[:, None]
    ).astype(jnp.bfloat16)
    theirs = jnp.einsum(
        "ej,jsl->esl", choose_strip, strips_all, preferred_element_type=jnp.float32
    )
    own_patch = jnp.take(picked_all, visit_pos, axis=2).astype(jnp.float32)
    denominator = jnp.sum(own_patch).reshape(1)
    roomy = padded
    blocks = jnp.asarray(
        np.stack([toeplitz_block(2 * BLOCK, HALO, HALO * part) for part in SIGMA_PARTS])
    )
    nearby = strip_tiles(offset, coeffs, blocks, roomy, tile_len)
    half = exp_dev // 2
    matched = band_tiles(coeffs, blocks, roomy, tile_len, 0, half, None)
    matched = band_tiles(coeffs, blocks, roomy, tile_len, half, exp_dev - half, matched)
    difference = nearby - theirs
    pixel_weight = 1.0 / (1.0 + theirs * theirs)
    strip_rows = row_pos * tile_len + offset[:, None] + jnp.arange(STRIP, dtype=jnp.int32)[None, :]
    ycoord = centred(strip_rows, height)[:, :, None]
    xcoord = centred(col_pos * tile_len + jnp.arange(tile_len, dtype=jnp.int32), breadth)
    xgrid = xcoord[None, None, :]
    weight_x = pixel_weight * xgrid
    weight_y = pixel_weight * ycoord
    sum_w = jnp.sum(pixel_weight, axis=(1, 2))
    sum_x = jnp.sum(weight_x, axis=(1, 2))
    sum_y = jnp.sum(weight_y, axis=(1, 2))
    sum_xx = jnp.sum(weight_x * xgrid, axis=(1, 2))
    sum_xy = jnp.sum(weight_x * ycoord, axis=(1, 2))
    sum_yy = jnp.sum(weight_y * ycoord, axis=(1, 2))
    normal = jnp.stack(
        [
            jnp.stack([sum_w, sum_x, sum_y], -1),
            jnp.stack([sum_x, sum_xx, sum_xy], -1),
            jnp.stack([sum_y, sum_xy, sum_yy], -1),
        ],
        1,
    )
    moments = jnp.stack(
        [
            jnp.sum(pixel_weight * difference, axis=(1, 2)),
            jnp.sum(weight_x * difference, axis=(1, 2)),
            jnp.sum(weight_y * difference, axis=(1, 2)),
        ],
        -1,
    )
    packed = jnp.concatenate([normal.reshape(exp_dev, 9), moments], axis=1)
    packed = butterfly_sum(packed, (("row", row_count), ("col", col_count)))
    normal = packed[:, :9].reshape(exp_dev, 3, 3)
    moments = packed[:, 9:]
    plane_fit = solve_three(normal, moments)
    row_coord = centred(row_pos * tile_len + jnp.arange(tile_len, dtype=jnp.int32), height)
    choose = warp_index[:, 0, 0, :]
    ring_order = (
        lax.broadcasted_iota(jnp.int32, (visit_count, visit_count), 0)
        == (visit_pos - lax.broadcasted_iota(jnp.int32, (visit_count, visit_count), 1) - 1)
        % visit_count
    ).astype(jnp.float32)
    picked_ring = jnp.dot(picked.astype(jnp.float32), ring_order, precision=lax.Precision.HIGHEST)
    halves = [warp_tiles(
        choose, plane_fit, picked_ring, xcoord.reshape(1, tile_len),
        row_coord.reshape(tile_len, 1), matched, resample_bank, part, 2) for part in range(2)]
    numerator = jnp.concatenate(
        [ring_scatter(piece, "visit", visit_count) for piece in halves], 0
    )[None]
    coadd_patch = numerator / denominator[:, None, None]
    return (coadd_patch, plane_fit)


def solution(mesh):
    in_specs = (
        P("visit", "row", "col"),
        P("visit", None),
        P(),
        P("visit", "row", "col"),
        P(),
        P("visit", "row", "col", None),
        P("visit", "row", "col", None),
        P("visit", "row", "col"),
    )
    out_specs = (P("visit", "row", "col"), P("visit", None))
    return jax.shard_map(shards, mesh=mesh, in_specs=in_specs, out_specs=out_specs, check_vma=False)
```

```python
import functools

import jax
import jax.numpy as jnp
import ml_dtypes
import numpy as np
from jax import lax
from jax.sharding import PartitionSpec as P
from jax.experimental import pallas as pl
from jax.experimental.pallas import tpu as pltpu

HALO = 16
STRIP = 32
MAXD = 4


SIGMA_PARTS = (0.0625, 0.125, 0.25)


def extended(value, sides, width):
    for axis, dim in sides:
        devices, length = (lax.axis_size(axis), value.shape[dim])
        last = lax.slice_in_dim(value, length - width, length, axis=dim)
        initial = lax.slice_in_dim(value, 0, width, axis=dim)
        minor = dim == value.ndim - 1
        if minor:
            flat = value.shape[:-2] + (-1,)
            turned = jnp.swapaxes(last, -1, -2).shape
            last = jnp.swapaxes(last, -1, -2).reshape(flat)
            initial = jnp.swapaxes(initial, -1, -2).reshape(flat)
        if devices == 2:
            position = lax.axis_index(axis)
            facing = jnp.where(position == 0, last, initial)
            arrived = lax.ppermute(facing, axis, [(0, 1), (1, 0)])
            empty = jnp.zeros_like(arrived)
            before = jnp.where(position == 1, arrived, empty)
            after = jnp.where(position == 0, arrived, empty)
        else:
            up = [(i, (i + 1) % devices) for i in range(devices - 1)]
            down = [(j, i) for i, j in up]
            before = lax.ppermute(last, axis, up)
            after = lax.ppermute(initial, axis, down)
        if minor:
            before = jnp.swapaxes(before.reshape(turned), -1, -2)
            after = jnp.swapaxes(after.reshape(turned), -1, -2)
        value = jnp.concatenate([before, value, after], axis=dim)
    return value


def toeplitz_block(size, width, sigma):
    spread = (np.arange(2 * width + 1) - width).astype(np.float32)
    scale = np.float32(2.0) * np.float32(sigma) * np.float32(sigma)
    total = np.float32(np.exp(-spread * spread / scale).astype(np.float32).sum(dtype=np.float32))
    offset = (np.arange(size)[None, :] - np.arange(size)[:, None] - width).astype(np.float32)
    values = (np.exp(-offset * offset / scale).astype(np.float32) / total).astype(np.float32)
    values = np.where(np.abs(offset) <= width, values, np.float32(0.0))
    return values.astype(ml_dtypes.bfloat16)


def band_table(length, width, sigma):
    spread = (jnp.arange(2 * width + 1) - width).astype(jnp.float32)
    curve = jnp.exp(-spread * spread / (2.0 * sigma * sigma))
    total = jnp.sum(curve)
    rows_grid = lax.broadcasted_iota(jnp.int32, (length, length + 2 * width), 0)
    cols_grid = lax.broadcasted_iota(jnp.int32, (length, length + 2 * width), 1)
    offset = (cols_grid - rows_grid - width).astype(jnp.float32)
    values = jnp.exp(-offset * offset / (2.0 * sigma * sigma)) / total
    return jnp.where(jnp.abs(offset) <= width, values, 0.0).astype(jnp.bfloat16)


def centred(index, length):
    return (index.astype(jnp.float32) + 0.5) / length * 2.0 - 1.0


def solve_three(normal, moments):
    l00 = jnp.sqrt(normal[..., 0, 0])
    l10 = normal[..., 1, 0] / l00
    l20 = normal[..., 2, 0] / l00
    l11 = jnp.sqrt(normal[..., 1, 1] - l10 * l10)
    l21 = (normal[..., 2, 1] - l20 * l10) / l11
    l22 = jnp.sqrt(normal[..., 2, 2] - l20 * l20 - l21 * l21)
    zero = jnp.zeros_like(l00)
    lower = jnp.stack(
        [jnp.stack([l00, zero, zero], -1), jnp.stack([l10, l11, zero], -1),
         jnp.stack([l20, l21, l22], -1)], -2,
    )
    first = moments[..., 0] / lower[..., 0, 0]
    second = (moments[..., 1] - lower[..., 1, 0] * first) / lower[..., 1, 1]
    third = (moments[..., 2] - lower[..., 2, 0] * first - lower[..., 2, 1] * second) / lower[
        ..., 2, 2
    ]
    upper_top = third / lower[..., 2, 2]
    upper_mid = (second - lower[..., 2, 1] * upper_top) / lower[..., 1, 1]
    upper_low = (first - lower[..., 1, 0] * upper_mid - lower[..., 2, 0] * upper_top) / lower[
        ..., 0, 0
    ]
    return jnp.stack([upper_low, upper_mid, upper_top], -1)


def butterfly_sum(values, axes):
    for axis, size in axes:
        if size & (size - 1) == 0:
            bit = 1
            while bit < size:
                pairs = [(i, i ^ bit) for i in range(size)]
                values = jax.tree.map(lambda v: v + lax.ppermute(v, axis, pairs), values)
                bit *= 2
        else:
            position = lax.axis_index(axis)
            def gathered(v):
                parts = [v]
                for shift in range(1, size):
                    pairs = [(i, (i + shift) % size) for i in range(size)]
                    parts.append(lax.ppermute(v, axis, pairs))
                stacked = jnp.stack(parts, 0)
                order = (position - jnp.arange(size)) % size
                canonical = jnp.zeros_like(stacked).at[order].set(stacked)
                return jnp.sum(canonical, axis=0)
            values = jax.tree.map(gathered, values)
    return values


def conv_body(coef_ref, vt_ref, ht_ref, padded_ref, out_ref):
    e = pl.program_id(0)
    image = padded_ref[0]
    total = None
    for kernel in range(len(SIGMA_PARTS)):
        across = jnp.dot(vt_ref[0, kernel], image, preferred_element_type=jnp.float32)
        smoothed = lax.dot_general(
            across.astype(jnp.bfloat16), ht_ref[kernel], (((1,), (1,)), ((), ())),
            preferred_element_type=jnp.float32,
        )
        term = coef_ref[e, kernel] * smoothed
        total = term if total is None else total + term
    out_ref[0] = total


def conv_tiles(coeffs, vtables, htables, padded, per_exposure):
    exp_dev, wide = padded.shape[0], padded.shape[1]
    nk, out_rows = vtables.shape[-3], vtables.shape[-2]
    tile_len = htables.shape[1]
    if per_exposure:
        vspec = pl.BlockSpec((1, nk, out_rows, wide), lambda e: (e, 0, 0, 0))
    else:
        vtables = vtables[None]
        vspec = pl.BlockSpec((1, nk, out_rows, wide), lambda e: (0, 0, 0, 0))
    flops = exp_dev * nk * 2 * out_rows * wide * (wide + tile_len)
    moved = exp_dev * wide * wide * 2 + exp_dev * out_rows * tile_len * 4
    return pl.pallas_call(
        conv_body,
        grid=(exp_dev,),
        in_specs=[
            pl.BlockSpec(memory_space=pltpu.SMEM),
            vspec,
            pl.BlockSpec((nk, tile_len, wide), lambda e: (0, 0, 0)),
            pl.BlockSpec((1, wide, wide), lambda e: (e, 0, 0)),
        ],
        out_specs=pl.BlockSpec((1, out_rows, tile_len), lambda e: (e, 0, 0)),
        out_shape=jax.ShapeDtypeStruct((exp_dev, out_rows, tile_len), jnp.float32),
        compiler_params=pltpu.CompilerParams(
            dimension_semantics=("arbitrary",), vmem_limit_bytes=48 * 1024 * 1024
        ),
        cost_estimate=pl.CostEstimate(flops=flops, bytes_accessed=moved, transcendentals=0),
    )(coeffs, vtables, htables, padded)


BLOCK = 128


def strip_body(off_ref, coef_ref, tb_ref, padded_ref, out_ref):
    e = pl.program_id(0)
    rows, tile_len = out_ref.shape[1], out_ref.shape[2]
    wide = padded_ref.shape[1]
    windows = [(start, min(2 * BLOCK, wide - start)) for start in range(0, tile_len, BLOCK)]
    anchor = off_ref[e]
    base = jnp.minimum((anchor // BLOCK) * BLOCK, wide - 2 * BLOCK)
    shift = anchor - base
    window = padded_ref[0, pl.ds(pl.multiple_of(base, 16), 2 * BLOCK), :]
    pick = (
        lax.broadcasted_iota(jnp.int32, (rows, 2 * BLOCK), 1)
        == lax.broadcasted_iota(jnp.int32, (rows, 2 * BLOCK), 0) + shift
    ).astype(jnp.bfloat16)
    total = None
    for kernel in range(len(SIGMA_PARTS)):
        table = tb_ref[kernel]
        strip_rows = jnp.dot(pick, table, preferred_element_type=jnp.float32).astype(jnp.bfloat16)
        across = jnp.dot(strip_rows, window, preferred_element_type=jnp.float32)
        across = across.astype(jnp.bfloat16)
        block = table[:BLOCK]
        cols = [
            lax.dot_general(
                across[:, start:start + reach], block[:, :reach], (((1,), (1,)), ((), ())),
                preferred_element_type=jnp.float32,
            )
            for start, reach in windows
        ]
        term = coef_ref[e, kernel] * jnp.concatenate(cols, 1)
        total = term if total is None else total + term
    out_ref[0] = total


def strip_tiles(offset, coeffs, tb, padded, tile_len):
    exp_dev, wide = padded.shape[0], padded.shape[1]
    nk = tb.shape[0]
    grid_spec = pltpu.PrefetchScalarGridSpec(
        num_scalar_prefetch=1,
        grid=(exp_dev,),
        in_specs=[
            pl.BlockSpec(memory_space=pltpu.SMEM),
            pl.BlockSpec((nk, 2 * BLOCK, 2 * BLOCK), lambda e, off: (0, 0, 0)),
            pl.BlockSpec((1, wide, wide), lambda e, off: (e, 0, 0)),
        ],
        out_specs=pl.BlockSpec((1, STRIP, tile_len), lambda e, off: (e, 0, 0)),
    )
    flops = exp_dev * nk * 2 * STRIP * 2 * BLOCK * (2 * BLOCK + wide + tile_len)
    moved = exp_dev * wide * wide * 2 + exp_dev * STRIP * tile_len * 4
    return pl.pallas_call(
        strip_body,
        grid_spec=grid_spec,
        out_shape=jax.ShapeDtypeStruct((exp_dev, STRIP, tile_len), jnp.float32),
        compiler_params=pltpu.CompilerParams(
            dimension_semantics=("arbitrary",), vmem_limit_bytes=48 * 1024 * 1024
        ),
        cost_estimate=pl.CostEstimate(flops=flops, bytes_accessed=moved, transcendentals=0),
    )(offset, coeffs, tb, padded)


def band_body(first, coef_ref, blk_ref, padded_ref, *rest):
    out_ref = rest[-1]
    e = pl.program_id(0) + first
    tile_len = out_ref.shape[1]
    wide = padded_ref.shape[1]
    windows = [(start, min(2 * BLOCK, wide - start)) for start in range(0, tile_len, BLOCK)]
    total = None
    for kernel in range(len(SIGMA_PARTS)):
        block = blk_ref[kernel][:BLOCK]
        rows = [
            jnp.dot(
                block[:, :reach], padded_ref[0, start:start + reach, :],
                preferred_element_type=jnp.float32,
            )
            for start, reach in windows
        ]
        across = jnp.concatenate(rows, 0).astype(jnp.bfloat16)
        cols = [
            lax.dot_general(
                across[:, start:start + reach], block[:, :reach], (((1,), (1,)), ((), ())),
                preferred_element_type=jnp.float32,
            )
            for start, reach in windows
        ]
        term = coef_ref[e, kernel] * jnp.concatenate(cols, 1)
        total = term if total is None else total + term
    out_ref[0] = total


def band_tiles(coeffs, blocks, padded, tile_len, first, count, into):
    exp_dev, wide = padded.shape[0], padded.shape[1]
    nk = blocks.shape[0]
    steps = tile_len // BLOCK
    flops = count * nk * steps * 2 * BLOCK * 2 * BLOCK * (wide + tile_len)
    moved = count * wide * wide * 2 + count * tile_len * tile_len * 4
    in_specs = [
        pl.BlockSpec(memory_space=pltpu.SMEM),
        pl.BlockSpec((nk, 2 * BLOCK, 2 * BLOCK), lambda e: (0, 0, 0)),
        pl.BlockSpec((1, wide, wide), lambda e: (e + first, 0, 0)),
    ]
    operands = [coeffs, blocks, padded]
    aliases = {}
    if into is not None:
        in_specs.append(pl.BlockSpec(memory_space=pl.ANY))
        operands.append(into)
        aliases = {3: 0}
    return pl.pallas_call(
        functools.partial(band_body, first),
        grid=(count,),
        in_specs=in_specs,
        out_specs=pl.BlockSpec((1, tile_len, tile_len), lambda e: (e + first, 0, 0)),
        out_shape=jax.ShapeDtypeStruct((exp_dev, tile_len, tile_len), jnp.float32),
        input_output_aliases=aliases,
        compiler_params=pltpu.CompilerParams(
            dimension_semantics=("arbitrary",), vmem_limit_bytes=48 * 1024 * 1024
        ),
        cost_estimate=pl.CostEstimate(flops=flops, bytes_accessed=moved, transcendentals=0),
    )(*operands)


def warp_body(extent, idx_ref, plane_ref, pick_ref, origin_ref, matched_ref, rmap_ref, cmap_ref,
              *rest):
    out_refs, acc_ref = rest[:-1], rest[-1]
    e = pl.program_id(0)
    side = matched_ref.shape[1]
    across_index = lax.broadcasted_iota(jnp.int32, (side, side), 1) + origin_ref[0]
    down_index = lax.broadcasted_iota(jnp.int32, (side, side), 0) + origin_ref[1]
    xrow = (across_index.astype(jnp.float32) + 0.5) / extent[0] * 2.0 - 1.0
    ycol = (down_index.astype(jnp.float32) + 0.5) / extent[1] * 2.0 - 1.0
    background = (
        plane_ref[e, 0] + plane_ref[e, 1] * xrow
    ) + plane_ref[e, 2] * ycol
    corrected = (matched_ref[0] - background).astype(jnp.bfloat16)
    halfway = jnp.dot(rmap_ref[0], corrected, preferred_element_type=jnp.float32)
    warped = lax.dot_general(
        halfway.astype(jnp.bfloat16), cmap_ref[0], (((1,), (1,)), ((), ())),
        preferred_element_type=jnp.float32,
    )
    warped = warped.astype(jnp.bfloat16).astype(jnp.float32)
    patches = acc_ref.shape[0]

    @pl.when(e == 0)
    def _():
        for v in range(patches):
            acc_ref[v] = pick_ref[e, v] * warped

    @pl.when(e > 0)
    def _():
        for v in range(patches):
            acc_ref[v] = acc_ref[v] + pick_ref[e, v] * warped

    @pl.when(e == pl.num_programs(0) - 1)
    def _():
        for v in range(patches):
            out_refs[v][...] = acc_ref[v].astype(jnp.bfloat16)


def warp_tiles(choose, plane, picked, origin, extent, matched, bank, part, pieces):
    exp_dev, tile_len = matched.shape[0], matched.shape[1]
    patches = picked.shape[1]
    rows = tile_len // pieces
    grid_spec = pltpu.PrefetchScalarGridSpec(
        num_scalar_prefetch=1,
        grid=(exp_dev,),
        in_specs=[
            pl.BlockSpec(memory_space=pltpu.SMEM),
            pl.BlockSpec(memory_space=pltpu.SMEM),
            pl.BlockSpec(memory_space=pltpu.SMEM),
            pl.BlockSpec((1, tile_len, tile_len), lambda e, idx: (e, 0, 0)),
            pl.BlockSpec((1, rows, tile_len), lambda e, idx: (idx[e, 0], part, 0)),
            pl.BlockSpec((1, tile_len, tile_len), lambda e, idx: (idx[e, 1], 0, 0)),
        ],
        out_specs=[pl.BlockSpec((rows, tile_len), lambda e, idx: (0, 0)) for _ in range(patches)],
        scratch_shapes=[pltpu.VMEM((patches, rows, tile_len), jnp.float32)],
    )
    flops = exp_dev * 4 * rows * tile_len * tile_len
    moved = exp_dev * tile_len * tile_len * (4 + 2) + exp_dev * rows * tile_len * 2
    moved = moved + patches * rows * tile_len * 2
    vmem = 60 * 1024 * 1024
    return pl.pallas_call(
        functools.partial(warp_body, extent),
        grid_spec=grid_spec,
        out_shape=[jax.ShapeDtypeStruct((rows, tile_len), jnp.bfloat16) for _ in range(patches)],
        compiler_params=pltpu.CompilerParams(
            dimension_semantics=("arbitrary",), vmem_limit_bytes=vmem
        ),
        cost_estimate=pl.CostEstimate(flops=flops, bytes_accessed=moved, transcendentals=0),
    )(choose, plane, picked, origin, matched, bank, bank)


def ring_scatter(parts, axis, size):
    ring = [(i, (i + 1) % size) for i in range(size)]
    travelling = None
    for step in range(size - 1):
        own = parts[step].astype(jnp.float32)
        outgoing = own if travelling is None else travelling + own
        travelling = lax.ppermute(outgoing.astype(jnp.bfloat16), axis, ring).astype(jnp.float32)
    own = parts[size - 1].astype(jnp.float32)
    return own if travelling is None else travelling + own


def rows_from(source, anchor):
    return lax.dynamic_slice_in_dim(source, anchor, STRIP, 0)


def shards(images, coeffs, pair_list, weights, resample_bank, warp_index, destinations, counts):
    exp_dev = images.shape[0]
    tile_len = images.shape[1]
    row_count = lax.axis_size("row")
    col_count = lax.axis_size("col")
    visit_count = lax.axis_size("visit")
    row_pos = lax.axis_index("row")
    col_pos = lax.axis_index("col")
    visit_pos = lax.axis_index("visit")
    height = row_count * tile_len
    breadth = col_count * tile_len
    padded = extended(images, (("col", 2), ("row", 1)), HALO)
    own_ids = visit_pos * exp_dev + jnp.arange(exp_dev, dtype=jnp.int32)
    first_col = pair_list[:, 0]
    second_col = pair_list[:, 1]
    offsets = pair_list[:, 2]
    hit_first = first_col[None, :] == own_ids[:, None]
    hit_second = second_col[None, :] == own_ids[:, None]
    partner = jnp.sum(
        jnp.where(hit_first, second_col[None, :], 0) + jnp.where(hit_second, first_col[None, :], 0),
        axis=1,
    )
    offset = jnp.sum(jnp.where(hit_first | hit_second, offsets[None, :], 0), axis=1)
    pick_rows = (
        lax.broadcasted_iota(jnp.int32, (exp_dev, STRIP, tile_len), 2)
        == offset[:, None, None] + lax.broadcasted_iota(jnp.int32, (exp_dev, STRIP, tile_len), 1)
    ).astype(jnp.bfloat16)
    own_strip = jnp.einsum(
        "esr,erl->esl", pick_rows, images, preferred_element_type=jnp.float32
    ).astype(jnp.bfloat16)
    listed = destinations[:, 0, 0, :]
    how_many = counts[:, 0, 0]
    usable = jnp.arange(MAXD, dtype=jnp.int32)[None, :] < how_many[:, None]
    owners = jnp.arange(visit_count, dtype=jnp.int32)
    member = jnp.any(usable[:, :, None] & (listed[:, :, None] == owners[None, None, :]), axis=1)
    tile_weight = weights[:, 0, 0]
    nothing = jnp.zeros((), jnp.bfloat16)
    picked = jnp.where(member, tile_weight[:, None], nothing)
    strip_rows_n = exp_dev * STRIP
    extra = -(-(exp_dev * visit_count) // tile_len)
    extra = -(-extra // 16) * 16
    tail = jnp.zeros((extra * tile_len,), jnp.bfloat16)
    tail = tail.at[: exp_dev * visit_count].set(picked.reshape(-1)).reshape(extra, tile_len)
    payload = jnp.concatenate([own_strip.reshape(strip_rows_n, tile_len), tail], axis=0)
    received = [payload]
    for shift in range(1, visit_count):
        pairs = [(i, (i + shift) % visit_count) for i in range(visit_count)]
        received.append(lax.ppermute(payload, "visit", pairs))
    stacked = jnp.stack(received, 0)
    strips_all = stacked[:, :strip_rows_n].reshape(visit_count * exp_dev, STRIP, tile_len)
    picked_all = stacked[:, strip_rows_n:].reshape(visit_count, -1)[:, : exp_dev * visit_count]
    picked_all = picked_all.reshape(visit_count, exp_dev, visit_count)
    partner_visit = partner // exp_dev
    slot = (visit_pos - partner_visit) % visit_count
    source = slot * exp_dev + partner % exp_dev
    choose_strip = (
        lax.broadcasted_iota(jnp.int32, (exp_dev, visit_count * exp_dev), 1) == source[:, None]
    ).astype(jnp.bfloat16)
    theirs = jnp.einsum(
        "ej,jsl->esl", choose_strip, strips_all, preferred_element_type=jnp.float32
    )
    own_patch = jnp.take(picked_all, visit_pos, axis=2).astype(jnp.float32)
    denominator = jnp.sum(own_patch).reshape(1)
    roomy = padded
    blocks = jnp.asarray(
        np.stack([toeplitz_block(2 * BLOCK, HALO, HALO * part) for part in SIGMA_PARTS])
    )
    nearby = strip_tiles(offset, coeffs, blocks, roomy, tile_len)
    half = exp_dev // 2
    matched = band_tiles(coeffs, blocks, roomy, tile_len, 0, half, None)
    matched = band_tiles(coeffs, blocks, roomy, tile_len, half, exp_dev - half, matched)
    difference = nearby - theirs
    pixel_weight = 1.0 / (1.0 + theirs * theirs)
    strip_rows = row_pos * tile_len + offset[:, None] + jnp.arange(STRIP, dtype=jnp.int32)[None, :]
    ycoord = centred(strip_rows, height)[:, :, None]
    xcoord = centred(col_pos * tile_len + jnp.arange(tile_len, dtype=jnp.int32), breadth)
    xgrid = xcoord[None, None, :]
    weight_x = pixel_weight * xgrid
    weight_y = pixel_weight * ycoord
    sum_w = jnp.sum(pixel_weight, axis=(1, 2))
    sum_x = jnp.sum(weight_x, axis=(1, 2))
    sum_y = jnp.sum(weight_y, axis=(1, 2))
    sum_xx = jnp.sum(weight_x * xgrid, axis=(1, 2))
    sum_xy = jnp.sum(weight_x * ycoord, axis=(1, 2))
    sum_yy = jnp.sum(weight_y * ycoord, axis=(1, 2))
    normal = jnp.stack(
        [
            jnp.stack([sum_w, sum_x, sum_y], -1),
            jnp.stack([sum_x, sum_xx, sum_xy], -1),
            jnp.stack([sum_y, sum_xy, sum_yy], -1),
        ],
        1,
    )
    moments = jnp.stack(
        [
            jnp.sum(pixel_weight * difference, axis=(1, 2)),
            jnp.sum(weight_x * difference, axis=(1, 2)),
            jnp.sum(weight_y * difference, axis=(1, 2)),
        ],
        -1,
    )
    packed = jnp.concatenate([normal.reshape(exp_dev, 9), moments], axis=1)
    packed = butterfly_sum(packed, (("row", row_count), ("col", col_count)))
    normal = packed[:, :9].reshape(exp_dev, 3, 3)
    moments = packed[:, 9:]
    plane_fit = solve_three(normal, moments)
    row_coord = centred(row_pos * tile_len + jnp.arange(tile_len, dtype=jnp.int32), height)
    choose = warp_index[:, 0, 0, :]
    ring_order = (
        lax.broadcasted_iota(jnp.int32, (visit_count, visit_count), 0)
        == (visit_pos - lax.broadcasted_iota(jnp.int32, (visit_count, visit_count), 1) - 1)
        % visit_count
    ).astype(jnp.float32)
    picked_ring = jnp.dot(picked.astype(jnp.float32), ring_order, precision=lax.Precision.HIGHEST)
    halves = [warp_tiles(
        choose, plane_fit, picked_ring,
        jnp.stack([col_pos * tile_len, row_pos * tile_len]).astype(jnp.int32),
        (float(breadth), float(height)), matched, resample_bank, part, 2) for part in range(2)]
    numerator = jnp.concatenate(
        [ring_scatter(piece, "visit", visit_count) for piece in halves], 0
    )[None]
    coadd_patch = numerator / denominator[:, None, None]
    return (coadd_patch, plane_fit)


def solution(mesh):
    in_specs = (
        P("visit", "row", "col"),
        P("visit", None),
        P(),
        P("visit", "row", "col"),
        P(),
        P("visit", "row", "col", None),
        P("visit", "row", "col", None),
        P("visit", "row", "col"),
    )
    out_specs = (P("visit", "row", "col"), P("visit", None))
    return jax.shard_map(shards, mesh=mesh, in_specs=in_specs, out_specs=out_specs, check_vma=False)
```
